32 devices in a mesh: groups: 2 (over x), seq: 16 (over z, y, core).
Axes of the slice: x: 2, y: 2, z: 4, core: 2. Of those that a mesh axis runs over, the one named last changes fastest.
Arguments:
- se_streams: bfloat16 [8192, 12288], P(('groups', 'seq')), parts along dimension 0, may hold values from -6 to 6
- mr_gates: bfloat16 [8192, 8192], P(('groups', 'seq')), parts along dimension 0, may hold values from -6 to 6
- se_feat: bfloat16 [7, 12288], replicated, may hold values from -2 to 2
- se_filter: bfloat16 [7, 256], replicated, may hold values from -2 to 2
- mr_feat: bfloat16 [7, 12288], replicated, may hold values from -2 to 2
- mr_filter: bfloat16 [128, 256], replicated, may hold values from -0.5 to 0.5
- mr_skip: bfloat16 [4096], replicated, may hold values from -1 to 1
- req_ends: int32 [32], P('groups'), parts along dimension 0, may hold values from 0 to 4095, as said below
- decode_row: int32 [32], P('groups'), parts along dimension 0, may hold values from 0 to 15, each once
Outputs:
- hyena_out: bfloat16 [8192, 4096], P(('groups', 'seq')), parts along dimension 0
- tail_cache: bfloat16 [32, 127, 4096], P('groups', None, 'seq'), parts along dimension 0
The draws below stay inside these ranges and needn't reach their ends.
There are 2 independent parts, one for each index of `groups`. The reference program is written for one: setup_inputs(seed, part) draws one part's arguments, and reference() takes and returns one part's arrays. A program takes and returns all parts, laid end to end along the dimension named above; an argument that names none is the same for every part. Nothing has to cross between parts.
Inputs may be any that keep to these rules, and one draw needn't show every extreme that they name: `req_ends`: the rows of one device hold at most 4 entries, and some device holds exactly 4.
All inputs are finite; a program needn't handle non-finite values.
Results may differ from the reference program's by a relative error of at most 0.0085.
Values may be sent and summed in bfloat16 or wider, within the bound.
No kernel may reach another device: no remote copies, remote signals or barrier semaphores. Data moves between devices by JAX's collectives and lax.ppermute only.
A program may use at most 192 MiB of HBM per device.

```python
import jax
import jax.numpy as jnp
from jax import lax

D = 4096
FILTERS = 256
SE_TAPS = 7
TAPS = 128
TOK_DEV = 256
ENDS_MAX = 4
SEQ_LEN = 4096
REQS = 16


def draw_req_ends(key, part):
    shards = SEQ_LEN // TOK_DEV
    slot_count = shards * ENDS_MAX
    sub_block = TOK_DEV // ENDS_MAX
    first_key, second_key, third_key = jax.random.split(key, 3)
    full_shard = jax.random.randint(first_key, (), 0, shards)
    shuffled = jax.random.permutation(second_key, slot_count).astype(jnp.int32)
    slot_ids = jnp.arange(slot_count, dtype=jnp.int32)
    priority = jnp.where(slot_ids // ENDS_MAX == full_shard, shuffled - slot_count, shuffled)
    chosen = jnp.argsort(priority, stable=True)[:REQS].astype(jnp.int32)
    chosen = jnp.sort(chosen)
    within = jax.random.randint(third_key, (REQS,), 0, sub_block)
    return (chosen // ENDS_MAX * TOK_DEV + chosen % ENDS_MAX * sub_block + within).astype(jnp.int32)


def level_of(rng, extent, cuts, low, high):
    gain = 1.0
    for position, blocks in cuts:
        steps = jax.random.uniform(jax.random.fold_in(jax.random.fold_in(rng, 6), position), (blocks,), jnp.float32, low / len(cuts), high / len(cuts))
        gain = gain * jnp.repeat(jnp.exp(steps), extent[position] // blocks).reshape((-1,) + (1,) * (len(extent) - 1 - position))
    return gain


def normal_values(key, dims, width, bound, cuts=(), kind=jnp.bfloat16):
    array = width * jax.random.normal(key, dims, jnp.float32)
    if cuts:
        array = array * level_of(key, dims, cuts, -0.22, 0.18)
    return jnp.clip(array, -bound, bound).astype(kind)


def setup_inputs(seed: int = 0, part: int = 0) -> dict:
    keys = jax.random.split(jax.random.key(seed), 10)
    own_keys = jax.random.split(jax.random.fold_in(keys[9], part), 10)
    se_streams = normal_values(own_keys[0], (SEQ_LEN, 3 * D), 1.0, 6.0, ((0, 16),))
    mr_gates = normal_values(own_keys[1], (SEQ_LEN, 2 * D), 1.0, 6.0, ((0, 16),))
    se_feat = normal_values(keys[2], (SE_TAPS, 3 * D), SE_TAPS ** -0.5, 2.0)
    se_filter = normal_values(keys[3], (SE_TAPS, FILTERS), SE_TAPS ** -0.5, 2.0)
    mr_feat = normal_values(keys[4], (SE_TAPS, 3 * D), SE_TAPS ** -0.5, 2.0)
    mr_filter = normal_values(keys[5], (TAPS, FILTERS), TAPS ** -0.5, 0.5)
    mr_skip = jnp.clip(jax.random.uniform(keys[6], (D,), jnp.float32, -1.0, 1.0), -1.0, 1.0).astype(jnp.bfloat16)
    req_ends = draw_req_ends(jax.random.fold_in(jax.random.fold_in(keys[9], part), 71), part)
    decode_row = jax.random.permutation(own_keys[8], REQS).astype(jnp.int32)
    return {"se_streams": se_streams, "mr_gates": mr_gates, "se_feat": se_feat, "se_filter": se_filter, "mr_feat": mr_feat, "mr_filter": mr_filter, "mr_skip": mr_skip, "req_ends": req_ends, "decode_row": decode_row}


def request_of(positions, req_ends):
    return jnp.sum((req_ends[None, :] < positions[:, None]).astype(jnp.int32), axis=1)


def short_conv(values, weights, segment):
    length = weights.shape[0]
    out_count = values.shape[0] - length + 1
    latest = length - 1
    current = segment[latest:]
    summed = values[latest:].astype(jnp.float32) * weights[0].astype(jnp.float32)
    for lag_step in range(1, length):
        earlier = values[latest - lag_step: latest - lag_step + out_count].astype(jnp.float32)
        same_req = segment[latest - lag_step: latest - lag_step + out_count] == current
        summed = summed + jnp.where(same_req[:, None], earlier * weights[lag_step].astype(jnp.float32), 0.0)
    return summed


def padded_short(values, weights, segment):
    reach_rows = weights.shape[0] - 1
    values_ext = jnp.concatenate([jnp.zeros((reach_rows, values.shape[1]), values.dtype), values], axis=0)
    seg_ext = jnp.concatenate([jnp.full((reach_rows,), -1, jnp.int32), segment], axis=0)
    return short_conv(values_ext, weights, seg_ext)


def toeplitz(taps_table):
    tap_count = taps_table.shape[0]
    zero_rows = jnp.zeros_like(taps_table)
    row_vector = jnp.concatenate([zero_rows, taps_table[::-1], zero_rows], axis=0)
    tiled = jnp.tile(row_vector, (tap_count, 1))[: tap_count * (3 * tap_count - 1)]
    skewed = tiled.reshape(tap_count, 3 * tap_count - 1, taps_table.shape[1])
    return skewed[:, tap_count - 1: 3 * tap_count - 1]


def pick_entries(lookup_table, indices):
    hits = indices[:, None] == jnp.arange(lookup_table.shape[0], dtype=jnp.int32)[None, :]
    return jnp.sum(jnp.where(hits, lookup_table[None, :], 0), axis=1).astype(jnp.int32)


def cut_tails(z_ext, req_ends, ext_start, requests, is_valid, tail_len):
    last_pos = pick_entries(req_ends, requests)
    first_pos = jnp.where(requests > 0, pick_entries(req_ends, jnp.maximum(requests - 1, 0)) + 1, 0)
    starts = (last_pos - tail_len + 1 - ext_start).astype(jnp.int32)
    pieces = jax.vmap(lambda begin: lax.dynamic_slice_in_dim(z_ext, begin, tail_len, 0))(starts)
    positions = last_pos[:, None] - tail_len + 1 + jnp.arange(tail_len, dtype=jnp.int32)[None, :]
    inside = (positions >= first_pos[:, None]) & is_valid[:, None]
    return jnp.where(inside[:, :, None], pieces, jnp.zeros((), pieces.dtype))


def reference(se_streams, mr_gates, se_feat, se_filter, mr_feat, mr_filter, mr_skip, req_ends, decode_row):
    seq_len = se_streams.shape[0]
    channels = mr_gates.shape[1] // 2
    group_ch = channels // se_filter.shape[1]
    segment = request_of(jnp.arange(seq_len, dtype=jnp.int32), req_ends)
    featured = padded_short(se_streams, se_feat, segment)
    z_one = (featured[:, channels:2 * channels] * featured[:, 2 * channels:]).astype(jnp.bfloat16)
    conv_one = padded_short(z_one, jnp.repeat(se_filter, group_ch, axis=1), segment)
    y_se = (featured[:, :channels] * conv_one).astype(jnp.bfloat16)
    gate_feat = padded_short(mr_gates, mr_feat[:, :2 * channels], segment)
    value_feat = padded_short(y_se, mr_feat[:, 2 * channels:], segment)
    z_two = (gate_feat[:, channels:] * value_feat).astype(jnp.bfloat16)
    z_ext = jnp.concatenate([jnp.zeros((TAPS, channels), jnp.bfloat16), z_two], axis=0)
    seg_ext = request_of(jnp.arange(seq_len + TAPS, dtype=jnp.int32) - TAPS, req_ends)
    matrix = toeplitz(mr_filter.astype(jnp.float32))

    def one_block(block_index):
        begin = block_index * TAPS
        window = lax.dynamic_slice_in_dim(z_ext, begin, 2 * TAPS, 0).astype(jnp.float32)
        window = window.reshape(2 * TAPS, FILTERS, group_ch)
        seg_window = lax.dynamic_slice_in_dim(seg_ext, begin, 2 * TAPS, 0)
        same_req = seg_window[TAPS:, None] == seg_window[None, :]
        masked = jnp.where(same_req[:, :, None], matrix, 0.0)
        result = jnp.einsum("tsg,sgk->tgk", masked, window, precision=lax.Precision.HIGHEST)
        return result.reshape(TAPS, channels)

    conv_two = lax.map(one_block, jnp.arange(seq_len // TAPS, dtype=jnp.int32)).reshape(seq_len, channels)
    mixed = (conv_two + mr_skip.astype(jnp.float32) * z_two.astype(jnp.float32)).astype(jnp.bfloat16)
    hyena_out = (gate_feat[:, :channels] * mixed.astype(jnp.float32)).astype(jnp.bfloat16)
    requests = jnp.arange(REQS, dtype=jnp.int32)
    states = cut_tails(z_ext, req_ends, -TAPS, requests, requests >= 0, TAPS - 1)
    tail_cache = jnp.zeros((REQS, TAPS - 1, channels), jnp.bfloat16).at[decode_row].set(states)
    return hyena_out, tail_cache
```

```python
import jax
import jax.numpy as jnp
from jax import lax
from jax.sharding import PartitionSpec as P
from jax.experimental import pallas as pl
from jax.experimental.pallas import tpu as pltpu

ENDS_MAX = 4


def passed_along(x, axis, by):
    length = lax.axis_size(axis)
    pairs = [(i, i + by) for i in range(length) if 0 <= i + by < length]
    return lax.ppermute(x, axis, pairs)


def request_of(positions, req_ends):
    return jnp.sum((req_ends[None, :] < positions[:, None]).astype(jnp.int32), axis=1)


def short_conv(values, weights, segment):
    length = weights.shape[0]
    out_count = values.shape[0] - length + 1
    latest = length - 1
    current = segment[latest:]
    summed = values[latest:].astype(jnp.float32) * weights[0].astype(jnp.float32)
    for lag_step in range(1, length):
        earlier = values[latest - lag_step : latest - lag_step + out_count].astype(jnp.float32)
        same_req = segment[latest - lag_step : latest - lag_step + out_count] == current
        summed = summed + jnp.where(
            same_req[:, None], earlier * weights[lag_step].astype(jnp.float32), 0.0
        )
    return summed


HALO = 32
TILE = 512


def chain_kernel(dist_ref, sq, sk, sv, hq, hk, hv, mq, mk, gq_h, gk_h, fq, fk, fv, filt, wq, wk, wv,
                 z2_ref, q2_ref, xq, xk, xv, xa, xb, zs, ys):
    rows = xq.shape[0]
    for main, halo, x in ((sq, hq, xq), (sk, hk, xk), (sv, hv, xv), (mq, gq_h, xa), (mk, gk_h, xb)):
        x[0:HALO, :] = halo[...].astype(jnp.float32)
        x[HALO:rows, :] = main[...].astype(jnp.float32)

    def sconv(x, w, first):
        dist = dist_ref[first:rows, :]
        acc = x[first:rows, :] * w[0:1, :]
        for lag in range(1, w.shape[0]):
            term = x[first - lag : rows - lag, :] * w[lag : lag + 1, :]
            acc = acc + jnp.where(dist >= lag, term, 0.0)
        return acc

    k1 = sconv(xk, fk, 16)
    v1 = sconv(xv, fv, 16)
    zs[16:rows, :] = (k1 * v1).astype(jnp.bfloat16).astype(jnp.float32)
    q1 = sconv(xq, fq, 24)
    c1 = sconv(zs, filt, 24)
    ys[24:rows, :] = (q1 * c1).astype(jnp.bfloat16).astype(jnp.float32)
    v2 = sconv(ys, wv, HALO)
    k2 = sconv(xb, wk, HALO)
    z2_ref[...] = (k2 * v2).astype(jnp.bfloat16)
    q2_ref[...] = sconv(xa, wq, HALO)


def short_chain(dist, se_streams, se_halo, mr_gates, mr_halo, se_feat, se_filt, mr_feat):
    tok_rows = se_streams.shape[0]
    channels = mr_gates.shape[1] // 2
    steps = channels // TILE
    rows = tok_rows + HALO
    taps = se_feat.shape[0]

    def col(part):
        return lambda j: (0, j + part * steps)

    main = [pl.BlockSpec((tok_rows, TILE), col(p)) for p in range(3)]
    halo = [pl.BlockSpec((HALO, TILE), col(p)) for p in range(3)]
    wts = [pl.BlockSpec((taps, TILE), col(p)) for p in range(3)]
    return pl.pallas_call(
        chain_kernel,
        grid=(steps,),
        in_specs=[pl.BlockSpec((rows, 1), lambda j: (0, 0))] + main + halo + main[:2] + halo[:2] + wts
        + [wts[0]] + wts,
        out_specs=[pl.BlockSpec((tok_rows, TILE), col(0)), pl.BlockSpec((tok_rows, TILE), col(0))],
        out_shape=[jax.ShapeDtypeStruct((tok_rows, channels), jnp.bfloat16),
                   jax.ShapeDtypeStruct((tok_rows, channels), jnp.float32)],
        scratch_shapes=[pltpu.VMEM((rows, TILE), jnp.float32) for _ in range(7)],
    )(dist, se_streams, se_streams, se_streams, se_halo, se_halo, se_halo, mr_gates, mr_gates,
      mr_halo, mr_halo, se_feat, se_feat, se_feat, se_filt, mr_feat, mr_feat, mr_feat)


def seg_start(positions, req_ends):
    seg = request_of(positions, req_ends)
    prev_end = jnp.where(seg > 0, pick_entries(req_ends, jnp.maximum(seg - 1, 0)), -1)
    return prev_end + 1


def toeplitz(taps_table):
    tap_count = taps_table.shape[0]
    t_ids = jnp.arange(tap_count, dtype=jnp.int32)[:, None, None]
    s_ids = jnp.arange(2 * tap_count, dtype=jnp.int32)[None, :, None]
    j_ids = jnp.arange(tap_count, dtype=jnp.int32)[None, None, :]
    onehot = (tap_count + t_ids - s_ids == j_ids).astype(taps_table.dtype)
    return jnp.einsum("tsj,jf->tsf", onehot, taps_table, preferred_element_type=jnp.float32).astype(
        taps_table.dtype
    )


def long_conv(z_ext, segment, taps_table, slot_count):
    tap_count = taps_table.shape[0]
    blocks = z_ext.shape[0] // tap_count - 1
    channels = z_ext.shape[1]
    filters = taps_table.shape[1]
    shaped = z_ext.reshape(blocks + 1, tap_count, channels)
    window = jnp.concatenate([shaped[:-1], shaped[1:]], axis=1)
    seg_shaped = segment.reshape(blocks + 1, tap_count)
    seg_window = jnp.concatenate([seg_shaped[:-1], seg_shaped[1:]], axis=1)
    base_seg = seg_shaped[1:, :1]
    rel_source = seg_window - base_seg
    rel_target = seg_shaped[1:] - base_seg
    slot_ids = jnp.arange(slot_count, dtype=jnp.int32)
    source_hit = rel_source[:, :, None] == slot_ids[None, None, :]
    grouped = window.reshape(blocks, 2 * tap_count, filters, channels // filters)
    stacked = jnp.where(
        source_hit[:, :, None, :, None], grouped[:, :, :, None, :], jnp.zeros((), grouped.dtype)
    )
    matrix = toeplitz(taps_table)
    result = jnp.einsum("tsf,bsfjg->btfjg", matrix, stacked, preferred_element_type=jnp.float32)
    target_hit = (rel_target[:, :, None] == slot_ids[None, None, :]).astype(jnp.float32)
    picked = jnp.sum(result * target_hit[:, :, None, :, None], axis=3)
    return picked.reshape(blocks * tap_count, channels)


def pick_entries(lookup_table, indices):
    hits = indices[:, None] == jnp.arange(lookup_table.shape[0], dtype=jnp.int32)[None, :]
    return jnp.sum(jnp.where(hits, lookup_table[None, :], 0), axis=1)


def cut_tails(z_ext, req_ends, ext_start, requests, is_valid, tail_len):
    last_pos = pick_entries(req_ends, requests)
    first_pos = jnp.where(requests > 0, pick_entries(req_ends, jnp.maximum(requests - 1, 0)) + 1, 0)
    offsets = jnp.arange(tail_len, dtype=jnp.int32)[None, :]
    positions = last_pos[:, None] - tail_len + 1 + offsets
    inside = (positions >= first_pos[:, None]) & is_valid[:, None]
    rows_wanted = positions - ext_start
    row_ids = jnp.arange(z_ext.shape[0], dtype=jnp.int32)
    select = ((rows_wanted[:, :, None] == row_ids[None, None, :]) & inside[:, :, None]).astype(
        jnp.bfloat16
    )
    picked = jnp.einsum("ris,sc->ric", select, z_ext, preferred_element_type=jnp.float32)
    return picked.astype(jnp.bfloat16)


def place_rows(states, target, row_count):
    placing = (jnp.arange(row_count, dtype=jnp.int32)[:, None] == target[None, :]).astype(
        jnp.bfloat16
    )
    placed = jnp.einsum("ts,sic->tic", placing, states, preferred_element_type=jnp.float32)
    return placed.astype(jnp.bfloat16)


def local(
    se_streams, mr_gates, se_feat, se_filter, mr_feat, mr_filter, mr_skip, req_ends, decode_row
):
    tok_rows = se_streams.shape[0]
    channels = mr_gates.shape[1] // 2
    shards = lax.axis_size("seq")
    device = lax.axis_index("seq")
    offset = device * tok_rows
    reach_rows = se_feat.shape[0] - 1
    tap_count = mr_filter.shape[0]
    tail_len = tap_count - 1
    group_ch = channels // se_filter.shape[1]
    total_req = req_ends.shape[0]
    slot_total = ENDS_MAX + 1
    rim_depth = 2 * reach_rows
    prev_se, prev_mr = passed_along(
        (se_streams[tok_rows - 3 * reach_rows :], mr_gates[tok_rows - reach_rows :]), "seq", 1
    )
    se_halo = jnp.pad(prev_se, ((HALO - 3 * reach_rows, 0), (0, 0)))
    mr_halo = jnp.pad(prev_mr, ((HALO - reach_rows, 0), (0, 0)))
    ext_pos = offset - HALO + jnp.arange(tok_rows + HALO, dtype=jnp.int32)
    dist = (ext_pos - seg_start(ext_pos, req_ends))[:, None]
    z_two, q_two = short_chain(
        dist,
        se_streams,
        se_halo,
        mr_gates,
        mr_halo,
        se_feat.astype(jnp.float32),
        jnp.repeat(se_filter, group_ch, axis=1).astype(jnp.float32),
        mr_feat.astype(jnp.float32),
    )
    prev_z = passed_along(z_two[tok_rows - tail_len :], "seq", 1)
    z_ext = jnp.concatenate([jnp.zeros((1, channels), jnp.bfloat16), prev_z, z_two], axis=0)
    seg_long = request_of(
        offset - tap_count + jnp.arange(tok_rows + tap_count, dtype=jnp.int32), req_ends
    )
    first_req = request_of(jnp.reshape(offset, (1,)), req_ends)[0]
    past_req = request_of(jnp.reshape(offset + tok_rows, (1,)), req_ends)[0]
    slot_local = jnp.arange(ENDS_MAX, dtype=jnp.int32)
    local_req = jnp.minimum(first_req + slot_local, total_req - 1)
    states = cut_tails(
        z_ext, req_ends, offset - tap_count, local_req, first_req + slot_local < past_req, tail_len
    )
    received = lax.all_to_all(states, "seq", split_axis=2, concat_axis=0, tiled=True)
    conv_two = long_conv(z_ext, seg_long, mr_filter, slot_total)
    mixed = (conv_two + mr_skip.astype(jnp.float32) * z_two.astype(jnp.float32)).astype(
        jnp.bfloat16
    )
    slot_index = jnp.arange(shards * ENDS_MAX, dtype=jnp.int32)
    source = slot_index // ENDS_MAX
    within = slot_index % ENDS_MAX
    source_first = request_of(source * tok_rows, req_ends)
    source_past = request_of((source + 1) * tok_rows, req_ends)
    requests = source_first + within
    is_valid = requests < source_past
    target = jnp.where(
        is_valid, pick_entries(decode_row, jnp.minimum(requests, total_req - 1)), total_req
    )
    tail_cache = place_rows(received, target, total_req)
    hyena_out = (q_two * mixed.astype(jnp.float32)).astype(jnp.bfloat16)
    return (hyena_out, tail_cache)


def solution(mesh):
    placed = (
        P(("groups", "seq"), None),
        P(("groups", "seq"), None),
        P(),
        P(),
        P(),
        P(),
        P(),
        P("groups"),
        P("groups"),
    )
    return jax.shard_map(
        local,
        mesh=mesh,
        in_specs=placed,
        out_specs=(P(("groups", "seq"), None), P("groups", None, "seq")),
        check_vma=False,
    )
```

```python
import jax
import jax.numpy as jnp
from jax import lax
from jax.sharding import PartitionSpec as P
from jax.experimental import pallas as pl
from jax.experimental.pallas import tpu as pltpu

ENDS_MAX = 4


def passed_along(x, axis, by):
    length = lax.axis_size(axis)
    pairs = [(i, i + by) for i in range(length) if 0 <= i + by < length]
    return lax.ppermute(x, axis, pairs)


def request_of(positions, req_ends):
    return jnp.sum((req_ends[None, :] < positions[:, None]).astype(jnp.int32), axis=1)


def short_conv(values, weights, segment):
    length = weights.shape[0]
    out_count = values.shape[0] - length + 1
    latest = length - 1
    current = segment[latest:]
    summed = values[latest:].astype(jnp.float32) * weights[0].astype(jnp.float32)
    for lag_step in range(1, length):
        earlier = values[latest - lag_step : latest - lag_step + out_count].astype(jnp.float32)
        same_req = segment[latest - lag_step : latest - lag_step + out_count] == current
        summed = summed + jnp.where(
            same_req[:, None], earlier * weights[lag_step].astype(jnp.float32), 0.0
        )
    return summed


HALO = 32
TILE = 512


def chain_kernel(dist_ref, sq, sk, sv, hq, hk, hv, mq, mk, gq_h, gk_h, fq, fk, fv, filt, wq, wk, wv,
                 z2_ref, q2_ref, xq, xk, xv, xa, xb, zs, ys):
    rows = xq.shape[0]
    for main, halo, x in ((sq, hq, xq), (sk, hk, xk), (sv, hv, xv), (mq, gq_h, xa), (mk, gk_h, xb)):
        x[0:HALO, :] = halo[...].astype(jnp.float32)
        x[HALO:rows, :] = main[...].astype(jnp.float32)

    def sconv(x, w, first):
        dist = dist_ref[first:rows, :]
        acc = x[first:rows, :] * w[0:1, :]
        for lag in range(1, w.shape[0]):
            term = x[first - lag : rows - lag, :] * w[lag : lag + 1, :]
            acc = acc + jnp.where(dist >= lag, term, 0.0)
        return acc

    k1 = sconv(xk, fk, 16)
    v1 = sconv(xv, fv, 16)
    zs[16:rows, :] = (k1 * v1).astype(jnp.bfloat16).astype(jnp.float32)
    q1 = sconv(xq, fq, 24)
    c1 = sconv(zs, filt, 24)
    ys[24:rows, :] = (q1 * c1).astype(jnp.bfloat16).astype(jnp.float32)
    v2 = sconv(ys, wv, HALO)
    k2 = sconv(xb, wk, HALO)
    z2_ref[...] = (k2 * v2).astype(jnp.bfloat16)
    q2_ref[...] = sconv(xa, wq, HALO)


def short_chain(dist, se_streams, se_halo, mr_gates, mr_halo, se_feat, se_filt, mr_feat):
    tok_rows = se_streams.shape[0]
    channels = mr_gates.shape[1] // 2
    steps = channels // TILE
    rows = tok_rows + HALO
    taps = se_feat.shape[0]

    def col(part):
        return lambda j: (0, j + part * steps)

    main = [pl.BlockSpec((tok_rows, TILE), col(p)) for p in range(3)]
    halo = [pl.BlockSpec((HALO, TILE), col(p)) for p in range(3)]
    wts = [pl.BlockSpec((taps, TILE), col(p)) for p in range(3)]
    return pl.pallas_call(
        chain_kernel,
        grid=(steps,),
        in_specs=[pl.BlockSpec((rows, 1), lambda j: (0, 0))] + main + halo + main[:2] + halo[:2] + wts
        + [wts[0]] + wts,
        out_specs=[pl.BlockSpec((tok_rows, TILE), col(0)), pl.BlockSpec((tok_rows, TILE), col(0))],
        out_shape=[jax.ShapeDtypeStruct((tok_rows, channels), jnp.bfloat16),
                   jax.ShapeDtypeStruct((tok_rows, channels), jnp.float32)],
        scratch_shapes=[pltpu.VMEM((rows, TILE), jnp.float32) for _ in range(7)],
    )(dist, se_streams, se_streams, se_streams, se_halo, se_halo, se_halo, mr_gates, mr_gates,
      mr_halo, mr_halo, se_feat, se_feat, se_feat, se_filt, mr_feat, mr_feat, mr_feat)


LANES = 256
GROUP_LANES = 128


def long_kernel(tss_ref, spos_ref, prev_ref, z_ref, q2_ref, skip_ref, u_ref, out_ref):
    blk = prev_ref.shape[0]
    tile = z_ref.shape[1]
    width = u_ref.shape[1]
    per_group = tile // u_ref.shape[0]
    z = z_ref[...]
    windows = (jnp.concatenate([prev_ref[...], z[:blk]], axis=0), z)
    masks = [
        spos_ref[:, b * blk : b * blk + width] >= tss_ref[b * blk : (b + 1) * blk, :] for b in range(2)
    ]
    lane_grp = lax.broadcasted_iota(jnp.int32, (1, GROUP_LANES), 1) // per_group
    halves = tile // GROUP_LANES
    groups_half = GROUP_LANES // per_group
    acc = [[jnp.zeros((blk, GROUP_LANES), jnp.float32) for _ in range(halves)] for _ in range(2)]
    for g in range(u_ref.shape[0]):
        half = g // groups_half
        row = jnp.broadcast_to(u_ref[g : g + 1, :], (blk, width))
        taps = pltpu.roll(row, 0, 1, stride=1, stride_axis=0)
        for b in range(2):
            mat = jnp.where(masks[b], taps, 0.0).astype(jnp.bfloat16)
            part = windows[b][:, half * GROUP_LANES : (half + 1) * GROUP_LANES]
            res = jnp.dot(mat, part, preferred_element_type=jnp.float32)
            acc[b][half] = jnp.where(lane_grp == g % groups_half, res, acc[b][half])
    conv = jnp.concatenate([jnp.concatenate(acc[b], axis=1) for b in range(2)], axis=0)
    mixed = (conv + skip_ref[...] * z.astype(jnp.float32)).astype(jnp.bfloat16)
    out_ref[...] = (q2_ref[...] * mixed.astype(jnp.float32)).astype(jnp.bfloat16)


def long_conv_out(tss, spos, prev_z, z_two, q_two, skip, taps_rows):
    tok_rows, channels = z_two.shape
    blk = prev_z.shape[0]
    steps = channels // LANES
    per_group = channels // taps_rows.shape[0]
    return pl.pallas_call(
        long_kernel,
        grid=(steps,),
        in_specs=[
            pl.BlockSpec(tss.shape, lambda j: (0, 0)),
            pl.BlockSpec(spos.shape, lambda j: (0, 0)),
            pl.BlockSpec((blk, LANES), lambda j: (0, j)),
            pl.BlockSpec((tok_rows, LANES), lambda j: (0, j)),
            pl.BlockSpec((tok_rows, LANES), lambda j: (0, j)),
            pl.BlockSpec((1, LANES), lambda j: (0, j)),
            pl.BlockSpec((LANES // per_group, taps_rows.shape[1]), lambda j: (j, 0)),
        ],
        out_specs=pl.BlockSpec((tok_rows, LANES), lambda j: (0, j)),
        out_shape=jax.ShapeDtypeStruct((tok_rows, channels), jnp.bfloat16),
    )(tss, spos, prev_z, z_two, q_two, skip, taps_rows)


def seg_start(positions, req_ends):
    seg = request_of(positions, req_ends)
    prev_end = jnp.where(seg > 0, pick_entries(req_ends, jnp.maximum(seg - 1, 0)), -1)
    return prev_end + 1


def toeplitz(taps_table):
    tap_count = taps_table.shape[0]
    t_ids = jnp.arange(tap_count, dtype=jnp.int32)[:, None, None]
    s_ids = jnp.arange(2 * tap_count, dtype=jnp.int32)[None, :, None]
    j_ids = jnp.arange(tap_count, dtype=jnp.int32)[None, None, :]
    onehot = (tap_count + t_ids - s_ids == j_ids).astype(taps_table.dtype)
    return jnp.einsum("tsj,jf->tsf", onehot, taps_table, preferred_element_type=jnp.float32).astype(
        taps_table.dtype
    )


def long_conv(z_ext, segment, taps_table, slot_count):
    tap_count = taps_table.shape[0]
    blocks = z_ext.shape[0] // tap_count - 1
    channels = z_ext.shape[1]
    filters = taps_table.shape[1]
    shaped = z_ext.reshape(blocks + 1, tap_count, channels)
    window = jnp.concatenate([shaped[:-1], shaped[1:]], axis=1)
    seg_shaped = segment.reshape(blocks + 1, tap_count)
    seg_window = jnp.concatenate([seg_shaped[:-1], seg_shaped[1:]], axis=1)
    base_seg = seg_shaped[1:, :1]
    rel_source = seg_window - base_seg
    rel_target = seg_shaped[1:] - base_seg
    slot_ids = jnp.arange(slot_count, dtype=jnp.int32)
    source_hit = rel_source[:, :, None] == slot_ids[None, None, :]
    grouped = window.reshape(blocks, 2 * tap_count, filters, channels // filters)
    stacked = jnp.where(
        source_hit[:, :, None, :, None], grouped[:, :, :, None, :], jnp.zeros((), grouped.dtype)
    )
    matrix = toeplitz(taps_table)
    result = jnp.einsum("tsf,bsfjg->btfjg", matrix, stacked, preferred_element_type=jnp.float32)
    target_hit = (rel_target[:, :, None] == slot_ids[None, None, :]).astype(jnp.float32)
    picked = jnp.sum(result * target_hit[:, :, None, :, None], axis=3)
    return picked.reshape(blocks * tap_count, channels)


def pick_entries(lookup_table, indices):
    hits = indices[:, None] == jnp.arange(lookup_table.shape[0], dtype=jnp.int32)[None, :]
    return jnp.sum(jnp.where(hits, lookup_table[None, :], 0), axis=1)


def cut_tails(z_ext, req_ends, ext_start, requests, is_valid, tail_len):
    last_pos = pick_entries(req_ends, requests)
    first_pos = jnp.where(requests > 0, pick_entries(req_ends, jnp.maximum(requests - 1, 0)) + 1, 0)
    offsets = jnp.arange(tail_len, dtype=jnp.int32)[None, :]
    positions = last_pos[:, None] - tail_len + 1 + offsets
    inside = (positions >= first_pos[:, None]) & is_valid[:, None]
    rows_wanted = positions - ext_start
    row_ids = jnp.arange(z_ext.shape[0], dtype=jnp.int32)
    select = ((rows_wanted[:, :, None] == row_ids[None, None, :]) & inside[:, :, None]).astype(
        jnp.bfloat16
    )
    picked = jnp.einsum("ris,sc->ric", select, z_ext, preferred_element_type=jnp.float32)
    return picked.astype(jnp.bfloat16)


def place_rows(states, target, row_count):
    placing = (jnp.arange(row_count, dtype=jnp.int32)[:, None] == target[None, :]).astype(
        jnp.bfloat16
    )
    placed = jnp.einsum("ts,sic->tic", placing, states, preferred_element_type=jnp.float32)
    return placed.astype(jnp.bfloat16)


def local(
    se_streams, mr_gates, se_feat, se_filter, mr_feat, mr_filter, mr_skip, req_ends, decode_row
):
    tok_rows = se_streams.shape[0]
    channels = mr_gates.shape[1] // 2
    shards = lax.axis_size("seq")
    device = lax.axis_index("seq")
    offset = device * tok_rows
    reach_rows = se_feat.shape[0] - 1
    tap_count = mr_filter.shape[0]
    tail_len = tap_count - 1
    group_ch = channels // se_filter.shape[1]
    total_req = req_ends.shape[0]
    slot_total = ENDS_MAX + 1
    rim_depth = 2 * reach_rows
    prev_se, prev_mr = passed_along(
        (se_streams[tok_rows - 3 * reach_rows :], mr_gates[tok_rows - reach_rows :]), "seq", 1
    )
    se_halo = jnp.pad(prev_se, ((HALO - 3 * reach_rows, 0), (0, 0)))
    mr_halo = jnp.pad(prev_mr, ((HALO - reach_rows, 0), (0, 0)))
    ext_pos = offset - HALO + jnp.arange(tok_rows + HALO, dtype=jnp.int32)
    dist = (ext_pos - seg_start(ext_pos, req_ends))[:, None]
    z_two, q_two = short_chain(
        dist,
        se_streams,
        se_halo,
        mr_gates,
        mr_halo,
        se_feat.astype(jnp.float32),
        jnp.repeat(se_filter, group_ch, axis=1).astype(jnp.float32),
        mr_feat.astype(jnp.float32),
    )
    prev_z = passed_along(z_two[tok_rows - tap_count :], "seq", 1)
    z_ext = jnp.concatenate([prev_z, z_two], axis=0)
    first_req = request_of(jnp.reshape(offset, (1,)), req_ends)[0]
    past_req = request_of(jnp.reshape(offset + tok_rows, (1,)), req_ends)[0]
    slot_local = jnp.arange(ENDS_MAX, dtype=jnp.int32)
    local_req = jnp.minimum(first_req + slot_local, total_req - 1)
    states = cut_tails(
        z_ext, req_ends, offset - tap_count, local_req, first_req + slot_local < past_req, tail_len
    )
    received = lax.all_to_all(states, "seq", split_axis=2, concat_axis=0, tiled=True)
    tgt_pos = offset + jnp.arange(tok_rows, dtype=jnp.int32)
    tss = seg_start(tgt_pos, req_ends)[:, None]
    spos = (offset - tap_count + jnp.arange(tok_rows + tap_count, dtype=jnp.int32))[None, :]
    filt_t = mr_filter[::-1].T.astype(jnp.float32)
    filters = filt_t.shape[0]
    taps_rows = jnp.concatenate(
        [jnp.zeros((filters, 1), jnp.float32), filt_t, jnp.zeros((filters, tap_count - 1), jnp.float32)],
        axis=1,
    )
    hyena_out = long_conv_out(
        tss, spos, prev_z, z_two, q_two, mr_skip.astype(jnp.float32)[None, :], taps_rows
    )
    slot_index = jnp.arange(shards * ENDS_MAX, dtype=jnp.int32)
    source = slot_index // ENDS_MAX
    within = slot_index % ENDS_MAX
    source_first = request_of(source * tok_rows, req_ends)
    source_past = request_of((source + 1) * tok_rows, req_ends)
    requests = source_first + within
    is_valid = requests < source_past
    target = jnp.where(
        is_valid, pick_entries(decode_row, jnp.minimum(requests, total_req - 1)), total_req
    )
    tail_cache = place_rows(received, target, total_req)
    return (hyena_out, tail_cache)


def solution(mesh):
    placed = (
        P(("groups", "seq"), None),
        P(("groups", "seq"), None),
        P(),
        P(),
        P(),
        P(),
        P(),
        P("groups"),
        P("groups"),
    )
    return jax.shard_map(
        local,
        mesh=mesh,
        in_specs=placed,
        out_specs=(P(("groups", "seq"), None), P("groups", None, "seq")),
        check_vma=False,
    )
```

```python
import jax
import jax.numpy as jnp
from jax import lax
from jax.sharding import PartitionSpec as P
from jax.experimental import pallas as pl
from jax.experimental.pallas import tpu as pltpu

ENDS_MAX = 4


def passed_along(x, axis, by):
    length = lax.axis_size(axis)
    pairs = [(i, i + by) for i in range(length) if 0 <= i + by < length]
    return lax.ppermute(x, axis, pairs)


def request_of(positions, req_ends):
    return jnp.sum((req_ends[None, :] < positions[:, None]).astype(jnp.int32), axis=1)


def short_conv(values, weights, segment):
    length = weights.shape[0]
    out_count = values.shape[0] - length + 1
    latest = length - 1
    current = segment[latest:]
    summed = values[latest:].astype(jnp.float32) * weights[0].astype(jnp.float32)
    for lag_step in range(1, length):
        earlier = values[latest - lag_step : latest - lag_step + out_count].astype(jnp.float32)
        same_req = segment[latest - lag_step : latest - lag_step + out_count] == current
        summed = summed + jnp.where(
            same_req[:, None], earlier * weights[lag_step].astype(jnp.float32), 0.0
        )
    return summed


HALO = 32
TILE = 512


def chain_kernel(dist_ref, sq, sk, sv, hq, hk, hv, mq, mk, gq_h, gk_h, fq, fk, fv, filt, wq, wk, wv,
                 z2_ref, q2_ref, xq, xk, xv, xa, xb, zs, ys):
    rows = xq.shape[0]
    for main, halo, x in ((sq, hq, xq), (sk, hk, xk), (sv, hv, xv), (mq, gq_h, xa), (mk, gk_h, xb)):
        x[0:HALO, :] = halo[...].astype(jnp.float32)
        x[HALO:rows, :] = main[...].astype(jnp.float32)

    def sconv(x, w, first):
        dist = dist_ref[first:rows, :]
        acc = x[first:rows, :] * w[0:1, :]
        for lag in range(1, w.shape[0]):
            term = x[first - lag : rows - lag, :] * w[lag : lag + 1, :]
            acc = acc + jnp.where(dist >= lag, term, 0.0)
        return acc

    k1 = sconv(xk, fk, 16)
    v1 = sconv(xv, fv, 16)
    zs[16:rows, :] = (k1 * v1).astype(jnp.bfloat16).astype(jnp.float32)
    q1 = sconv(xq, fq, 24)
    c1 = sconv(zs, filt, 24)
    ys[24:rows, :] = (q1 * c1).astype(jnp.bfloat16).astype(jnp.float32)
    v2 = sconv(ys, wv, HALO)
    k2 = sconv(xb, wk, HALO)
    z2 = (k2 * v2).astype(jnp.bfloat16)
    chunk = z2_ref.shape[2]
    for i in range(z2_ref.shape[0]):
        z2_ref[i] = z2[:, i * chunk : (i + 1) * chunk]
    q2_ref[...] = sconv(xa, wq, HALO)


def short_chain(dist, se_streams, se_halo, mr_gates, mr_halo, se_feat, se_filt, mr_feat, shards):
    tok_rows = se_streams.shape[0]
    channels = mr_gates.shape[1] // 2
    steps = channels // TILE
    rows = tok_rows + HALO
    taps = se_feat.shape[0]
    chunk = channels // shards

    def col(part):
        return lambda j: (0, j + part * steps)

    main = [pl.BlockSpec((tok_rows, TILE), col(p)) for p in range(3)]
    halo = [pl.BlockSpec((HALO, TILE), col(p)) for p in range(3)]
    wts = [pl.BlockSpec((taps, TILE), col(p)) for p in range(3)]
    return pl.pallas_call(
        chain_kernel,
        grid=(steps,),
        in_specs=[pl.BlockSpec((rows, 1), lambda j: (0, 0))] + main + halo + main[:2] + halo[:2] + wts
        + [wts[0]] + wts,
        out_specs=[
            pl.BlockSpec((TILE // chunk, tok_rows, chunk), lambda j: (j, 0, 0)),
            pl.BlockSpec((tok_rows, TILE), col(0)),
        ],
        out_shape=[jax.ShapeDtypeStruct((shards, tok_rows, chunk), jnp.bfloat16),
                   jax.ShapeDtypeStruct((tok_rows, channels), jnp.float32)],
        scratch_shapes=[pltpu.VMEM((rows, TILE), jnp.float32) for _ in range(7)],
    )(dist, se_streams, se_streams, se_streams, se_halo, se_halo, se_halo, mr_gates, mr_gates,
      mr_halo, mr_halo, se_feat, se_feat, se_feat, se_filt, mr_feat, mr_feat, mr_feat)


GROUP_LANES = 128


def long_kernel(tss_ref, spos_ref, prev_ref, z_ref, q2_ref, skip_ref, u_ref, out_ref):
    blk = prev_ref.shape[1]
    tile = z_ref.shape[2]
    width = u_ref.shape[1]
    per_group = tile // u_ref.shape[0]
    z = z_ref[0]
    windows = (jnp.concatenate([prev_ref[0], z[:blk]], axis=0), z)
    masks = [
        spos_ref[:, b * blk : b * blk + width] >= tss_ref[b * blk : (b + 1) * blk, :] for b in range(2)
    ]
    lane_grp = lax.broadcasted_iota(jnp.int32, (1, GROUP_LANES), 1) // per_group
    halves = tile // GROUP_LANES
    groups_half = GROUP_LANES // per_group
    acc = [[jnp.zeros((blk, GROUP_LANES), jnp.float32) for _ in range(halves)] for _ in range(2)]
    for g in range(u_ref.shape[0]):
        half = g // groups_half
        row = jnp.broadcast_to(u_ref[g : g + 1, :], (blk, width))
        taps = pltpu.roll(row, 0, 1, stride=1, stride_axis=0)
        for b in range(2):
            mat = jnp.where(masks[b], taps, 0.0).astype(jnp.bfloat16)
            part = windows[b][:, half * GROUP_LANES : (half + 1) * GROUP_LANES]
            res = jnp.dot(mat, part, preferred_element_type=jnp.float32)
            acc[b][half] = jnp.where(lane_grp == g % groups_half, res, acc[b][half])
    conv = jnp.concatenate([jnp.concatenate(acc[b], axis=1) for b in range(2)], axis=0)
    mixed = (conv + skip_ref[...] * z.astype(jnp.float32)).astype(jnp.bfloat16)
    out_ref[...] = (q2_ref[...] * mixed.astype(jnp.float32)).astype(jnp.bfloat16)


def long_conv_out(tss, spos, prev_z, z_two, q_two, skip, taps_rows):
    steps, tok_rows, lanes = z_two.shape
    channels = steps * lanes
    blk = prev_z.shape[1]
    per_group = channels // taps_rows.shape[0]
    return pl.pallas_call(
        long_kernel,
        grid=(steps,),
        in_specs=[
            pl.BlockSpec(tss.shape, lambda j: (0, 0)),
            pl.BlockSpec(spos.shape, lambda j: (0, 0)),
            pl.BlockSpec((1, blk, lanes), lambda j: (j, 0, 0)),
            pl.BlockSpec((1, tok_rows, lanes), lambda j: (j, 0, 0)),
            pl.BlockSpec((tok_rows, lanes), lambda j: (0, j)),
            pl.BlockSpec((1, lanes), lambda j: (0, j)),
            pl.BlockSpec((lanes // per_group, taps_rows.shape[1]), lambda j: (j, 0)),
        ],
        out_specs=pl.BlockSpec((tok_rows, lanes), lambda j: (0, j)),
        out_shape=jax.ShapeDtypeStruct((tok_rows, channels), jnp.bfloat16),
    )(tss, spos, prev_z, z_two, q_two, skip, taps_rows)


def seg_start(positions, req_ends):
    seg = request_of(positions, req_ends)
    prev_end = jnp.where(seg > 0, pick_entries(req_ends, jnp.maximum(seg - 1, 0)), -1)
    return prev_end + 1


def toeplitz(taps_table):
    tap_count = taps_table.shape[0]
    t_ids = jnp.arange(tap_count, dtype=jnp.int32)[:, None, None]
    s_ids = jnp.arange(2 * tap_count, dtype=jnp.int32)[None, :, None]
    j_ids = jnp.arange(tap_count, dtype=jnp.int32)[None, None, :]
    onehot = (tap_count + t_ids - s_ids == j_ids).astype(taps_table.dtype)
    return jnp.einsum("tsj,jf->tsf", onehot, taps_table, preferred_element_type=jnp.float32).astype(
        taps_table.dtype
    )


def long_conv(z_ext, segment, taps_table, slot_count):
    tap_count = taps_table.shape[0]
    blocks = z_ext.shape[0] // tap_count - 1
    channels = z_ext.shape[1]
    filters = taps_table.shape[1]
    shaped = z_ext.reshape(blocks + 1, tap_count, channels)
    window = jnp.concatenate([shaped[:-1], shaped[1:]], axis=1)
    seg_shaped = segment.reshape(blocks + 1, tap_count)
    seg_window = jnp.concatenate([seg_shaped[:-1], seg_shaped[1:]], axis=1)
    base_seg = seg_shaped[1:, :1]
    rel_source = seg_window - base_seg
    rel_target = seg_shaped[1:] - base_seg
    slot_ids = jnp.arange(slot_count, dtype=jnp.int32)
    source_hit = rel_source[:, :, None] == slot_ids[None, None, :]
    grouped = window.reshape(blocks, 2 * tap_count, filters, channels // filters)
    stacked = jnp.where(
        source_hit[:, :, None, :, None], grouped[:, :, :, None, :], jnp.zeros((), grouped.dtype)
    )
    matrix = toeplitz(taps_table)
    result = jnp.einsum("tsf,bsfjg->btfjg", matrix, stacked, preferred_element_type=jnp.float32)
    target_hit = (rel_target[:, :, None] == slot_ids[None, None, :]).astype(jnp.float32)
    picked = jnp.sum(result * target_hit[:, :, None, :, None], axis=3)
    return picked.reshape(blocks * tap_count, channels)


def pick_entries(lookup_table, indices):
    hits = indices[:, None] == jnp.arange(lookup_table.shape[0], dtype=jnp.int32)[None, :]
    return jnp.sum(jnp.where(hits, lookup_table[None, :], 0), axis=1)


def cut_tails(z_ext, req_ends, ext_start, requests, is_valid, tail_len):
    last_pos = pick_entries(req_ends, requests)
    first_pos = jnp.where(requests > 0, pick_entries(req_ends, jnp.maximum(requests - 1, 0)) + 1, 0)
    offsets = jnp.arange(tail_len, dtype=jnp.int32)[None, :]
    positions = last_pos[:, None] - tail_len + 1 + offsets
    inside = (positions >= first_pos[:, None]) & is_valid[:, None]
    rows_wanted = positions - ext_start
    row_ids = jnp.arange(z_ext.shape[0], dtype=jnp.int32)
    select = ((rows_wanted[:, :, None] == row_ids[None, None, :]) & inside[:, :, None]).astype(
        jnp.bfloat16
    )
    picked = jnp.einsum("ris,sc->ric", select, z_ext, preferred_element_type=jnp.float32)
    return picked.astype(jnp.bfloat16)


def place_rows(states, target, row_count):
    placing = (jnp.arange(row_count, dtype=jnp.int32)[:, None] == target[None, :]).astype(
        jnp.bfloat16
    )
    placed = jnp.einsum("ts,sic->tic", placing, states, preferred_element_type=jnp.float32)
    return placed.astype(jnp.bfloat16)


def local(
    se_streams, mr_gates, se_feat, se_filter, mr_feat, mr_filter, mr_skip, req_ends, decode_row
):
    tok_rows = se_streams.shape[0]
    channels = mr_gates.shape[1] // 2
    shards = lax.axis_size("seq")
    device = lax.axis_index("seq")
    offset = device * tok_rows
    reach_rows = se_feat.shape[0] - 1
    tap_count = mr_filter.shape[0]
    tail_len = tap_count - 1
    group_ch = channels // se_filter.shape[1]
    total_req = req_ends.shape[0]
    slot_total = ENDS_MAX + 1
    rim_depth = 2 * reach_rows
    prev_se, prev_mr = passed_along(
        (se_streams[tok_rows - 3 * reach_rows :], mr_gates[tok_rows - reach_rows :]), "seq", 1
    )
    se_halo = jnp.pad(prev_se, ((HALO - 3 * reach_rows, 0), (0, 0)))
    mr_halo = jnp.pad(prev_mr, ((HALO - reach_rows, 0), (0, 0)))
    ext_pos = offset - HALO + jnp.arange(tok_rows + HALO, dtype=jnp.int32)
    dist = (ext_pos - seg_start(ext_pos, req_ends))[:, None]
    z_two, q_two = short_chain(
        dist,
        se_streams,
        se_halo,
        mr_gates,
        mr_halo,
        se_feat.astype(jnp.float32),
        jnp.repeat(se_filter, group_ch, axis=1).astype(jnp.float32),
        mr_feat.astype(jnp.float32),
        shards,
    )
    prev_z = passed_along(z_two[:, tok_rows - tap_count :], "seq", 1)
    received = lax.all_to_all(z_two, "seq", split_axis=0, concat_axis=0, tiled=True)
    tgt_pos = offset + jnp.arange(tok_rows, dtype=jnp.int32)
    tss = seg_start(tgt_pos, req_ends)[:, None]
    spos = (offset - tap_count + jnp.arange(tok_rows + tap_count, dtype=jnp.int32))[None, :]
    filt_t = mr_filter[::-1].T.astype(jnp.float32)
    filters = filt_t.shape[0]
    taps_rows = jnp.concatenate(
        [jnp.zeros((filters, 1), jnp.float32), filt_t, jnp.zeros((filters, tap_count - 1), jnp.float32)],
        axis=1,
    )
    hyena_out = long_conv_out(
        tss, spos, prev_z, z_two, q_two, mr_skip.astype(jnp.float32)[None, :], taps_rows
    )
    z_all = received.reshape(shards * tok_rows, received.shape[2])
    z_all = jnp.concatenate([jnp.zeros((tap_count, z_all.shape[1]), z_all.dtype), z_all], axis=0)
    rows_ids = jnp.arange(total_req, dtype=jnp.int32)
    owner = jnp.sum(
        jnp.where(decode_row[None, :] == rows_ids[:, None], rows_ids[None, :], 0), axis=1
    )
    last_pos = pick_entries(req_ends, owner)
    first_pos = jnp.where(owner > 0, pick_entries(req_ends, jnp.maximum(owner - 1, 0)) + 1, 0)
    pieces = jax.vmap(
        lambda begin: lax.dynamic_slice_in_dim(z_all, begin, tail_len, 0)
    )(last_pos - tail_len + 1 + tap_count)
    positions = last_pos[:, None] - tail_len + 1 + jnp.arange(tail_len, dtype=jnp.int32)[None, :]
    inside = positions >= first_pos[:, None]
    tail_cache = jnp.where(inside[:, :, None], pieces, jnp.zeros((), pieces.dtype))
    return (hyena_out, tail_cache)


def solution(mesh):
    placed = (
        P(("groups", "seq"), None),
        P(("groups", "seq"), None),
        P(),
        P(),
        P(),
        P(),
        P(),
        P("groups"),
        P("groups"),
    )
    return jax.shard_map(
        local,
        mesh=mesh,
        in_specs=placed,
        out_specs=(P(("groups", "seq"), None), P("groups", None, "seq")),
        check_vma=False,
    )
```

```python
import jax
import jax.numpy as jnp
from jax import lax
from jax.sharding import PartitionSpec as P
from jax.experimental import pallas as pl
from jax.experimental.pallas import tpu as pltpu

ENDS_MAX = 4


def passed_along(x, axis, by):
    length = lax.axis_size(axis)
    pairs = [(i, i + by) for i in range(length) if 0 <= i + by < length]
    return lax.ppermute(x, axis, pairs)


def request_of(positions, req_ends):
    return jnp.sum((req_ends[None, :] < positions[:, None]).astype(jnp.int32), axis=1)


def short_conv(values, weights, segment):
    length = weights.shape[0]
    out_count = values.shape[0] - length + 1
    latest = length - 1
    current = segment[latest:]
    summed = values[latest:].astype(jnp.float32) * weights[0].astype(jnp.float32)
    for lag_step in range(1, length):
        earlier = values[latest - lag_step : latest - lag_step + out_count].astype(jnp.float32)
        same_req = segment[latest - lag_step : latest - lag_step + out_count] == current
        summed = summed + jnp.where(
            same_req[:, None], earlier * weights[lag_step].astype(jnp.float32), 0.0
        )
    return summed


HALO = 32
TILE = 512
GROUP_LANES = 128
WINDOW = 144


def short_conv_rows(x, w, first, dist_ref):
    rows = x.shape[0]
    dist = dist_ref[first:rows, :]
    acc = x[first:rows, :] * w[0:1, :].astype(jnp.float32)
    for lag in range(1, w.shape[0]):
        term = x[first - lag : rows - lag, :] * w[lag : lag + 1, :].astype(jnp.float32)
        acc = acc + jnp.where(dist >= lag, term, 0.0)
    return acc


def chain_kernel(dist_ref, sq, sk, sv, hq, hk, hv, mk, gk_h, fq, fk, fv, filt, wk, wv,
                 z2_ref, xq, xk, xv, xb, zs, ys):
    rows = xq.shape[0]
    for main, halo, x in ((sq, hq, xq), (sk, hk, xk), (sv, hv, xv), (mk, gk_h, xb)):
        reach = halo.shape[0]
        x[0 : HALO - reach, :] = jnp.zeros((HALO - reach, x.shape[1]), jnp.float32)
        x[HALO - reach : HALO, :] = halo[...].astype(jnp.float32)
        x[HALO:rows, :] = main[...].astype(jnp.float32)

    k1 = short_conv_rows(xk, fk, 16, dist_ref)
    v1 = short_conv_rows(xv, fv, 16, dist_ref)
    zs[16:rows, :] = (k1 * v1).astype(jnp.bfloat16).astype(jnp.float32)
    q1 = short_conv_rows(xq, fq, 24, dist_ref)
    c1 = short_conv_rows(zs, filt, 24, dist_ref)
    ys[24:rows, :] = (q1 * c1).astype(jnp.bfloat16).astype(jnp.float32)
    v2 = short_conv_rows(ys, wv, HALO, dist_ref)
    k2 = short_conv_rows(xb, wk, HALO, dist_ref)
    z2 = (k2 * v2).astype(jnp.bfloat16)
    chunk = z2_ref.shape[2]
    for i in range(z2_ref.shape[0]):
        z2_ref[i] = z2[:, i * chunk : (i + 1) * chunk]


def short_chain(dist, se_streams, se_halo, mr_gates, mr_halo, se_feat, se_filt, mr_feat, shards):
    tok_rows = se_streams.shape[0]
    channels = mr_gates.shape[1] // 2
    steps = channels // TILE
    rows = tok_rows + HALO
    taps = se_feat.shape[0]
    chunk = channels // shards

    def col(part):
        return lambda j: (0, j + part * steps)

    main = [pl.BlockSpec((tok_rows, TILE), col(p)) for p in range(3)]
    halo = [pl.BlockSpec((se_halo.shape[0], TILE), col(p)) for p in range(3)]
    mhalo = pl.BlockSpec((mr_halo.shape[0], TILE), col(1))
    wts = [pl.BlockSpec((taps, TILE), col(p)) for p in range(3)]
    return pl.pallas_call(
        chain_kernel,
        grid=(steps,),
        in_specs=[pl.BlockSpec((rows, 1), lambda j: (0, 0))] + main + halo + [main[1], mhalo] + wts
        + [wts[0], wts[1], wts[2]],
        out_specs=pl.BlockSpec((TILE // chunk, tok_rows, chunk), lambda j: (j, 0, 0)),
        out_shape=jax.ShapeDtypeStruct((shards, tok_rows, chunk), jnp.bfloat16),
        scratch_shapes=[pltpu.VMEM((rows, TILE), jnp.float32) for _ in range(6)],
    )(dist, se_streams, se_streams, se_streams, se_halo, se_halo, se_halo, mr_gates,
      mr_halo, se_feat, se_feat, se_feat, se_filt, mr_feat, mr_feat)


def long_kernel(dist_ref, tss_ref, spos_ref, mg_ref, mh_ref, wq_ref, prev_ref, z_ref, skip_ref, u_ref,
                out_ref, xa):
    rows = xa.shape[0]
    reach = mh_ref.shape[0]
    xa[HALO - reach : HALO, :] = mh_ref[...].astype(jnp.float32)
    xa[HALO:rows, :] = mg_ref[...].astype(jnp.float32)
    q2 = short_conv_rows(xa, wq_ref, HALO, dist_ref)
    blk = prev_ref.shape[1]
    tile = z_ref.shape[2]
    width = u_ref.shape[1]
    per_group = tile // u_ref.shape[0]
    z = z_ref[0]
    windows = (jnp.concatenate([prev_ref[0], z[:blk]], axis=0), z)
    masks = [
        spos_ref[:, b * blk : b * blk + width] >= tss_ref[b * blk : (b + 1) * blk, :] for b in range(2)
    ]
    lane_grp = lax.broadcasted_iota(jnp.int32, (1, GROUP_LANES), 1) // per_group
    halves = tile // GROUP_LANES
    groups_half = GROUP_LANES // per_group
    acc = [[jnp.zeros((blk, GROUP_LANES), jnp.float32) for _ in range(halves)] for _ in range(2)]
    for g in range(u_ref.shape[0]):
        half = g // groups_half
        row = jnp.broadcast_to(u_ref[g : g + 1, :], (blk, width))
        taps = pltpu.roll(row, 0, 1, stride=1, stride_axis=0)
        for b in range(2):
            mat = jnp.where(masks[b], taps, 0.0).astype(jnp.bfloat16)
            part = windows[b][:, half * GROUP_LANES : (half + 1) * GROUP_LANES]
            res = jnp.dot(mat, part, preferred_element_type=jnp.float32)
            acc[b][half] = jnp.where(lane_grp == g % groups_half, res, acc[b][half])
    conv = jnp.concatenate([jnp.concatenate(acc[b], axis=1) for b in range(2)], axis=0)
    mixed = (conv + skip_ref[...].astype(jnp.float32) * z.astype(jnp.float32)).astype(jnp.bfloat16)
    out_ref[...] = (q2 * mixed.astype(jnp.float32)).astype(jnp.bfloat16)


def long_conv_out(dist, tss, spos, mr_gates, mr_halo, mr_feat, prev_z, z_two, skip, taps_rows):
    steps, tok_rows, lanes = z_two.shape
    channels = steps * lanes
    blk = prev_z.shape[1]
    per_group = channels // taps_rows.shape[0]
    return pl.pallas_call(
        long_kernel,
        grid=(steps,),
        in_specs=[
            pl.BlockSpec(dist.shape, lambda j: (0, 0)),
            pl.BlockSpec(tss.shape, lambda j: (0, 0)),
            pl.BlockSpec(spos.shape, lambda j: (0, 0)),
            pl.BlockSpec((tok_rows, lanes), lambda j: (0, j)),
            pl.BlockSpec((mr_halo.shape[0], lanes), lambda j: (0, j)),
            pl.BlockSpec((mr_feat.shape[0], lanes), lambda j: (0, j)),
            pl.BlockSpec((1, blk, lanes), lambda j: (j, 0, 0)),
            pl.BlockSpec((1, tok_rows, lanes), lambda j: (j, 0, 0)),
            pl.BlockSpec((1, lanes), lambda j: (0, j)),
            pl.BlockSpec((lanes // per_group, taps_rows.shape[1]), lambda j: (j, 0)),
        ],
        out_specs=pl.BlockSpec((tok_rows, lanes), lambda j: (0, j)),
        out_shape=jax.ShapeDtypeStruct((tok_rows, channels), jnp.bfloat16),
        scratch_shapes=[pltpu.VMEM((tok_rows + HALO, lanes), jnp.float32)],
    )(dist, tss, spos, mr_gates, mr_halo, mr_feat, prev_z, z_two, skip, taps_rows)


def tail_kernel(begin_ref, first_ref, z_ref, out_ref):
    t = pl.program_id(0)
    begin = begin_ref[t]
    total = z_ref.shape[0]
    tail_len = out_ref.shape[1]
    start = jnp.clip((begin // 16) * 16, 0, total - WINDOW)
    shift = begin - start
    window = z_ref[pl.ds(pl.multiple_of(start, 16), WINDOW), :].astype(jnp.float32)
    moved = pltpu.roll(window, (WINDOW - shift) % WINDOW, 0)[:tail_len]
    pos = begin + lax.broadcasted_iota(jnp.int32, (tail_len, 1), 0)
    out_ref[0] = jnp.where(pos >= first_ref[t], moved, 0.0).astype(out_ref.dtype)


def cut_tails_all(z_all, begins, firsts, tail_len):
    total, lanes = z_all.shape
    count = begins.shape[0]
    return pl.pallas_call(
        tail_kernel,
        grid_spec=pltpu.PrefetchScalarGridSpec(
            num_scalar_prefetch=2,
            grid=(count,),
            in_specs=[pl.BlockSpec((total, lanes), lambda t, b, f: (0, 0))],
            out_specs=pl.BlockSpec((1, tail_len, lanes), lambda t, b, f: (t, 0, 0)),
        ),
        out_shape=jax.ShapeDtypeStruct((count, tail_len, lanes), z_all.dtype),
    )(begins, firsts, z_all)


def seg_start(positions, req_ends):
    seg = request_of(positions, req_ends)
    prev_end = jnp.where(seg > 0, pick_entries(req_ends, jnp.maximum(seg - 1, 0)), -1)
    return prev_end + 1


def pick_entries(lookup_table, indices):
    hits = indices[:, None] == jnp.arange(lookup_table.shape[0], dtype=jnp.int32)[None, :]
    return jnp.sum(jnp.where(hits, lookup_table[None, :], 0), axis=1)


def local(
    se_streams, mr_gates, se_feat, se_filter, mr_feat, mr_filter, mr_skip, req_ends, decode_row
):
    tok_rows = se_streams.shape[0]
    channels = mr_gates.shape[1] // 2
    shards = lax.axis_size("seq")
    device = lax.axis_index("seq")
    offset = device * tok_rows
    reach_rows = se_feat.shape[0] - 1
    tap_count = mr_filter.shape[0]
    tail_len = tap_count - 1
    group_ch = channels // se_filter.shape[1]
    total_req = req_ends.shape[0]
    slot_total = ENDS_MAX + 1
    rim_depth = 2 * reach_rows
    prev_se, prev_mr = passed_along(
        (se_streams[tok_rows - 3 * reach_rows :], mr_gates[tok_rows - reach_rows :]), "seq", 1
    )
    ext_pos = offset - HALO + jnp.arange(tok_rows + HALO, dtype=jnp.int32)
    dist = (ext_pos - seg_start(ext_pos, req_ends))[:, None]
    z_two = short_chain(
        dist,
        se_streams,
        prev_se,
        mr_gates,
        prev_mr,
        se_feat,
        jnp.repeat(se_filter, group_ch, axis=1),
        mr_feat,
        shards,
    )
    prev_z = passed_along(z_two[:, tok_rows - tap_count :], "seq", 1)
    received = lax.all_to_all(z_two, "seq", split_axis=0, concat_axis=0, tiled=True)
    tgt_pos = offset + jnp.arange(tok_rows, dtype=jnp.int32)
    tss = seg_start(tgt_pos, req_ends)[:, None]
    spos = (offset - tap_count + jnp.arange(tok_rows + tap_count, dtype=jnp.int32))[None, :]
    filt_t = mr_filter[::-1].T.astype(jnp.float32)
    filters = filt_t.shape[0]
    taps_rows = jnp.concatenate(
        [jnp.zeros((filters, 1), jnp.float32), filt_t, jnp.zeros((filters, tap_count - 1), jnp.float32)],
        axis=1,
    )
    hyena_out = long_conv_out(
        dist, tss, spos, mr_gates, prev_mr, mr_feat, prev_z, z_two, mr_skip[None, :], taps_rows
    )
    z_all = received.reshape(shards * tok_rows, received.shape[2])
    rows_ids = jnp.arange(total_req, dtype=jnp.int32)
    owner = jnp.sum(
        jnp.where(decode_row[None, :] == rows_ids[:, None], rows_ids[None, :], 0), axis=1
    )
    last_pos = pick_entries(req_ends, owner)
    first_pos = jnp.where(owner > 0, pick_entries(req_ends, jnp.maximum(owner - 1, 0)) + 1, 0)
    tail_cache = cut_tails_all(z_all, last_pos - tail_len + 1, first_pos, tail_len)
    return (hyena_out, tail_cache)


def solution(mesh):
    placed = (
        P(("groups", "seq"), None),
        P(("groups", "seq"), None),
        P(),
        P(),
        P(),
        P(),
        P(),
        P("groups"),
        P("groups"),
    )
    return jax.shard_map(
        local,
        mesh=mesh,
        in_specs=placed,
        out_specs=(P(("groups", "seq"), None), P("groups", None, "seq")),
        check_vma=False,
    )
```

```python
import jax
import jax.numpy as jnp
from jax import lax
from jax.sharding import PartitionSpec as P
from jax.experimental import pallas as pl
from jax.experimental.pallas import tpu as pltpu

ENDS_MAX = 4


def passed_along(x, axis, by):
    length = lax.axis_size(axis)
    pairs = [(i, i + by) for i in range(length) if 0 <= i + by < length]
    return lax.ppermute(x, axis, pairs)


def request_of(positions, req_ends):
    return jnp.sum((req_ends[None, :] < positions[:, None]).astype(jnp.int32), axis=1)


def short_conv(values, weights, segment):
    length = weights.shape[0]
    out_count = values.shape[0] - length + 1
    latest = length - 1
    current = segment[latest:]
    summed = values[latest:].astype(jnp.float32) * weights[0].astype(jnp.float32)
    for lag_step in range(1, length):
        earlier = values[latest - lag_step : latest - lag_step + out_count].astype(jnp.float32)
        same_req = segment[latest - lag_step : latest - lag_step + out_count] == current
        summed = summed + jnp.where(
            same_req[:, None], earlier * weights[lag_step].astype(jnp.float32), 0.0
        )
    return summed


HALO = 32
TILE = 512
GROUP_LANES = 128
WINDOW = 144


def short_conv_rows(x, w, first, dist_ref):
    rows = x.shape[0]
    dist = dist_ref[first:rows, :]
    acc = x[first:rows, :] * w[0:1, :].astype(jnp.float32)
    for lag in range(1, w.shape[0]):
        term = x[first - lag : rows - lag, :] * w[lag : lag + 1, :].astype(jnp.float32)
        acc = acc + jnp.where(dist >= lag, term, 0.0)
    return acc


def chain_kernel(dist_ref, sq, sk, sv, hq, hk, hv, mk, gk_h, fq, fk, fv, filt, wk, wv,
                 z2_ref, xq, xk, xv, xb, zs, ys):
    rows = xq.shape[0]
    for main, halo, x in ((sq, hq, xq), (sk, hk, xk), (sv, hv, xv), (mk, gk_h, xb)):
        reach = halo.shape[0]
        if reach < HALO:
            x[0 : HALO - reach, :] = jnp.zeros((HALO - reach, x.shape[1]), jnp.float32)
        x[HALO - reach : HALO, :] = halo[...].astype(jnp.float32)
        x[HALO:rows, :] = main[...].astype(jnp.float32)

    k1 = short_conv_rows(xk, fk, 16, dist_ref)
    v1 = short_conv_rows(xv, fv, 16, dist_ref)
    zs[16:rows, :] = (k1 * v1).astype(jnp.bfloat16).astype(jnp.float32)
    q1 = short_conv_rows(xq, fq, 24, dist_ref)
    c1 = short_conv_rows(zs, filt, 24, dist_ref)
    ys[24:rows, :] = (q1 * c1).astype(jnp.bfloat16).astype(jnp.float32)
    v2 = short_conv_rows(ys, wv, HALO, dist_ref)
    k2 = short_conv_rows(xb, wk, HALO, dist_ref)
    z2 = (k2 * v2).astype(jnp.bfloat16)
    chunk = z2_ref.shape[2]
    for i in range(z2_ref.shape[0]):
        z2_ref[i] = z2[:, i * chunk : (i + 1) * chunk]


def short_chain(dist, se_streams, se_halo, mr_gates, mr_halo, se_feat, se_filt, mr_feat, shards, half):
    tok_rows = dist.shape[0] - HALO
    channels = mr_gates.shape[1] // 2
    steps = channels // TILE
    rows = tok_rows + HALO
    taps = se_feat.shape[0]
    chunk = channels // shards

    def col(part, row_block=half):
        return lambda j: (row_block, j + part * steps)

    def halo_spec(halo, part):
        if halo.shape[0] < HALO:
            return pl.BlockSpec((halo.shape[0], TILE), col(part, 0))
        return pl.BlockSpec((HALO, TILE), col(part, half * tok_rows // HALO - 1))

    main = [pl.BlockSpec((tok_rows, TILE), col(p)) for p in range(3)]
    halo = [halo_spec(se_halo, p) for p in range(3)]
    wts = [pl.BlockSpec((taps, TILE), col(p, 0)) for p in range(3)]
    return pl.pallas_call(
        chain_kernel,
        grid=(steps,),
        in_specs=[pl.BlockSpec((rows, 1), lambda j: (0, 0))] + main + halo
        + [main[1], halo_spec(mr_halo, 1)] + wts + [wts[0], wts[1], wts[2]],
        out_specs=pl.BlockSpec((TILE // chunk, tok_rows, chunk), lambda j: (j, 0, 0)),
        out_shape=jax.ShapeDtypeStruct((shards, tok_rows, chunk), jnp.bfloat16),
        scratch_shapes=[pltpu.VMEM((rows, TILE), jnp.float32) for _ in range(6)],
    )(dist, se_streams, se_streams, se_streams, se_halo, se_halo, se_halo, mr_gates,
      mr_halo, se_feat, se_feat, se_feat, se_filt, mr_feat, mr_feat)


def long_kernel(dist_ref, tss_ref, spos_ref, mg_ref, mh_ref, wq_ref, first_ref, second_ref, skip_ref,
                u_ref, *rest):
    out_ref, xa = rest[-2], rest[-1]
    rows = xa.shape[0]
    reach = mh_ref.shape[0]
    xa[HALO - reach : HALO, :] = mh_ref[...].astype(jnp.float32)
    xa[HALO:rows, :] = mg_ref[...].astype(jnp.float32)
    q2 = short_conv_rows(xa, wq_ref, HALO, dist_ref)
    blk = second_ref.shape[1]
    tile = second_ref.shape[2]
    width = u_ref.shape[1]
    per_group = tile // u_ref.shape[0]
    z = second_ref[0]
    window = jnp.concatenate([first_ref[0], z], axis=0)
    mask = spos_ref[...] >= tss_ref[...]
    lane_grp = lax.broadcasted_iota(jnp.int32, (1, GROUP_LANES), 1) // per_group
    halves = tile // GROUP_LANES
    groups_half = GROUP_LANES // per_group
    acc = [jnp.zeros((blk, GROUP_LANES), jnp.float32) for _ in range(halves)]
    for g in range(u_ref.shape[0]):
        half = g // groups_half
        row = jnp.broadcast_to(u_ref[g : g + 1, :], (blk, width))
        taps = pltpu.roll(row, 0, 1, stride=1, stride_axis=0)
        mat = jnp.where(mask, taps, 0.0).astype(jnp.bfloat16)
        part = window[:, half * GROUP_LANES : (half + 1) * GROUP_LANES]
        res = jnp.dot(mat, part, preferred_element_type=jnp.float32)
        acc[half] = jnp.where(lane_grp == g % groups_half, res, acc[half])
    conv = jnp.concatenate(acc, axis=1)
    mixed = (conv + skip_ref[...].astype(jnp.float32) * z.astype(jnp.float32)).astype(jnp.bfloat16)
    out_ref[...] = (q2 * mixed.astype(jnp.float32)).astype(jnp.bfloat16)


def long_block(dist, tss, spos, mr_gates, mr_halo, mr_feat, first, second, skip, taps_rows, half,
               out_rows, earlier=None):
    steps, blk, lanes = second.shape
    channels = steps * lanes
    per_group = channels // taps_rows.shape[0]
    if mr_halo.shape[0] < HALO:
        halo_spec = pl.BlockSpec((mr_halo.shape[0], lanes), lambda j: (0, j))
    else:
        halo_spec = pl.BlockSpec((HALO, lanes), lambda j: (half * blk // HALO - 1, j))
    in_specs = [
        pl.BlockSpec(dist.shape, lambda j: (0, 0)),
        pl.BlockSpec(tss.shape, lambda j: (0, 0)),
        pl.BlockSpec(spos.shape, lambda j: (0, 0)),
        pl.BlockSpec((blk, lanes), lambda j: (half, j)),
        halo_spec,
        pl.BlockSpec((mr_feat.shape[0], lanes), lambda j: (0, j)),
        pl.BlockSpec((1, blk, lanes), lambda j: (j, 0, 0)),
        pl.BlockSpec((1, blk, lanes), lambda j: (j, 0, 0)),
        pl.BlockSpec((1, lanes), lambda j: (0, j)),
        pl.BlockSpec((lanes // per_group, taps_rows.shape[1]), lambda j: (j, 0)),
    ]
    args = [dist, tss, spos, mr_gates, mr_halo, mr_feat, first, second, skip, taps_rows]
    aliases = {}
    if earlier is not None:
        in_specs.append(pl.BlockSpec(memory_space=pl.ANY))
        aliases = {len(args): 0}
        args.append(earlier)
    return pl.pallas_call(
        long_kernel,
        grid=(steps,),
        in_specs=in_specs,
        out_specs=pl.BlockSpec((blk, lanes), lambda j: (half, j)),
        out_shape=jax.ShapeDtypeStruct((out_rows, channels), jnp.bfloat16),
        scratch_shapes=[pltpu.VMEM((blk + HALO, lanes), jnp.float32)],
        input_output_aliases=aliases,
    )(*args)


def tail_kernel(begin_ref, first_ref, z_ref, out_ref):
    t = pl.program_id(0)
    begin = begin_ref[t]
    total = z_ref.shape[0]
    tail_len = out_ref.shape[1]
    start = jnp.clip((begin // 16) * 16, 0, total - WINDOW)
    shift = begin - start
    window = z_ref[pl.ds(pl.multiple_of(start, 16), WINDOW), :].astype(jnp.float32)
    moved = pltpu.roll(window, (WINDOW - shift) % WINDOW, 0)[:tail_len]
    pos = begin + lax.broadcasted_iota(jnp.int32, (tail_len, 1), 0)
    out_ref[0] = jnp.where(pos >= first_ref[t], moved, 0.0).astype(out_ref.dtype)


def cut_tails_all(z_all, begins, firsts, tail_len):
    total, lanes = z_all.shape
    count = begins.shape[0]
    return pl.pallas_call(
        tail_kernel,
        grid_spec=pltpu.PrefetchScalarGridSpec(
            num_scalar_prefetch=2,
            grid=(count,),
            in_specs=[pl.BlockSpec((total, lanes), lambda t, b, f: (0, 0))],
            out_specs=pl.BlockSpec((1, tail_len, lanes), lambda t, b, f: (t, 0, 0)),
        ),
        out_shape=jax.ShapeDtypeStruct((count, tail_len, lanes), z_all.dtype),
    )(begins, firsts, z_all)


def seg_start(positions, req_ends):
    seg = request_of(positions, req_ends)
    prev_end = jnp.where(seg > 0, pick_entries(req_ends, jnp.maximum(seg - 1, 0)), -1)
    return prev_end + 1


def pick_entries(lookup_table, indices):
    hits = indices[:, None] == jnp.arange(lookup_table.shape[0], dtype=jnp.int32)[None, :]
    return jnp.sum(jnp.where(hits, lookup_table[None, :], 0), axis=1)


def local(
    se_streams, mr_gates, se_feat, se_filter, mr_feat, mr_filter, mr_skip, req_ends, decode_row
):
    tok_rows = se_streams.shape[0]
    channels = mr_gates.shape[1] // 2
    shards = lax.axis_size("seq")
    device = lax.axis_index("seq")
    offset = device * tok_rows
    reach_rows = se_feat.shape[0] - 1
    tap_count = mr_filter.shape[0]
    tail_len = tap_count - 1
    group_ch = channels // se_filter.shape[1]
    total_req = req_ends.shape[0]
    slot_total = ENDS_MAX + 1
    rim_depth = 2 * reach_rows
    prev_se, prev_mr = passed_along(
        (se_streams[tok_rows - 3 * reach_rows :], mr_gates[tok_rows - reach_rows :]), "seq", 1
    )
    blk = tok_rows // 2
    se_filt = jnp.repeat(se_filter, group_ch, axis=1)

    def dist_of(half):
        ext_pos = offset + half * blk - HALO + jnp.arange(blk + HALO, dtype=jnp.int32)
        return (ext_pos - seg_start(ext_pos, req_ends))[:, None]

    dists = [dist_of(0), dist_of(1)]
    z_hi = short_chain(
        dists[1], se_streams, se_streams, mr_gates, mr_gates, se_feat, se_filt, mr_feat, shards, 1
    )
    prev_z = passed_along(z_hi, "seq", 1)
    z_hi, prev_se, prev_mr = lax.optimization_barrier((z_hi, prev_se, prev_mr))
    recv_hi = lax.all_to_all(z_hi, "seq", split_axis=0, concat_axis=0, tiled=True)
    z_lo = short_chain(
        dists[0], se_streams, prev_se, mr_gates, prev_mr, se_feat, se_filt, mr_feat, shards, 0
    )
    recv_lo = lax.all_to_all(z_lo, "seq", split_axis=0, concat_axis=0, tiled=True)
    filt_t = mr_filter[::-1].T.astype(jnp.float32)
    filters = filt_t.shape[0]
    taps_rows = jnp.concatenate(
        [jnp.zeros((filters, 1), jnp.float32), filt_t, jnp.zeros((filters, tap_count - 1), jnp.float32)],
        axis=1,
    )

    def masks_of(half):
        tgt = offset + half * blk + jnp.arange(blk, dtype=jnp.int32)
        src = (offset + half * blk - blk + jnp.arange(2 * blk, dtype=jnp.int32))[None, :]
        return seg_start(tgt, req_ends)[:, None], src

    tss1, spos1 = masks_of(1)
    part = long_block(
        dists[1], tss1, spos1, mr_gates, mr_gates, mr_feat, z_lo, z_hi, mr_skip[None, :], taps_rows,
        1, tok_rows,
    )
    tss0, spos0 = masks_of(0)
    hyena_out = long_block(
        dists[0], tss0, spos0, mr_gates, prev_mr, mr_feat, prev_z, z_lo, mr_skip[None, :], taps_rows,
        0, tok_rows, part,
    )
    received = jnp.stack([recv_lo, recv_hi], axis=1)
    z_all = received.reshape(shards * tok_rows, received.shape[3])
    rows_ids = jnp.arange(total_req, dtype=jnp.int32)
    owner = jnp.sum(
        jnp.where(decode_row[None, :] == rows_ids[:, None], rows_ids[None, :], 0), axis=1
    )
    last_pos = pick_entries(req_ends, owner)
    first_pos = jnp.where(owner > 0, pick_entries(req_ends, jnp.maximum(owner - 1, 0)) + 1, 0)
    tail_cache = cut_tails_all(z_all, last_pos - tail_len + 1, first_pos, tail_len)
    return (hyena_out, tail_cache)


def solution(mesh):
    placed = (
        P(("groups", "seq"), None),
        P(("groups", "seq"), None),
        P(),
        P(),
        P(),
        P(),
        P(),
        P("groups"),
        P("groups"),
    )
    return jax.shard_map(
        local,
        mesh=mesh,
        in_specs=placed,
        out_specs=(P(("groups", "seq"), None), P("groups", None, "seq")),
        check_vma=False,
    )
```

```python
import jax
import jax.numpy as jnp
from jax import lax
from jax.sharding import PartitionSpec as P
from jax.experimental import pallas as pl
from jax.experimental.pallas import tpu as pltpu

ENDS_MAX = 4


def passed_along(x, axis, by):
    length = lax.axis_size(axis)
    pairs = [(i, i + by) for i in range(length) if 0 <= i + by < length]
    return lax.ppermute(x, axis, pairs)


def request_of(positions, req_ends):
    return jnp.sum((req_ends[None, :] < positions[:, None]).astype(jnp.int32), axis=1)


def short_conv(values, weights, segment):
    length = weights.shape[0]
    out_count = values.shape[0] - length + 1
    latest = length - 1
    current = segment[latest:]
    summed = values[latest:].astype(jnp.float32) * weights[0].astype(jnp.float32)
    for lag_step in range(1, length):
        earlier = values[latest - lag_step : latest - lag_step + out_count].astype(jnp.float32)
        same_req = segment[latest - lag_step : latest - lag_step + out_count] == current
        summed = summed + jnp.where(
            same_req[:, None], earlier * weights[lag_step].astype(jnp.float32), 0.0
        )
    return summed


HALO = 32
TILE = 512
GROUP_LANES = 128
WINDOW = 144


def short_conv_rows(x, w, first, dist_ref):
    rows = x.shape[0]
    dist = dist_ref[first:rows, :]
    acc = x[first:rows, :] * w[0:1, :].astype(jnp.float32)
    for lag in range(1, w.shape[0]):
        term = x[first - lag : rows - lag, :] * w[lag : lag + 1, :].astype(jnp.float32)
        acc = acc + jnp.where(dist >= lag, term, 0.0)
    return acc


def chain_kernel(dist_ref, sq, sk, sv, hq, hk, hv, mk, gk_h, fq, fk, fv, filt, wk, wv,
                 z2_ref, xq, xk, xv, xb, zs, ys):
    rows = xq.shape[0]
    for main, halo, x in ((sq, hq, xq), (sk, hk, xk), (sv, hv, xv), (mk, gk_h, xb)):
        reach = halo.shape[0]
        if reach < HALO:
            x[0 : HALO - reach, :] = jnp.zeros((HALO - reach, x.shape[1]), jnp.float32)
        x[HALO - reach : HALO, :] = halo[...].astype(jnp.float32)
        x[HALO:rows, :] = main[...].astype(jnp.float32)

    k1 = short_conv_rows(xk, fk, 16, dist_ref)
    v1 = short_conv_rows(xv, fv, 16, dist_ref)
    zs[16:rows, :] = (k1 * v1).astype(jnp.bfloat16).astype(jnp.float32)
    q1 = short_conv_rows(xq, fq, 24, dist_ref)
    c1 = short_conv_rows(zs, filt, 24, dist_ref)
    ys[24:rows, :] = (q1 * c1).astype(jnp.bfloat16).astype(jnp.float32)
    v2 = short_conv_rows(ys, wv, HALO, dist_ref)
    k2 = short_conv_rows(xb, wk, HALO, dist_ref)
    z2 = (k2 * v2).astype(jnp.bfloat16)
    chunk = z2_ref.shape[2]
    for i in range(z2_ref.shape[0]):
        z2_ref[i] = z2[:, i * chunk : (i + 1) * chunk]


def short_chain(dist, se_streams, se_halo, mr_gates, mr_halo, se_feat, se_filt, mr_feat, shards, half):
    tok_rows = dist.shape[0] - HALO
    channels = mr_gates.shape[1] // 2
    steps = channels // TILE
    rows = tok_rows + HALO
    taps = se_feat.shape[0]
    chunk = channels // shards

    def col(part, row_block=half):
        return lambda j: (row_block, j + part * steps)

    def halo_spec(halo, part):
        if halo.shape[0] < HALO:
            return pl.BlockSpec((halo.shape[0], TILE), col(part, 0))
        return pl.BlockSpec((HALO, TILE), col(part, half * tok_rows // HALO - 1))

    main = [pl.BlockSpec((tok_rows, TILE), col(p)) for p in range(3)]
    halo = [halo_spec(se_halo, p) for p in range(3)]
    wts = [pl.BlockSpec((taps, TILE), col(p, 0)) for p in range(3)]
    return pl.pallas_call(
        chain_kernel,
        grid=(steps,),
        in_specs=[pl.BlockSpec((rows, 1), lambda j: (0, 0))] + main + halo
        + [main[1], halo_spec(mr_halo, 1)] + wts + [wts[0], wts[1], wts[2]],
        out_specs=pl.BlockSpec((TILE // chunk, tok_rows, chunk), lambda j: (j, 0, 0)),
        out_shape=jax.ShapeDtypeStruct((shards, tok_rows, chunk), jnp.bfloat16),
        scratch_shapes=[pltpu.VMEM((rows, TILE), jnp.float32) for _ in range(6)],
    )(dist, se_streams, se_streams, se_streams, se_halo, se_halo, se_halo, mr_gates,
      mr_halo, se_feat, se_feat, se_feat, se_filt, mr_feat, mr_feat)


def long_kernel(dist_ref, tss_ref, spos_ref, mg_ref, mh_ref, wq_ref, prev_ref, lo_ref, hi_ref, skip_ref,
                u_ref, out_ref, xa):
    rows = xa.shape[0]
    reach = mh_ref.shape[0]
    xa[HALO - reach : HALO, :] = mh_ref[...].astype(jnp.float32)
    xa[HALO:rows, :] = mg_ref[...].astype(jnp.float32)
    q2 = short_conv_rows(xa, wq_ref, HALO, dist_ref)
    blk = lo_ref.shape[1]
    tile = lo_ref.shape[2]
    width = u_ref.shape[1]
    per_group = tile // u_ref.shape[0]
    lo = lo_ref[0]
    hi = hi_ref[0]
    windows = (jnp.concatenate([prev_ref[0], lo], axis=0), jnp.concatenate([lo, hi], axis=0))
    masks = [
        spos_ref[:, b * blk : b * blk + width] >= tss_ref[b * blk : (b + 1) * blk, :] for b in range(2)
    ]
    lane_grp = lax.broadcasted_iota(jnp.int32, (1, GROUP_LANES), 1) // per_group
    halves = tile // GROUP_LANES
    groups_half = GROUP_LANES // per_group
    acc = [[jnp.zeros((blk, GROUP_LANES), jnp.float32) for _ in range(halves)] for _ in range(2)]
    for g in range(u_ref.shape[0]):
        half = g // groups_half
        row = jnp.broadcast_to(u_ref[g : g + 1, :], (blk, width))
        taps = pltpu.roll(row, 0, 1, stride=1, stride_axis=0)
        for b in range(2):
            mat = jnp.where(masks[b], taps, 0.0).astype(jnp.bfloat16)
            part = windows[b][:, half * GROUP_LANES : (half + 1) * GROUP_LANES]
            res = jnp.dot(mat, part, preferred_element_type=jnp.float32)
            acc[b][half] = jnp.where(lane_grp == g % groups_half, res, acc[b][half])
    conv = jnp.concatenate([jnp.concatenate(acc[b], axis=1) for b in range(2)], axis=0)
    z = jnp.concatenate([lo, hi], axis=0).astype(jnp.float32)
    mixed = (conv + skip_ref[...].astype(jnp.float32) * z).astype(jnp.bfloat16)
    out_ref[...] = (q2 * mixed.astype(jnp.float32)).astype(jnp.bfloat16)


def long_conv_out(dist, tss, spos, mr_gates, mr_halo, mr_feat, prev_z, z_lo, z_hi, skip, taps_rows):
    steps, blk, lanes = z_lo.shape
    tok_rows = 2 * blk
    channels = steps * lanes
    per_group = channels // taps_rows.shape[0]
    piece = pl.BlockSpec((1, blk, lanes), lambda j: (j, 0, 0))
    return pl.pallas_call(
        long_kernel,
        grid=(steps,),
        in_specs=[
            pl.BlockSpec(dist.shape, lambda j: (0, 0)),
            pl.BlockSpec(tss.shape, lambda j: (0, 0)),
            pl.BlockSpec(spos.shape, lambda j: (0, 0)),
            pl.BlockSpec((tok_rows, lanes), lambda j: (0, j)),
            pl.BlockSpec((mr_halo.shape[0], lanes), lambda j: (0, j)),
            pl.BlockSpec((mr_feat.shape[0], lanes), lambda j: (0, j)),
            piece,
            piece,
            piece,
            pl.BlockSpec((1, lanes), lambda j: (0, j)),
            pl.BlockSpec((lanes // per_group, taps_rows.shape[1]), lambda j: (j, 0)),
        ],
        out_specs=pl.BlockSpec((tok_rows, lanes), lambda j: (0, j)),
        out_shape=jax.ShapeDtypeStruct((tok_rows, channels), jnp.bfloat16),
        scratch_shapes=[pltpu.VMEM((tok_rows + HALO, lanes), jnp.float32)],
    )(dist, tss, spos, mr_gates, mr_halo, mr_feat, prev_z, z_lo, z_hi, skip, taps_rows)


def tail_kernel(begin_ref, first_ref, lo_ref, hi_ref, out_ref, z_all):
    shards, blk, lanes = lo_ref.shape
    tail_len = out_ref.shape[0]
    total = z_all.shape[0]
    for src in range(shards):
        z_all[2 * src * blk : (2 * src + 1) * blk, :] = lo_ref[src].astype(jnp.float32)
        z_all[(2 * src + 1) * blk : (2 * src + 2) * blk, :] = hi_ref[src].astype(jnp.float32)
    for t in range(out_ref.shape[1]):
        begin = begin_ref[t]
        start = jnp.clip((begin // 16) * 16, 0, total - WINDOW)
        shift = begin - start
        window = z_all[pl.ds(pl.multiple_of(start, 16), WINDOW), :]
        moved = pltpu.roll(window, (WINDOW - shift) % WINDOW, 0)[:tail_len]
        pos = begin + lax.broadcasted_iota(jnp.int32, (tail_len, 1), 0)
        out_ref[:, t, :] = jnp.where(pos >= first_ref[t], moved, 0.0).astype(out_ref.dtype)


def cut_tails_all(z_lo, z_hi, begins, firsts, tail_len):
    shards, blk, lanes = z_lo.shape
    count = begins.shape[0]
    smem = pl.BlockSpec(memory_space=pltpu.SMEM)
    vmem = pl.BlockSpec(memory_space=pltpu.VMEM)
    out = pl.pallas_call(
        tail_kernel,
        in_specs=[smem, smem, vmem, vmem],
        out_specs=vmem,
        out_shape=jax.ShapeDtypeStruct((tail_len, count, lanes), z_lo.dtype),
        scratch_shapes=[pltpu.VMEM((2 * shards * blk, lanes), jnp.float32)],
    )(begins, firsts, z_lo, z_hi)
    return jnp.transpose(out, (1, 0, 2))


def seg_start(positions, req_ends):
    seg = request_of(positions, req_ends)
    prev_end = jnp.where(seg > 0, pick_entries(req_ends, jnp.maximum(seg - 1, 0)), -1)
    return prev_end + 1


def pick_entries(lookup_table, indices):
    hits = indices[:, None] == jnp.arange(lookup_table.shape[0], dtype=jnp.int32)[None, :]
    return jnp.sum(jnp.where(hits, lookup_table[None, :], 0), axis=1)


def local(
    se_streams, mr_gates, se_feat, se_filter, mr_feat, mr_filter, mr_skip, req_ends, decode_row
):
    tok_rows = se_streams.shape[0]
    channels = mr_gates.shape[1] // 2
    shards = lax.axis_size("seq")
    device = lax.axis_index("seq")
    offset = device * tok_rows
    reach_rows = se_feat.shape[0] - 1
    tap_count = mr_filter.shape[0]
    tail_len = tap_count - 1
    group_ch = channels // se_filter.shape[1]
    total_req = req_ends.shape[0]
    slot_total = ENDS_MAX + 1
    rim_depth = 2 * reach_rows
    prev_se, prev_mr = passed_along(
        (se_streams[tok_rows - 3 * reach_rows :], mr_gates[tok_rows - reach_rows :]), "seq", 1
    )
    blk = tok_rows // 2
    se_filt = jnp.repeat(se_filter, group_ch, axis=1)

    def dist_of(half):
        ext_pos = offset + half * blk - HALO + jnp.arange(blk + HALO, dtype=jnp.int32)
        return (ext_pos - seg_start(ext_pos, req_ends))[:, None]

    dists = [dist_of(0), dist_of(1)]
    z_hi = short_chain(
        dists[1], se_streams, se_streams, mr_gates, mr_gates, se_feat, se_filt, mr_feat, shards, 1
    )
    prev_z = passed_along(z_hi, "seq", 1)
    z_hi, prev_se, prev_mr = lax.optimization_barrier((z_hi, prev_se, prev_mr))
    recv_hi = lax.all_to_all(z_hi, "seq", split_axis=0, concat_axis=0, tiled=True)
    z_lo = short_chain(
        dists[0], se_streams, prev_se, mr_gates, prev_mr, se_feat, se_filt, mr_feat, shards, 0
    )
    z_lo, recv_hi = lax.optimization_barrier((z_lo, recv_hi))
    recv_lo = lax.all_to_all(z_lo, "seq", split_axis=0, concat_axis=0, tiled=True)
    filt_t = mr_filter[::-1].T.astype(jnp.float32)
    filters = filt_t.shape[0]
    taps_rows = jnp.concatenate(
        [jnp.zeros((filters, 1), jnp.float32), filt_t, jnp.zeros((filters, tap_count - 1), jnp.float32)],
        axis=1,
    )

    tgt_pos = offset + jnp.arange(tok_rows, dtype=jnp.int32)
    tss = seg_start(tgt_pos, req_ends)[:, None]
    spos = (offset - blk + jnp.arange(tok_rows + blk, dtype=jnp.int32))[None, :]
    ext_pos = offset - HALO + jnp.arange(tok_rows + HALO, dtype=jnp.int32)
    dist = (ext_pos - seg_start(ext_pos, req_ends))[:, None]
    hyena_out = long_conv_out(
        dist, tss, spos, mr_gates, prev_mr, mr_feat, prev_z, z_lo, z_hi, mr_skip[None, :], taps_rows
    )
    rows_ids = jnp.arange(total_req, dtype=jnp.int32)
    owner = jnp.sum(
        jnp.where(decode_row[None, :] == rows_ids[:, None], rows_ids[None, :], 0), axis=1
    )
    last_pos = pick_entries(req_ends, owner)
    first_pos = jnp.where(owner > 0, pick_entries(req_ends, jnp.maximum(owner - 1, 0)) + 1, 0)
    tail_cache = cut_tails_all(recv_lo, recv_hi, last_pos - tail_len + 1, first_pos, tail_len)
    return (hyena_out, tail_cache)


def solution(mesh):
    placed = (
        P(("groups", "seq"), None),
        P(("groups", "seq"), None),
        P(),
        P(),
        P(),
        P(),
        P(),
        P("groups"),
        P("groups"),
    )
    return jax.shard_map(
        local,
        mesh=mesh,
        in_specs=placed,
        out_specs=(P(("groups", "seq"), None), P("groups", None, "seq")),
        check_vma=False,
    )
```

```python
import jax
import jax.numpy as jnp
from jax import lax
from jax.sharding import PartitionSpec as P
from jax.experimental import pallas as pl
from jax.experimental.pallas import tpu as pltpu

ENDS_MAX = 4


def passed_along(x, axis, by):
    length = lax.axis_size(axis)
    pairs = [(i, i + by) for i in range(length) if 0 <= i + by < length]
    return lax.ppermute(x, axis, pairs)


def request_of(positions, req_ends):
    return jnp.sum((req_ends[None, :] < positions[:, None]).astype(jnp.int32), axis=1)


def short_conv(values, weights, segment):
    length = weights.shape[0]
    out_count = values.shape[0] - length + 1
    latest = length - 1
    current = segment[latest:]
    summed = values[latest:].astype(jnp.float32) * weights[0].astype(jnp.float32)
    for lag_step in range(1, length):
        earlier = values[latest - lag_step : latest - lag_step + out_count].astype(jnp.float32)
        same_req = segment[latest - lag_step : latest - lag_step + out_count] == current
        summed = summed + jnp.where(
            same_req[:, None], earlier * weights[lag_step].astype(jnp.float32), 0.0
        )
    return summed


HALO = 32
TILE = 1024
GROUP_LANES = 128
WINDOW = 144


def short_conv_rows(x, w, first, dist_ref):
    rows = x.shape[0]
    dist = dist_ref[first:rows, :]
    acc = x[first:rows, :] * w[0:1, :].astype(jnp.float32)
    for lag in range(1, w.shape[0]):
        term = x[first - lag : rows - lag, :] * w[lag : lag + 1, :].astype(jnp.float32)
        acc = acc + jnp.where(dist >= lag, term, 0.0)
    return acc


def chain_kernel(dist_ref, sq, sk, sv, hq, hk, hv, mk, gk_h, fq, fk, fv, filt, wk, wv,
                 z2_ref, xq, xk, xv, xb, zs, ys):
    rows = xq.shape[0]
    for main, halo, x in ((sq, hq, xq), (sk, hk, xk), (sv, hv, xv), (mk, gk_h, xb)):
        reach = halo.shape[0]
        if reach < HALO:
            x[0 : HALO - reach, :] = jnp.zeros((HALO - reach, x.shape[1]), jnp.float32)
        x[HALO - reach : HALO, :] = halo[...].astype(jnp.float32)
        x[HALO:rows, :] = main[...].astype(jnp.float32)

    k1 = short_conv_rows(xk, fk, 16, dist_ref)
    v1 = short_conv_rows(xv, fv, 16, dist_ref)
    zs[16:rows, :] = (k1 * v1).astype(jnp.bfloat16).astype(jnp.float32)
    q1 = short_conv_rows(xq, fq, 24, dist_ref)
    c1 = short_conv_rows(zs, filt, 24, dist_ref)
    ys[24:rows, :] = (q1 * c1).astype(jnp.bfloat16).astype(jnp.float32)
    v2 = short_conv_rows(ys, wv, HALO, dist_ref)
    k2 = short_conv_rows(xb, wk, HALO, dist_ref)
    z2 = (k2 * v2).astype(jnp.bfloat16)
    chunk = z2_ref.shape[2]
    for i in range(z2_ref.shape[0]):
        z2_ref[i] = z2[:, i * chunk : (i + 1) * chunk]


def short_chain(dist, se_streams, se_halo, mr_gates, mr_halo, se_feat, se_filt, mr_feat, shards, half):
    tok_rows = dist.shape[0] - HALO
    channels = mr_gates.shape[1] // 2
    steps = channels // TILE
    rows = tok_rows + HALO
    taps = se_feat.shape[0]
    chunk = channels // shards

    def col(part, row_block=half):
        return lambda j: (row_block, j + part * steps)

    def halo_spec(halo, part):
        if halo.shape[0] < HALO:
            return pl.BlockSpec((halo.shape[0], TILE), col(part, 0))
        return pl.BlockSpec((HALO, TILE), col(part, half * tok_rows // HALO - 1))

    main = [pl.BlockSpec((tok_rows, TILE), col(p)) for p in range(3)]
    halo = [halo_spec(se_halo, p) for p in range(3)]
    wts = [pl.BlockSpec((taps, TILE), col(p, 0)) for p in range(3)]
    return pl.pallas_call(
        chain_kernel,
        grid=(steps,),
        in_specs=[pl.BlockSpec((rows, 1), lambda j: (0, 0))] + main + halo
        + [main[1], halo_spec(mr_halo, 1)] + wts + [wts[0], wts[1], wts[2]],
        out_specs=pl.BlockSpec((TILE // chunk, tok_rows, chunk), lambda j: (j, 0, 0)),
        out_shape=jax.ShapeDtypeStruct((shards, tok_rows, chunk), jnp.bfloat16),
        scratch_shapes=[pltpu.VMEM((rows, TILE), jnp.float32) for _ in range(6)],
    )(dist, se_streams, se_streams, se_streams, se_halo, se_halo, se_halo, mr_gates,
      mr_halo, se_feat, se_feat, se_feat, se_filt, mr_feat, mr_feat)


def long_kernel(dist_ref, tss_ref, spos_ref, mg_ref, mh_ref, wq_ref, prev_ref, lo_ref, hi_ref, skip_ref,
                u_ref, out_ref, xa):
    rows = xa.shape[0]
    reach = mh_ref.shape[0]
    xa[HALO - reach : HALO, :] = mh_ref[...].astype(jnp.float32)
    xa[HALO:rows, :] = mg_ref[...].astype(jnp.float32)
    q2 = short_conv_rows(xa, wq_ref, HALO, dist_ref)
    blk = lo_ref.shape[1]
    tile = lo_ref.shape[2]
    width = u_ref.shape[1]
    per_group = tile // u_ref.shape[0]
    lo = lo_ref[0]
    hi = hi_ref[0]
    windows = (jnp.concatenate([prev_ref[0], lo], axis=0), jnp.concatenate([lo, hi], axis=0))
    masks = [
        spos_ref[:, b * blk : b * blk + width] >= tss_ref[b * blk : (b + 1) * blk, :] for b in range(2)
    ]
    lane_grp = lax.broadcasted_iota(jnp.int32, (1, GROUP_LANES), 1) // per_group
    halves = tile // GROUP_LANES
    groups_half = GROUP_LANES // per_group
    acc = [[jnp.zeros((blk, GROUP_LANES), jnp.float32) for _ in range(halves)] for _ in range(2)]
    for g in range(u_ref.shape[0]):
        half = g // groups_half
        row = jnp.broadcast_to(u_ref[g : g + 1, :], (blk, width))
        taps = pltpu.roll(row, 0, 1, stride=1, stride_axis=0)
        for b in range(2):
            mat = jnp.where(masks[b], taps, 0.0).astype(jnp.bfloat16)
            part = windows[b][:, half * GROUP_LANES : (half + 1) * GROUP_LANES]
            res = jnp.dot(mat, part, preferred_element_type=jnp.float32)
            acc[b][half] = jnp.where(lane_grp == g % groups_half, res, acc[b][half])
    conv = jnp.concatenate([jnp.concatenate(acc[b], axis=1) for b in range(2)], axis=0)
    z = jnp.concatenate([lo, hi], axis=0).astype(jnp.float32)
    mixed = (conv + skip_ref[...].astype(jnp.float32) * z).astype(jnp.bfloat16)
    out_ref[...] = (q2 * mixed.astype(jnp.float32)).astype(jnp.bfloat16)


def long_conv_out(dist, tss, spos, mr_gates, mr_halo, mr_feat, prev_z, z_lo, z_hi, skip, taps_rows):
    steps, blk, lanes = z_lo.shape
    tok_rows = 2 * blk
    channels = steps * lanes
    per_group = channels // taps_rows.shape[0]
    piece = pl.BlockSpec((1, blk, lanes), lambda j: (j, 0, 0))
    return pl.pallas_call(
        long_kernel,
        grid=(steps,),
        in_specs=[
            pl.BlockSpec(dist.shape, lambda j: (0, 0)),
            pl.BlockSpec(tss.shape, lambda j: (0, 0)),
            pl.BlockSpec(spos.shape, lambda j: (0, 0)),
            pl.BlockSpec((tok_rows, lanes), lambda j: (0, j)),
            pl.BlockSpec((mr_halo.shape[0], lanes), lambda j: (0, j)),
            pl.BlockSpec((mr_feat.shape[0], lanes), lambda j: (0, j)),
            piece,
            piece,
            piece,
            pl.BlockSpec((1, lanes), lambda j: (0, j)),
            pl.BlockSpec((lanes // per_group, taps_rows.shape[1]), lambda j: (j, 0)),
        ],
        out_specs=pl.BlockSpec((tok_rows, lanes), lambda j: (0, j)),
        out_shape=jax.ShapeDtypeStruct((tok_rows, channels), jnp.bfloat16),
        scratch_shapes=[pltpu.VMEM((tok_rows + HALO, lanes), jnp.float32)],
    )(dist, tss, spos, mr_gates, mr_halo, mr_feat, prev_z, z_lo, z_hi, skip, taps_rows)


def tail_kernel(begin_ref, first_ref, lo_ref, hi_ref, out_ref, z_all):
    shards, blk, lanes = lo_ref.shape
    tail_len = out_ref.shape[0]
    total = z_all.shape[0]
    for src in range(shards):
        z_all[2 * src * blk : (2 * src + 1) * blk, :] = lo_ref[src].astype(jnp.float32)
        z_all[(2 * src + 1) * blk : (2 * src + 2) * blk, :] = hi_ref[src].astype(jnp.float32)
    for t in range(out_ref.shape[1]):
        begin = begin_ref[t]
        start = jnp.clip((begin // 16) * 16, 0, total - WINDOW)
        shift = begin - start
        window = z_all[pl.ds(pl.multiple_of(start, 16), WINDOW), :]
        moved = pltpu.roll(window, (WINDOW - shift) % WINDOW, 0)[:tail_len]
        pos = begin + lax.broadcasted_iota(jnp.int32, (tail_len, 1), 0)
        out_ref[:, t, :] = jnp.where(pos >= first_ref[t], moved, 0.0).astype(out_ref.dtype)


def cut_tails_all(z_lo, z_hi, begins, firsts, tail_len):
    shards, blk, lanes = z_lo.shape
    count = begins.shape[0]
    smem = pl.BlockSpec(memory_space=pltpu.SMEM)
    vmem = pl.BlockSpec(memory_space=pltpu.VMEM)
    out = pl.pallas_call(
        tail_kernel,
        in_specs=[smem, smem, vmem, vmem],
        out_specs=vmem,
        out_shape=jax.ShapeDtypeStruct((tail_len, count, lanes), z_lo.dtype),
        scratch_shapes=[pltpu.VMEM((2 * shards * blk, lanes), jnp.float32)],
    )(begins, firsts, z_lo, z_hi)
    return jnp.transpose(out, (1, 0, 2))


def seg_start(positions, req_ends):
    seg = request_of(positions, req_ends)
    prev_end = jnp.where(seg > 0, pick_entries(req_ends, jnp.maximum(seg - 1, 0)), -1)
    return prev_end + 1


def pick_entries(lookup_table, indices):
    hits = indices[:, None] == jnp.arange(lookup_table.shape[0], dtype=jnp.int32)[None, :]
    return jnp.sum(jnp.where(hits, lookup_table[None, :], 0), axis=1)


def local(
    se_streams, mr_gates, se_feat, se_filter, mr_feat, mr_filter, mr_skip, req_ends, decode_row
):
    tok_rows = se_streams.shape[0]
    channels = mr_gates.shape[1] // 2
    shards = lax.axis_size("seq")
    device = lax.axis_index("seq")
    offset = device * tok_rows
    reach_rows = se_feat.shape[0] - 1
    tap_count = mr_filter.shape[0]
    tail_len = tap_count - 1
    group_ch = channels // se_filter.shape[1]
    total_req = req_ends.shape[0]
    slot_total = ENDS_MAX + 1
    rim_depth = 2 * reach_rows
    prev_se, prev_mr = passed_along(
        (se_streams[tok_rows - 3 * reach_rows :], mr_gates[tok_rows - reach_rows :]), "seq", 1
    )
    blk = tok_rows // 2
    se_filt = jnp.repeat(se_filter, group_ch, axis=1)

    def dist_of(half):
        ext_pos = offset + half * blk - HALO + jnp.arange(blk + HALO, dtype=jnp.int32)
        return (ext_pos - seg_start(ext_pos, req_ends))[:, None]

    dists = [dist_of(0), dist_of(1)]
    z_hi = short_chain(
        dists[1], se_streams, se_streams, mr_gates, mr_gates, se_feat, se_filt, mr_feat, shards, 1
    )
    prev_z = passed_along(z_hi, "seq", 1)
    z_hi, prev_se, prev_mr = lax.optimization_barrier((z_hi, prev_se, prev_mr))
    recv_hi = lax.all_to_all(z_hi, "seq", split_axis=0, concat_axis=0, tiled=True)
    z_lo = short_chain(
        dists[0], se_streams, prev_se, mr_gates, prev_mr, se_feat, se_filt, mr_feat, shards, 0
    )
    z_lo, recv_hi = lax.optimization_barrier((z_lo, recv_hi))
    recv_lo = lax.all_to_all(z_lo, "seq", split_axis=0, concat_axis=0, tiled=True)
    filt_t = mr_filter[::-1].T.astype(jnp.float32)
    filters = filt_t.shape[0]
    taps_rows = jnp.concatenate(
        [jnp.zeros((filters, 1), jnp.float32), filt_t, jnp.zeros((filters, tap_count - 1), jnp.float32)],
        axis=1,
    )

    tgt_pos = offset + jnp.arange(tok_rows, dtype=jnp.int32)
    tss = seg_start(tgt_pos, req_ends)[:, None]
    spos = (offset - blk + jnp.arange(tok_rows + blk, dtype=jnp.int32))[None, :]
    ext_pos = offset - HALO + jnp.arange(tok_rows + HALO, dtype=jnp.int32)
    dist = (ext_pos - seg_start(ext_pos, req_ends))[:, None]
    hyena_out = long_conv_out(
        dist, tss, spos, mr_gates, prev_mr, mr_feat, prev_z, z_lo, z_hi, mr_skip[None, :], taps_rows
    )
    rows_ids = jnp.arange(total_req, dtype=jnp.int32)
    owner = jnp.sum(
        jnp.where(decode_row[None, :] == rows_ids[:, None], rows_ids[None, :], 0), axis=1
    )
    last_pos = pick_entries(req_ends, owner)
    first_pos = jnp.where(owner > 0, pick_entries(req_ends, jnp.maximum(owner - 1, 0)) + 1, 0)
    tail_cache = cut_tails_all(recv_lo, recv_hi, last_pos - tail_len + 1, first_pos, tail_len)
    return (hyena_out, tail_cache)


def solution(mesh):
    placed = (
        P(("groups", "seq"), None),
        P(("groups", "seq"), None),
        P(),
        P(),
        P(),
        P(),
        P(),
        P("groups"),
        P("groups"),
    )
    return jax.shard_map(
        local,
        mesh=mesh,
        in_specs=placed,
        out_specs=(P(("groups", "seq"), None), P("groups", None, "seq")),
        check_vma=False,
    )
```

```python
import functools

import jax
import jax.numpy as jnp
from jax import lax
from jax.sharding import PartitionSpec as P
from jax.experimental import pallas as pl
from jax.experimental.pallas import tpu as pltpu

ENDS_MAX = 4


def passed_along(x, axis, by):
    length = lax.axis_size(axis)
    pairs = [(i, i + by) for i in range(length) if 0 <= i + by < length]
    return lax.ppermute(x, axis, pairs)


def request_of(positions, req_ends):
    return jnp.sum((req_ends[None, :] < positions[:, None]).astype(jnp.int32), axis=1)


def short_conv(values, weights, segment):
    length = weights.shape[0]
    out_count = values.shape[0] - length + 1
    latest = length - 1
    current = segment[latest:]
    summed = values[latest:].astype(jnp.float32) * weights[0].astype(jnp.float32)
    for lag_step in range(1, length):
        earlier = values[latest - lag_step : latest - lag_step + out_count].astype(jnp.float32)
        same_req = segment[latest - lag_step : latest - lag_step + out_count] == current
        summed = summed + jnp.where(
            same_req[:, None], earlier * weights[lag_step].astype(jnp.float32), 0.0
        )
    return summed


HALO = 32
TILE = 512
GROUP_LANES = 128
WINDOW = 144


def short_conv_rows(x, w, first, dist_ref):
    rows = x.shape[0]
    dist = dist_ref[first:rows, :]
    acc = x[first:rows, :] * w[0:1, :].astype(jnp.float32)
    for lag in range(1, w.shape[0]):
        term = x[first - lag : rows - lag, :] * w[lag : lag + 1, :].astype(jnp.float32)
        acc = acc + jnp.where(dist >= lag, term, 0.0)
    return acc


def chain_kernel(dist_ref, sq, sk, sv, hq, hk, hv, mk, gk_h, fq, fk, fv, filt_ref, wk, wv,
                 z2_ref, xq, xk, xv, xb, zs, ys, group_ch):
    rows, tile = xq.shape
    filters = filt_ref.shape[1]
    lane_ch = pl.program_id(0) * tile + lax.broadcasted_iota(jnp.int32, (filters, tile), 1)
    spread = (lane_ch // group_ch == lax.broadcasted_iota(jnp.int32, (filters, tile), 0))
    filt = jnp.dot(filt_ref[...], spread.astype(filt_ref.dtype), preferred_element_type=jnp.float32)
    for main, halo, x in ((sq, hq, xq), (sk, hk, xk), (sv, hv, xv), (mk, gk_h, xb)):
        reach = halo.shape[0]
        if reach < HALO:
            x[0 : HALO - reach, :] = jnp.zeros((HALO - reach, x.shape[1]), jnp.float32)
        x[HALO - reach : HALO, :] = halo[...].astype(jnp.float32)
        x[HALO:rows, :] = main[...].astype(jnp.float32)

    k1 = short_conv_rows(xk, fk, 16, dist_ref)
    v1 = short_conv_rows(xv, fv, 16, dist_ref)
    zs[16:rows, :] = (k1 * v1).astype(jnp.bfloat16).astype(jnp.float32)
    q1 = short_conv_rows(xq, fq, 24, dist_ref)
    c1 = short_conv_rows(zs, filt, 24, dist_ref)
    ys[24:rows, :] = (q1 * c1).astype(jnp.bfloat16).astype(jnp.float32)
    v2 = short_conv_rows(ys, wv, HALO, dist_ref)
    k2 = short_conv_rows(xb, wk, HALO, dist_ref)
    z2 = (k2 * v2).astype(jnp.bfloat16)
    chunk = z2_ref.shape[2]
    for i in range(z2_ref.shape[0]):
        z2_ref[i] = z2[:, i * chunk : (i + 1) * chunk]


def short_chain(dist, se_streams, se_halo, mr_gates, mr_halo, se_feat, se_filt, mr_feat, shards, half):
    tok_rows = dist.shape[0] - HALO
    channels = mr_gates.shape[1] // 2
    steps = channels // TILE
    rows = tok_rows + HALO
    taps = se_feat.shape[0]
    chunk = channels // shards

    def col(part, row_block=half):
        return lambda j: (row_block, j + part * steps)

    def halo_spec(halo, part):
        if halo.shape[0] < HALO:
            return pl.BlockSpec((halo.shape[0], TILE), col(part, 0))
        return pl.BlockSpec((HALO, TILE), col(part, half * tok_rows // HALO - 1))

    main = [pl.BlockSpec((tok_rows, TILE), col(p)) for p in range(3)]
    halo = [halo_spec(se_halo, p) for p in range(3)]
    wts = [pl.BlockSpec((taps, TILE), col(p, 0)) for p in range(3)]
    return pl.pallas_call(
        functools.partial(chain_kernel, group_ch=channels // se_filt.shape[1]),
        grid=(steps,),
        in_specs=[pl.BlockSpec((rows, 1), lambda j: (0, 0))] + main + halo
        + [main[1], halo_spec(mr_halo, 1)] + wts
        + [pl.BlockSpec(se_filt.shape, lambda j: (0, 0)), wts[1], wts[2]],
        out_specs=pl.BlockSpec((TILE // chunk, tok_rows, chunk), lambda j: (j, 0, 0)),
        out_shape=jax.ShapeDtypeStruct((shards, tok_rows, chunk), jnp.bfloat16),
        scratch_shapes=[pltpu.VMEM((rows, TILE), jnp.float32) for _ in range(6)],
    )(dist, se_streams, se_streams, se_streams, se_halo, se_halo, se_halo, mr_gates,
      mr_halo, se_feat, se_feat, se_feat, se_filt, mr_feat, mr_feat)


def long_kernel(dist_ref, tss_ref, spos_ref, mg_ref, mh_ref, wq_ref, prev_ref, lo_ref, hi_ref, skip_ref,
                u_ref, out_ref, xa):
    rows = xa.shape[0]
    reach = mh_ref.shape[0]
    xa[HALO - reach : HALO, :] = mh_ref[...].astype(jnp.float32)
    xa[HALO:rows, :] = mg_ref[...].astype(jnp.float32)
    q2 = short_conv_rows(xa, wq_ref, HALO, dist_ref)
    blk = lo_ref.shape[1]
    tile = lo_ref.shape[2]
    width = u_ref.shape[1]
    per_group = tile // u_ref.shape[0]
    lo = lo_ref[0]
    hi = hi_ref[0]
    windows = (jnp.concatenate([prev_ref[0], lo], axis=0), jnp.concatenate([lo, hi], axis=0))
    masks = [
        spos_ref[:, b * blk : b * blk + width] >= tss_ref[b * blk : (b + 1) * blk, :] for b in range(2)
    ]
    lane_grp = lax.broadcasted_iota(jnp.int32, (1, GROUP_LANES), 1) // per_group
    halves = tile // GROUP_LANES
    groups_half = GROUP_LANES // per_group
    acc = [[jnp.zeros((blk, GROUP_LANES), jnp.float32) for _ in range(halves)] for _ in range(2)]
    for g in range(u_ref.shape[0]):
        half = g // groups_half
        row = jnp.broadcast_to(u_ref[g : g + 1, :], (blk, width))
        taps = pltpu.roll(row, 0, 1, stride=1, stride_axis=0)
        for b in range(2):
            mat = jnp.where(masks[b], taps, 0.0).astype(jnp.bfloat16)
            part = windows[b][:, half * GROUP_LANES : (half + 1) * GROUP_LANES]
            res = jnp.dot(mat, part, preferred_element_type=jnp.float32)
            acc[b][half] = jnp.where(lane_grp == g % groups_half, res, acc[b][half])
    conv = jnp.concatenate([jnp.concatenate(acc[b], axis=1) for b in range(2)], axis=0)
    z = jnp.concatenate([lo, hi], axis=0).astype(jnp.float32)
    mixed = (conv + skip_ref[...].astype(jnp.float32) * z).astype(jnp.bfloat16)
    out_ref[...] = (q2 * mixed.astype(jnp.float32)).astype(jnp.bfloat16)


def long_conv_out(dist, tss, spos, mr_gates, mr_halo, mr_feat, prev_z, z_lo, z_hi, skip, taps_rows):
    steps, blk, lanes = z_lo.shape
    tok_rows = 2 * blk
    channels = steps * lanes
    per_group = channels // taps_rows.shape[0]
    piece = pl.BlockSpec((1, blk, lanes), lambda j: (j, 0, 0))
    return pl.pallas_call(
        long_kernel,
        grid=(steps,),
        in_specs=[
            pl.BlockSpec(dist.shape, lambda j: (0, 0)),
            pl.BlockSpec(tss.shape, lambda j: (0, 0)),
            pl.BlockSpec(spos.shape, lambda j: (0, 0)),
            pl.BlockSpec((tok_rows, lanes), lambda j: (0, j)),
            pl.BlockSpec((mr_halo.shape[0], lanes), lambda j: (0, j)),
            pl.BlockSpec((mr_feat.shape[0], lanes), lambda j: (0, j)),
            piece,
            piece,
            piece,
            pl.BlockSpec((1, lanes), lambda j: (0, j)),
            pl.BlockSpec((lanes // per_group, taps_rows.shape[1]), lambda j: (j, 0)),
        ],
        out_specs=pl.BlockSpec((tok_rows, lanes), lambda j: (0, j)),
        out_shape=jax.ShapeDtypeStruct((tok_rows, channels), jnp.bfloat16),
        scratch_shapes=[pltpu.VMEM((tok_rows + HALO, lanes), jnp.float32)],
    )(dist, tss, spos, mr_gates, mr_halo, mr_feat, prev_z, z_lo, z_hi, skip, taps_rows)


def tail_kernel(begin_ref, first_ref, lo_ref, hi_ref, out_ref, z_all):
    shards, blk, lanes = lo_ref.shape
    tail_len = out_ref.shape[0]
    total = z_all.shape[0]
    for src in range(shards):
        z_all[2 * src * blk : (2 * src + 1) * blk, :] = lo_ref[src].astype(jnp.float32)
        z_all[(2 * src + 1) * blk : (2 * src + 2) * blk, :] = hi_ref[src].astype(jnp.float32)
    for t in range(out_ref.shape[1]):
        begin = begin_ref[t]
        start = jnp.clip((begin // 16) * 16, 0, total - WINDOW)
        shift = begin - start
        window = z_all[pl.ds(pl.multiple_of(start, 16), WINDOW), :]
        moved = pltpu.roll(window, (WINDOW - shift) % WINDOW, 0)[:tail_len]
        pos = begin + lax.broadcasted_iota(jnp.int32, (tail_len, 1), 0)
        out_ref[:, t, :] = jnp.where(pos >= first_ref[t], moved, 0.0).astype(out_ref.dtype)


def cut_tails_all(z_lo, z_hi, begins, firsts, tail_len):
    shards, blk, lanes = z_lo.shape
    count = begins.shape[0]
    smem = pl.BlockSpec(memory_space=pltpu.SMEM)
    vmem = pl.BlockSpec(memory_space=pltpu.VMEM)
    out = pl.pallas_call(
        tail_kernel,
        in_specs=[smem, smem, vmem, vmem],
        out_specs=vmem,
        out_shape=jax.ShapeDtypeStruct((tail_len, count, lanes), z_lo.dtype),
        scratch_shapes=[pltpu.VMEM((2 * shards * blk, lanes), jnp.float32)],
    )(begins, firsts, z_lo, z_hi)
    return jnp.transpose(out, (1, 0, 2))


def seg_start(positions, req_ends):
    seg = request_of(positions, req_ends)
    prev_end = jnp.where(seg > 0, pick_entries(req_ends, jnp.maximum(seg - 1, 0)), -1)
    return prev_end + 1


def pick_entries(lookup_table, indices):
    hits = indices[:, None] == jnp.arange(lookup_table.shape[0], dtype=jnp.int32)[None, :]
    return jnp.sum(jnp.where(hits, lookup_table[None, :], 0), axis=1)


def local(
    se_streams, mr_gates, se_feat, se_filter, mr_feat, mr_filter, mr_skip, req_ends, decode_row
):
    tok_rows = se_streams.shape[0]
    channels = mr_gates.shape[1] // 2
    shards = lax.axis_size("seq")
    device = lax.axis_index("seq")
    offset = device * tok_rows
    reach_rows = se_feat.shape[0] - 1
    tap_count = mr_filter.shape[0]
    tail_len = tap_count - 1
    group_ch = channels // se_filter.shape[1]
    total_req = req_ends.shape[0]
    slot_total = ENDS_MAX + 1
    rim_depth = 2 * reach_rows
    prev_se, prev_mr = passed_along(
        (se_streams[tok_rows - 3 * reach_rows :], mr_gates[tok_rows - reach_rows :]), "seq", 1
    )
    blk = tok_rows // 2
    se_filt = se_filter

    def dist_of(half):
        ext_pos = offset + half * blk - HALO + jnp.arange(blk + HALO, dtype=jnp.int32)
        return (ext_pos - seg_start(ext_pos, req_ends))[:, None]

    dists = [dist_of(0), dist_of(1)]
    z_hi = short_chain(
        dists[1], se_streams, se_streams, mr_gates, mr_gates, se_feat, se_filt, mr_feat, shards, 1
    )
    prev_z = passed_along(z_hi, "seq", 1)
    z_hi, prev_se, prev_mr = lax.optimization_barrier((z_hi, prev_se, prev_mr))
    recv_hi = lax.all_to_all(z_hi, "seq", split_axis=0, concat_axis=0, tiled=True)
    z_lo = short_chain(
        dists[0], se_streams, prev_se, mr_gates, prev_mr, se_feat, se_filt, mr_feat, shards, 0
    )
    z_lo, recv_hi = lax.optimization_barrier((z_lo, recv_hi))
    recv_lo = lax.all_to_all(z_lo, "seq", split_axis=0, concat_axis=0, tiled=True)
    filt_t = mr_filter[::-1].T.astype(jnp.float32)
    filters = filt_t.shape[0]
    taps_rows = jnp.concatenate(
        [jnp.zeros((filters, 1), jnp.float32), filt_t, jnp.zeros((filters, tap_count - 1), jnp.float32)],
        axis=1,
    )

    tgt_pos = offset + jnp.arange(tok_rows, dtype=jnp.int32)
    tss = seg_start(tgt_pos, req_ends)[:, None]
    spos = (offset - blk + jnp.arange(tok_rows + blk, dtype=jnp.int32))[None, :]
    ext_pos = offset - HALO + jnp.arange(tok_rows + HALO, dtype=jnp.int32)
    dist = (ext_pos - seg_start(ext_pos, req_ends))[:, None]
    hyena_out = long_conv_out(
        dist, tss, spos, mr_gates, prev_mr, mr_feat, prev_z, z_lo, z_hi, mr_skip[None, :], taps_rows
    )
    rows_ids = jnp.arange(total_req, dtype=jnp.int32)
    owner = jnp.sum(
        jnp.where(decode_row[None, :] == rows_ids[:, None], rows_ids[None, :], 0), axis=1
    )
    last_pos = pick_entries(req_ends, owner)
    first_pos = jnp.where(owner > 0, pick_entries(req_ends, jnp.maximum(owner - 1, 0)) + 1, 0)
    tail_cache = cut_tails_all(recv_lo, recv_hi, last_pos - tail_len + 1, first_pos, tail_len)
    return (hyena_out, tail_cache)


def solution(mesh):
    placed = (
        P(("groups", "seq"), None),
        P(("groups", "seq"), None),
        P(),
        P(),
        P(),
        P(),
        P(),
        P("groups"),
        P("groups"),
    )
    return jax.shard_map(
        local,
        mesh=mesh,
        in_specs=placed,
        out_specs=(P(("groups", "seq"), None), P("groups", None, "seq")),
        check_vma=False,
    )
```

```python
import functools

import jax
import jax.numpy as jnp
from jax import lax
from jax.sharding import PartitionSpec as P
from jax.experimental import pallas as pl
from jax.experimental.pallas import tpu as pltpu

ENDS_MAX = 4


def passed_along(x, axis, by):
    length = lax.axis_size(axis)
    pairs = [(i, i + by) for i in range(length) if 0 <= i + by < length]
    return lax.ppermute(x, axis, pairs)


def request_of(positions, req_ends):
    return jnp.sum((req_ends[None, :] < positions[:, None]).astype(jnp.int32), axis=1)


def short_conv(values, weights, segment):
    length = weights.shape[0]
    out_count = values.shape[0] - length + 1
    latest = length - 1
    current = segment[latest:]
    summed = values[latest:].astype(jnp.float32) * weights[0].astype(jnp.float32)
    for lag_step in range(1, length):
        earlier = values[latest - lag_step : latest - lag_step + out_count].astype(jnp.float32)
        same_req = segment[latest - lag_step : latest - lag_step + out_count] == current
        summed = summed + jnp.where(
            same_req[:, None], earlier * weights[lag_step].astype(jnp.float32), 0.0
        )
    return summed


HALO = 32
TILE = 512
GROUP_LANES = 128
WINDOW = 144


def short_conv_rows(x, w, first, dist_all):
    rows = x.shape[0]
    dist = dist_all[first:rows, :]
    acc = x[first:rows, :] * w[0:1, :].astype(jnp.float32)
    for lag in range(1, w.shape[0]):
        term = x[first - lag : rows - lag, :] * w[lag : lag + 1, :].astype(jnp.float32)
        acc = acc + jnp.where(dist >= lag, term, 0.0)
    return acc


def rel_dist(rel_ref, base, count):
    index = base + lax.broadcasted_iota(jnp.int32, (count, 1), 0)
    return index - rel_ref[base : base + count, :]


def chain_kernel(rel_ref, sq, sk, sv, hq, hk, hv, mk, gk_h, fq, fk, fv, filt_ref, wk, wv,
                 z2_ref, xq, xk, xv, xb, zs, ys, group_ch, base):
    rows, tile = xq.shape
    dist_ref = rel_dist(rel_ref, base, rows)
    filters = filt_ref.shape[1]
    lane_ch = pl.program_id(0) * tile + lax.broadcasted_iota(jnp.int32, (filters, tile), 1)
    spread = (lane_ch // group_ch == lax.broadcasted_iota(jnp.int32, (filters, tile), 0))
    filt = jnp.dot(filt_ref[...], spread.astype(filt_ref.dtype), preferred_element_type=jnp.float32)
    for main, halo, x in ((sq, hq, xq), (sk, hk, xk), (sv, hv, xv), (mk, gk_h, xb)):
        reach = halo.shape[0]
        if reach < HALO:
            x[0 : HALO - reach, :] = jnp.zeros((HALO - reach, x.shape[1]), jnp.float32)
        x[HALO - reach : HALO, :] = halo[...].astype(jnp.float32)
        x[HALO:rows, :] = main[...].astype(jnp.float32)

    k1 = short_conv_rows(xk, fk, 16, dist_ref)
    v1 = short_conv_rows(xv, fv, 16, dist_ref)
    zs[16:rows, :] = (k1 * v1).astype(jnp.bfloat16).astype(jnp.float32)
    q1 = short_conv_rows(xq, fq, 24, dist_ref)
    c1 = short_conv_rows(zs, filt, 24, dist_ref)
    ys[24:rows, :] = (q1 * c1).astype(jnp.bfloat16).astype(jnp.float32)
    v2 = short_conv_rows(ys, wv, HALO, dist_ref)
    k2 = short_conv_rows(xb, wk, HALO, dist_ref)
    z2 = (k2 * v2).astype(jnp.bfloat16)
    chunk = z2_ref.shape[2]
    for i in range(z2_ref.shape[0]):
        z2_ref[i] = z2[:, i * chunk : (i + 1) * chunk]


def short_chain(rel, se_streams, se_halo, mr_gates, mr_halo, se_feat, se_filt, mr_feat, shards, half):
    tok_rows = se_streams.shape[0] // 2
    channels = mr_gates.shape[1] // 2
    steps = channels // TILE
    rows = tok_rows + HALO
    taps = se_feat.shape[0]
    chunk = channels // shards

    def col(part, row_block=half):
        return lambda j: (row_block, j + part * steps)

    def halo_spec(halo, part):
        if halo.shape[0] < HALO:
            return pl.BlockSpec((halo.shape[0], TILE), col(part, 0))
        return pl.BlockSpec((HALO, TILE), col(part, half * tok_rows // HALO - 1))

    main = [pl.BlockSpec((tok_rows, TILE), col(p)) for p in range(3)]
    halo = [halo_spec(se_halo, p) for p in range(3)]
    wts = [pl.BlockSpec((taps, TILE), col(p, 0)) for p in range(3)]
    return pl.pallas_call(
        functools.partial(
            chain_kernel, group_ch=channels // se_filt.shape[1], base=half * tok_rows + tok_rows - HALO
        ),
        grid=(steps,),
        in_specs=[pl.BlockSpec(rel.shape, lambda j: (0, 0))] + main + halo
        + [main[1], halo_spec(mr_halo, 1)] + wts
        + [pl.BlockSpec(se_filt.shape, lambda j: (0, 0)), wts[1], wts[2]],
        out_specs=pl.BlockSpec((TILE // chunk, tok_rows, chunk), lambda j: (j, 0, 0)),
        out_shape=jax.ShapeDtypeStruct((shards, tok_rows, chunk), jnp.bfloat16),
        scratch_shapes=[pltpu.VMEM((rows, TILE), jnp.float32) for _ in range(6)],
    )(rel, se_streams, se_streams, se_streams, se_halo, se_halo, se_halo, mr_gates,
      mr_halo, se_feat, se_feat, se_feat, se_filt, mr_feat, mr_feat)


def long_kernel(rel_ref, mg_ref, mh_ref, wq_ref, prev_ref, lo_ref, hi_ref, skip_ref,
                u_ref, out_ref, xa):
    rows = xa.shape[0]
    reach = mh_ref.shape[0]
    xa[HALO - reach : HALO, :] = mh_ref[...].astype(jnp.float32)
    xa[HALO:rows, :] = mg_ref[...].astype(jnp.float32)
    blk = lo_ref.shape[1]
    q2 = short_conv_rows(xa, wq_ref, HALO, rel_dist(rel_ref, blk - HALO, rows))
    blk = lo_ref.shape[1]
    tile = lo_ref.shape[2]
    width = u_ref.shape[1]
    per_group = tile // u_ref.shape[0]
    lo = lo_ref[0]
    hi = hi_ref[0]
    windows = (jnp.concatenate([prev_ref[0], lo], axis=0), jnp.concatenate([lo, hi], axis=0))
    masks = [
        lax.broadcasted_iota(jnp.int32, (1, width), 1) + b * blk >= rel_ref[(b + 1) * blk : (b + 2) * blk, :]
        for b in range(2)
    ]
    lane_grp = lax.broadcasted_iota(jnp.int32, (1, GROUP_LANES), 1) // per_group
    halves = tile // GROUP_LANES
    groups_half = GROUP_LANES // per_group
    acc = [[jnp.zeros((blk, GROUP_LANES), jnp.float32) for _ in range(halves)] for _ in range(2)]
    for g in range(u_ref.shape[0]):
        half = g // groups_half
        row = jnp.broadcast_to(u_ref[g : g + 1, :], (blk, width))
        taps = pltpu.roll(row, 0, 1, stride=1, stride_axis=0)
        for b in range(2):
            mat = jnp.where(masks[b], taps, 0.0).astype(jnp.bfloat16)
            part = windows[b][:, half * GROUP_LANES : (half + 1) * GROUP_LANES]
            res = jnp.dot(mat, part, preferred_element_type=jnp.float32)
            acc[b][half] = jnp.where(lane_grp == g % groups_half, res, acc[b][half])
    conv = jnp.concatenate([jnp.concatenate(acc[b], axis=1) for b in range(2)], axis=0)
    z = jnp.concatenate([lo, hi], axis=0).astype(jnp.float32)
    mixed = (conv + skip_ref[...].astype(jnp.float32) * z).astype(jnp.bfloat16)
    out_ref[...] = (q2 * mixed.astype(jnp.float32)).astype(jnp.bfloat16)


def long_conv_out(rel, mr_gates, mr_halo, mr_feat, prev_z, z_lo, z_hi, skip, taps_rows):
    steps, blk, lanes = z_lo.shape
    tok_rows = 2 * blk
    channels = steps * lanes
    per_group = channels // taps_rows.shape[0]
    piece = pl.BlockSpec((1, blk, lanes), lambda j: (j, 0, 0))
    return pl.pallas_call(
        long_kernel,
        grid=(steps,),
        in_specs=[
            pl.BlockSpec(rel.shape, lambda j: (0, 0)),
            pl.BlockSpec((tok_rows, lanes), lambda j: (0, j)),
            pl.BlockSpec((mr_halo.shape[0], lanes), lambda j: (0, j)),
            pl.BlockSpec((mr_feat.shape[0], lanes), lambda j: (0, j)),
            piece,
            piece,
            piece,
            pl.BlockSpec((1, lanes), lambda j: (0, j)),
            pl.BlockSpec((lanes // per_group, taps_rows.shape[1]), lambda j: (j, 0)),
        ],
        out_specs=pl.BlockSpec((tok_rows, lanes), lambda j: (0, j)),
        out_shape=jax.ShapeDtypeStruct((tok_rows, channels), jnp.bfloat16),
        scratch_shapes=[pltpu.VMEM((tok_rows + HALO, lanes), jnp.float32)],
    )(rel, mr_gates, mr_halo, mr_feat, prev_z, z_lo, z_hi, skip, taps_rows)


def tail_kernel(begin_ref, first_ref, lo_ref, hi_ref, out_ref, z_all):
    shards, blk, lanes = lo_ref.shape
    tail_len = out_ref.shape[0]
    total = z_all.shape[0]
    for src in range(shards):
        z_all[2 * src * blk : (2 * src + 1) * blk, :] = lo_ref[src].astype(jnp.float32)
        z_all[(2 * src + 1) * blk : (2 * src + 2) * blk, :] = hi_ref[src].astype(jnp.float32)
    for t in range(out_ref.shape[1]):
        begin = begin_ref[t]
        start = jnp.clip((begin // 16) * 16, 0, total - WINDOW)
        shift = begin - start
        window = z_all[pl.ds(pl.multiple_of(start, 16), WINDOW), :]
        moved = pltpu.roll(window, (WINDOW - shift) % WINDOW, 0)[:tail_len]
        pos = begin + lax.broadcasted_iota(jnp.int32, (tail_len, 1), 0)
        out_ref[:, t, :] = jnp.where(pos >= first_ref[t], moved, 0.0).astype(out_ref.dtype)


def cut_tails_all(z_lo, z_hi, begins, firsts, tail_len):
    shards, blk, lanes = z_lo.shape
    count = begins.shape[0]
    smem = pl.BlockSpec(memory_space=pltpu.SMEM)
    vmem = pl.BlockSpec(memory_space=pltpu.VMEM)
    out = pl.pallas_call(
        tail_kernel,
        in_specs=[smem, smem, vmem, vmem],
        out_specs=vmem,
        out_shape=jax.ShapeDtypeStruct((tail_len, count, lanes), z_lo.dtype),
        scratch_shapes=[pltpu.VMEM((2 * shards * blk, lanes), jnp.float32)],
    )(begins, firsts, z_lo, z_hi)
    return jnp.transpose(out, (1, 0, 2))


def seg_start(positions, req_ends):
    seg = request_of(positions, req_ends)
    prev_end = jnp.where(seg > 0, pick_entries(req_ends, jnp.maximum(seg - 1, 0)), -1)
    return prev_end + 1


def pick_entries(lookup_table, indices):
    hits = indices[:, None] == jnp.arange(lookup_table.shape[0], dtype=jnp.int32)[None, :]
    return jnp.sum(jnp.where(hits, lookup_table[None, :], 0), axis=1)


def local(
    se_streams, mr_gates, se_feat, se_filter, mr_feat, mr_filter, mr_skip, req_ends, decode_row
):
    tok_rows = se_streams.shape[0]
    channels = mr_gates.shape[1] // 2
    shards = lax.axis_size("seq")
    device = lax.axis_index("seq")
    offset = device * tok_rows
    reach_rows = se_feat.shape[0] - 1
    tap_count = mr_filter.shape[0]
    tail_len = tap_count - 1
    group_ch = channels // se_filter.shape[1]
    total_req = req_ends.shape[0]
    slot_total = ENDS_MAX + 1
    rim_depth = 2 * reach_rows
    prev_se, prev_mr = passed_along(
        (se_streams[tok_rows - 3 * reach_rows :], mr_gates[tok_rows - reach_rows :]), "seq", 1
    )
    blk = tok_rows // 2
    se_filt = se_filter

    window_pos = offset - blk + jnp.arange(tok_rows + blk, dtype=jnp.int32)
    rel = (seg_start(window_pos, req_ends) - (offset - blk))[:, None]
    z_hi = short_chain(
        rel, se_streams, se_streams, mr_gates, mr_gates, se_feat, se_filt, mr_feat, shards, 1
    )
    prev_z = passed_along(z_hi, "seq", 1)
    z_hi, prev_se, prev_mr = lax.optimization_barrier((z_hi, prev_se, prev_mr))
    recv_hi = lax.all_to_all(z_hi, "seq", split_axis=0, concat_axis=0, tiled=True)
    z_lo = short_chain(
        rel, se_streams, prev_se, mr_gates, prev_mr, se_feat, se_filt, mr_feat, shards, 0
    )
    z_lo, recv_hi = lax.optimization_barrier((z_lo, recv_hi))
    recv_lo = lax.all_to_all(z_lo, "seq", split_axis=0, concat_axis=0, tiled=True)
    filt_t = mr_filter[::-1].T.astype(jnp.float32)
    filters = filt_t.shape[0]
    taps_rows = jnp.concatenate(
        [jnp.zeros((filters, 1), jnp.float32), filt_t, jnp.zeros((filters, tap_count - 1), jnp.float32)],
        axis=1,
    )

    hyena_out = long_conv_out(
        rel, mr_gates, prev_mr, mr_feat, prev_z, z_lo, z_hi, mr_skip[None, :], taps_rows
    )
    rows_ids = jnp.arange(total_req, dtype=jnp.int32)
    owner = jnp.sum(
        jnp.where(decode_row[None, :] == rows_ids[:, None], rows_ids[None, :], 0), axis=1
    )
    last_pos = pick_entries(req_ends, owner)
    first_pos = jnp.where(owner > 0, pick_entries(req_ends, jnp.maximum(owner - 1, 0)) + 1, 0)
    tail_cache = cut_tails_all(recv_lo, recv_hi, last_pos - tail_len + 1, first_pos, tail_len)
    return (hyena_out, tail_cache)


def solution(mesh):
    placed = (
        P(("groups", "seq"), None),
        P(("groups", "seq"), None),
        P(),
        P(),
        P(),
        P(),
        P(),
        P("groups"),
        P("groups"),
    )
    return jax.shard_map(
        local,
        mesh=mesh,
        in_specs=placed,
        out_specs=(P(("groups", "seq"), None), P("groups", None, "seq")),
        check_vma=False,
    )
```

```python
import functools

import jax
import jax.numpy as jnp
from jax import lax
from jax.sharding import PartitionSpec as P
from jax.experimental import pallas as pl
from jax.experimental.pallas import tpu as pltpu

ENDS_MAX = 4


def passed_along(x, axis, by):
    length = lax.axis_size(axis)
    pairs = [(i, i + by) for i in range(length) if 0 <= i + by < length]
    return lax.ppermute(x, axis, pairs)


def request_of(positions, req_ends):
    return jnp.sum((req_ends[None, :] < positions[:, None]).astype(jnp.int32), axis=1)


def short_conv(values, weights, segment):
    length = weights.shape[0]
    out_count = values.shape[0] - length + 1
    latest = length - 1
    current = segment[latest:]
    summed = values[latest:].astype(jnp.float32) * weights[0].astype(jnp.float32)
    for lag_step in range(1, length):
        earlier = values[latest - lag_step : latest - lag_step + out_count].astype(jnp.float32)
        same_req = segment[latest - lag_step : latest - lag_step + out_count] == current
        summed = summed + jnp.where(
            same_req[:, None], earlier * weights[lag_step].astype(jnp.float32), 0.0
        )
    return summed


HALO = 32
TILE = 512
GROUP_LANES = 128
WINDOW = 144


def short_conv_rows(x, w, first, dist_all):
    rows = x.shape[0]
    dist = dist_all[first:rows, :]
    acc = x[first:rows, :] * w[0:1, :].astype(jnp.float32)
    for lag in range(1, w.shape[0]):
        term = x[first - lag : rows - lag, :] * w[lag : lag + 1, :].astype(jnp.float32)
        acc = acc + jnp.where(dist >= lag, term, 0.0)
    return acc


def rel_dist(rel_ref, base, count):
    index = base + lax.broadcasted_iota(jnp.int32, (count, 1), 0)
    return index - rel_ref[base : base + count, :]


def chain_kernel(rel_ref, sq, sk, sv, hq, hk, hv, mk, gk_h, fq, fk, fv, filt_ref, wk, wv,
                 z2_ref, xq, xk, xv, xb, zs, ys, group_ch, base):
    rows, tile = xq.shape
    dist_ref = rel_dist(rel_ref, base, rows)
    filters = filt_ref.shape[1]
    lane_ch = pl.program_id(0) * tile + lax.broadcasted_iota(jnp.int32, (filters, tile), 1)
    spread = (lane_ch // group_ch == lax.broadcasted_iota(jnp.int32, (filters, tile), 0))
    filt = jnp.dot(filt_ref[...], spread.astype(filt_ref.dtype), preferred_element_type=jnp.float32)
    for main, halo, x in ((sq, hq, xq), (sk, hk, xk), (sv, hv, xv), (mk, gk_h, xb)):
        reach = halo.shape[0]
        if reach < HALO:
            x[0 : HALO - reach, :] = jnp.zeros((HALO - reach, x.shape[1]), jnp.float32)
        x[HALO - reach : HALO, :] = halo[...].astype(jnp.float32)
        x[HALO:rows, :] = main[...].astype(jnp.float32)

    k1 = short_conv_rows(xk, fk, 16, dist_ref)
    v1 = short_conv_rows(xv, fv, 16, dist_ref)
    zs[16:rows, :] = (k1 * v1).astype(jnp.bfloat16).astype(jnp.float32)
    q1 = short_conv_rows(xq, fq, 24, dist_ref)
    c1 = short_conv_rows(zs, filt, 24, dist_ref)
    ys[24:rows, :] = (q1 * c1).astype(jnp.bfloat16).astype(jnp.float32)
    v2 = short_conv_rows(ys, wv, HALO, dist_ref)
    k2 = short_conv_rows(xb, wk, HALO, dist_ref)
    z2 = (k2 * v2).astype(jnp.bfloat16)
    chunk = z2_ref.shape[2]
    for i in range(z2_ref.shape[0]):
        z2_ref[i] = z2[:, i * chunk : (i + 1) * chunk]


def short_chain(rel, se_streams, se_halo, mr_gates, mr_halo, se_feat, se_filt, mr_feat, shards, half):
    tok_rows = se_streams.shape[0] // 2
    channels = mr_gates.shape[1] // 2
    steps = channels // TILE
    rows = tok_rows + HALO
    taps = se_feat.shape[0]
    chunk = channels // shards

    def col(part, row_block=half):
        return lambda j: (row_block, j + part * steps)

    def halo_spec(halo, part):
        if halo.shape[0] < HALO:
            return pl.BlockSpec((halo.shape[0], TILE), col(part, 0))
        return pl.BlockSpec((HALO, TILE), col(part, half * tok_rows // HALO - 1))

    main = [pl.BlockSpec((tok_rows, TILE), col(p)) for p in range(3)]
    halo = [halo_spec(se_halo, p) for p in range(3)]
    wts = [pl.BlockSpec((taps, TILE), col(p, 0)) for p in range(3)]
    return pl.pallas_call(
        functools.partial(
            chain_kernel, group_ch=channels // se_filt.shape[1], base=half * tok_rows + tok_rows - HALO
        ),
        grid=(steps,),
        in_specs=[pl.BlockSpec(rel.shape, lambda j: (0, 0))] + main + halo
        + [main[1], halo_spec(mr_halo, 1)] + wts
        + [pl.BlockSpec(se_filt.shape, lambda j: (0, 0)), wts[1], wts[2]],
        out_specs=pl.BlockSpec((TILE // chunk, tok_rows, chunk), lambda j: (j, 0, 0)),
        out_shape=jax.ShapeDtypeStruct((shards, tok_rows, chunk), jnp.bfloat16),
        scratch_shapes=[pltpu.VMEM((rows, TILE), jnp.float32) for _ in range(6)],
    )(rel, se_streams, se_streams, se_streams, se_halo, se_halo, se_halo, mr_gates,
      mr_halo, se_feat, se_feat, se_feat, se_filt, mr_feat, mr_feat)


def long_kernel(rel_ref, mg_ref, mh_ref, wq_ref, prev_ref, lo_ref, hi_ref, skip_ref,
                u_ref, out_ref, xa):
    rows = xa.shape[0]
    reach = mh_ref.shape[0]
    xa[HALO - reach : HALO, :] = mh_ref[...].astype(jnp.float32)
    xa[HALO:rows, :] = mg_ref[...].astype(jnp.float32)
    blk = lo_ref.shape[1]
    q2 = short_conv_rows(xa, wq_ref, HALO, rel_dist(rel_ref, blk - HALO, rows))
    blk = lo_ref.shape[1]
    tile = lo_ref.shape[2]
    width = u_ref.shape[1]
    per_group = tile // u_ref.shape[0]
    lo = lo_ref[0]
    hi = hi_ref[0]
    windows = (jnp.concatenate([prev_ref[0], lo], axis=0), jnp.concatenate([lo, hi], axis=0))
    masks = [
        lax.broadcasted_iota(jnp.int32, (1, width), 1) + b * blk >= rel_ref[(b + 1) * blk : (b + 2) * blk, :]
        for b in range(2)
    ]
    lane_grp = lax.broadcasted_iota(jnp.int32, (1, GROUP_LANES), 1) // per_group
    halves = tile // GROUP_LANES
    groups_half = GROUP_LANES // per_group
    acc = [[jnp.zeros((blk, GROUP_LANES), jnp.float32) for _ in range(halves)] for _ in range(2)]
    for g in range(u_ref.shape[0]):
        half = g // groups_half
        row = jnp.broadcast_to(u_ref[g : g + 1, :], (blk, width))
        taps = pltpu.roll(row, 0, 1, stride=1, stride_axis=0)
        for b in range(2):
            mat = jnp.where(masks[b], taps, 0.0).astype(jnp.bfloat16)
            part = windows[b][:, half * GROUP_LANES : (half + 1) * GROUP_LANES]
            res = jnp.dot(mat, part, preferred_element_type=jnp.float32)
            acc[b][half] = jnp.where(lane_grp == g % groups_half, res, acc[b][half])
    conv = jnp.concatenate([jnp.concatenate(acc[b], axis=1) for b in range(2)], axis=0)
    z = jnp.concatenate([lo, hi], axis=0).astype(jnp.float32)
    mixed = (conv + skip_ref[...].astype(jnp.float32) * z).astype(jnp.bfloat16)
    out_ref[...] = (q2 * mixed.astype(jnp.float32)).astype(jnp.bfloat16)


def long_conv_out(rel, mr_gates, mr_halo, mr_feat, prev_z, z_lo, z_hi, skip, taps_rows):
    steps, blk, lanes = z_lo.shape
    tok_rows = 2 * blk
    channels = steps * lanes
    per_group = channels // taps_rows.shape[0]
    piece = pl.BlockSpec((1, blk, lanes), lambda j: (j, 0, 0))
    return pl.pallas_call(
        long_kernel,
        grid=(steps,),
        in_specs=[
            pl.BlockSpec(rel.shape, lambda j: (0, 0)),
            pl.BlockSpec((tok_rows, lanes), lambda j: (0, j)),
            pl.BlockSpec((mr_halo.shape[0], lanes), lambda j: (0, j)),
            pl.BlockSpec((mr_feat.shape[0], lanes), lambda j: (0, j)),
            piece,
            piece,
            piece,
            pl.BlockSpec((1, lanes), lambda j: (0, j)),
            pl.BlockSpec((lanes // per_group, taps_rows.shape[1]), lambda j: (j, 0)),
        ],
        out_specs=pl.BlockSpec((tok_rows, lanes), lambda j: (0, j)),
        out_shape=jax.ShapeDtypeStruct((tok_rows, channels), jnp.bfloat16),
        scratch_shapes=[pltpu.VMEM((tok_rows + HALO, lanes), jnp.float32)],
    )(rel, mr_gates, mr_halo, mr_feat, prev_z, z_lo, z_hi, skip, taps_rows)


def tail_kernel(begin_ref, first_ref, lo_ref, hi_ref, out_ref, z_all):
    shards, blk, lanes = lo_ref.shape
    tail_len = out_ref.shape[0]
    total = z_all.shape[0]
    for src in range(shards):
        z_all[2 * src * blk : (2 * src + 1) * blk, :] = lo_ref[src].astype(jnp.float32)
        z_all[(2 * src + 1) * blk : (2 * src + 2) * blk, :] = hi_ref[src].astype(jnp.float32)
    for t in range(out_ref.shape[1]):
        begin = begin_ref[t]
        start = jnp.clip((begin // 16) * 16, 0, total - WINDOW)
        shift = begin - start
        window = z_all[pl.ds(pl.multiple_of(start, 16), WINDOW), :]
        moved = pltpu.roll(window, (WINDOW - shift) % WINDOW, 0)[:tail_len]
        pos = begin + lax.broadcasted_iota(jnp.int32, (tail_len, 1), 0)
        out_ref[:, t, :] = jnp.where(pos >= first_ref[t], moved, 0.0).astype(out_ref.dtype)


def cut_tails_all(z_lo, z_hi, begins, firsts, tail_len):
    shards, blk, lanes = z_lo.shape
    count = begins.shape[0]
    smem = pl.BlockSpec(memory_space=pltpu.SMEM)
    vmem = pl.BlockSpec(memory_space=pltpu.VMEM)
    out = pl.pallas_call(
        tail_kernel,
        in_specs=[smem, smem, vmem, vmem],
        out_specs=vmem,
        out_shape=jax.ShapeDtypeStruct((tail_len, count, lanes), z_lo.dtype),
        scratch_shapes=[pltpu.VMEM((2 * shards * blk, lanes), jnp.float32)],
    )(begins, firsts, z_lo, z_hi)
    return jnp.transpose(out, (1, 0, 2))


def seg_start(positions, req_ends):
    seg = request_of(positions, req_ends)
    prev_end = jnp.where(seg > 0, pick_entries(req_ends, jnp.maximum(seg - 1, 0)), -1)
    return prev_end + 1


def pick_entries(lookup_table, indices):
    hits = indices[:, None] == jnp.arange(lookup_table.shape[0], dtype=jnp.int32)[None, :]
    return jnp.sum(jnp.where(hits, lookup_table[None, :], 0), axis=1)


def local(
    se_streams, mr_gates, se_feat, se_filter, mr_feat, mr_filter, mr_skip, req_ends, decode_row
):
    tok_rows = se_streams.shape[0]
    channels = mr_gates.shape[1] // 2
    shards = lax.axis_size("seq")
    device = lax.axis_index("seq")
    offset = device * tok_rows
    reach_rows = se_feat.shape[0] - 1
    tap_count = mr_filter.shape[0]
    tail_len = tap_count - 1
    group_ch = channels // se_filter.shape[1]
    total_req = req_ends.shape[0]
    slot_total = ENDS_MAX + 1
    rim_depth = 2 * reach_rows
    prev_se, prev_mr = passed_along(
        (se_streams[tok_rows - 3 * reach_rows :], mr_gates[tok_rows - reach_rows :]), "seq", 1
    )
    blk = tok_rows // 2
    se_filt = se_filter

    window_pos = offset - blk + jnp.arange(tok_rows + blk, dtype=jnp.int32)
    rel = (seg_start(window_pos, req_ends) - (offset - blk))[:, None]
    z_hi = short_chain(
        rel, se_streams, se_streams, mr_gates, mr_gates, se_feat, se_filt, mr_feat, shards, 1
    )
    prev_z = passed_along(z_hi, "seq", 1)
    z_hi, prev_se, prev_mr = lax.optimization_barrier((z_hi, prev_se, prev_mr))
    recv_hi = lax.all_to_all(z_hi, "seq", split_axis=0, concat_axis=0, tiled=True)
    z_lo = short_chain(
        rel, se_streams, prev_se, mr_gates, prev_mr, se_feat, se_filt, mr_feat, shards, 0
    )
    z_lo, recv_hi, prev_z = lax.optimization_barrier((z_lo, recv_hi, prev_z))
    recv_lo = lax.all_to_all(z_lo, "seq", split_axis=0, concat_axis=0, tiled=True)
    filt_t = mr_filter[::-1].T.astype(jnp.float32)
    filters = filt_t.shape[0]
    taps_rows = jnp.concatenate(
        [jnp.zeros((filters, 1), jnp.float32), filt_t, jnp.zeros((filters, tap_count - 1), jnp.float32)],
        axis=1,
    )

    hyena_out = long_conv_out(
        rel, mr_gates, prev_mr, mr_feat, prev_z, z_lo, z_hi, mr_skip[None, :], taps_rows
    )
    rows_ids = jnp.arange(total_req, dtype=jnp.int32)
    owner = jnp.sum(
        jnp.where(decode_row[None, :] == rows_ids[:, None], rows_ids[None, :], 0), axis=1
    )
    last_pos = pick_entries(req_ends, owner)
    first_pos = jnp.where(owner > 0, pick_entries(req_ends, jnp.maximum(owner - 1, 0)) + 1, 0)
    tail_cache = cut_tails_all(recv_lo, recv_hi, last_pos - tail_len + 1, first_pos, tail_len)
    return (hyena_out, tail_cache)


def solution(mesh):
    placed = (
        P(("groups", "seq"), None),
        P(("groups", "seq"), None),
        P(),
        P(),
        P(),
        P(),
        P(),
        P("groups"),
        P("groups"),
    )
    return jax.shard_map(
        local,
        mesh=mesh,
        in_specs=placed,
        out_specs=(P(("groups", "seq"), None), P("groups", None, "seq")),
        check_vma=False,
    )
```

```python
import functools

import jax
import jax.numpy as jnp
from jax import lax
from jax.sharding import PartitionSpec as P
from jax.experimental import pallas as pl
from jax.experimental.pallas import tpu as pltpu

ENDS_MAX = 4


def passed_along(x, axis, by):
    length = lax.axis_size(axis)
    pairs = [(i, i + by) for i in range(length) if 0 <= i + by < length]
    return lax.ppermute(x, axis, pairs)


def request_of(positions, req_ends):
    return jnp.sum((req_ends[None, :] < positions[:, None]).astype(jnp.int32), axis=1)


def short_conv(values, weights, segment):
    length = weights.shape[0]
    out_count = values.shape[0] - length + 1
    latest = length - 1
    current = segment[latest:]
    summed = values[latest:].astype(jnp.float32) * weights[0].astype(jnp.float32)
    for lag_step in range(1, length):
        earlier = values[latest - lag_step : latest - lag_step + out_count].astype(jnp.float32)
        same_req = segment[latest - lag_step : latest - lag_step + out_count] == current
        summed = summed + jnp.where(
            same_req[:, None], earlier * weights[lag_step].astype(jnp.float32), 0.0
        )
    return summed


HALO = 32
TILE = 512
GROUP_LANES = 128
WINDOW = 144


def short_conv_rows(x, w, first, dist_all):
    rows = x.shape[0]
    dist = dist_all[first:rows, :]
    acc = x[first:rows, :] * w[0:1, :].astype(jnp.float32)
    for lag in range(1, w.shape[0]):
        term = x[first - lag : rows - lag, :] * w[lag : lag + 1, :].astype(jnp.float32)
        acc = acc + jnp.where(dist >= lag, term, 0.0)
    return acc


def rel_dist(rel_ref, base, count):
    index = base + lax.broadcasted_iota(jnp.int32, (count, 1), 0)
    return index - rel_ref[base : base + count, :]


def chain_kernel(rel_ref, sq, sk, sv, hq, hk, hv, mk, gk_h, fq, fk, fv, filt_ref, wk, wv,
                 z2_ref, xq, xk, xv, xb, zs, ys, group_ch, base):
    rows, tile = xq.shape
    dist_ref = rel_dist(rel_ref, base, rows)
    filters = filt_ref.shape[1]
    lane_ch = pl.program_id(0) * tile + lax.broadcasted_iota(jnp.int32, (filters, tile), 1)
    spread = (lane_ch // group_ch == lax.broadcasted_iota(jnp.int32, (filters, tile), 0))
    filt = jnp.dot(filt_ref[...], spread.astype(filt_ref.dtype), preferred_element_type=jnp.float32)
    for main, halo, x in ((sq, hq, xq), (sk, hk, xk), (sv, hv, xv), (mk, gk_h, xb)):
        reach = halo.shape[0]
        if reach < HALO:
            x[0 : HALO - reach, :] = jnp.zeros((HALO - reach, x.shape[1]), jnp.float32)
        x[HALO - reach : HALO, :] = halo[...].astype(jnp.float32)
        x[HALO:rows, :] = main[...].astype(jnp.float32)

    k1 = short_conv_rows(xk, fk, 16, dist_ref)
    v1 = short_conv_rows(xv, fv, 16, dist_ref)
    zs[16:rows, :] = (k1 * v1).astype(jnp.bfloat16).astype(jnp.float32)
    q1 = short_conv_rows(xq, fq, 24, dist_ref)
    c1 = short_conv_rows(zs, filt, 24, dist_ref)
    ys[24:rows, :] = (q1 * c1).astype(jnp.bfloat16).astype(jnp.float32)
    v2 = short_conv_rows(ys, wv, HALO, dist_ref)
    k2 = short_conv_rows(xb, wk, HALO, dist_ref)
    z2 = (k2 * v2).astype(jnp.bfloat16)
    chunk = z2_ref.shape[2]
    for i in range(z2_ref.shape[0]):
        z2_ref[i] = z2[:, i * chunk : (i + 1) * chunk]


def short_chain(rel, se_streams, se_halo, mr_gates, mr_halo, se_feat, se_filt, mr_feat, shards, half):
    tok_rows = se_streams.shape[0] // 2
    channels = mr_gates.shape[1] // 2
    steps = channels // TILE
    rows = tok_rows + HALO
    taps = se_feat.shape[0]
    chunk = channels // shards

    def col(part, row_block=half):
        return lambda j: (row_block, j + part * steps)

    def halo_spec(halo, part):
        if halo.shape[0] < HALO:
            return pl.BlockSpec((halo.shape[0], TILE), col(part, 0))
        return pl.BlockSpec((HALO, TILE), col(part, half * tok_rows // HALO - 1))

    main = [pl.BlockSpec((tok_rows, TILE), col(p)) for p in range(3)]
    halo = [halo_spec(se_halo, p) for p in range(3)]
    wts = [pl.BlockSpec((taps, TILE), col(p, 0)) for p in range(3)]
    return pl.pallas_call(
        functools.partial(
            chain_kernel, group_ch=channels // se_filt.shape[1], base=half * tok_rows + tok_rows - HALO
        ),
        grid=(steps,),
        in_specs=[pl.BlockSpec(rel.shape, lambda j: (0, 0))] + main + halo
        + [main[1], halo_spec(mr_halo, 1)] + wts
        + [pl.BlockSpec(se_filt.shape, lambda j: (0, 0)), wts[1], wts[2]],
        out_specs=pl.BlockSpec((TILE // chunk, tok_rows, chunk), lambda j: (j, 0, 0)),
        out_shape=jax.ShapeDtypeStruct((shards, tok_rows, chunk), jnp.bfloat16),
        scratch_shapes=[pltpu.VMEM((rows, TILE), jnp.float32) for _ in range(6)],
    )(rel, se_streams, se_streams, se_streams, se_halo, se_halo, se_halo, mr_gates,
      mr_halo, se_feat, se_feat, se_feat, se_filt, mr_feat, mr_feat)


def long_kernel(rel_ref, mg_ref, mh_ref, wq_ref, prev_ref, lo_ref, hi_ref, skip_ref,
                filt_ref, out_ref, xa, group_ch):
    rows = xa.shape[0]
    reach = mh_ref.shape[0]
    xa[HALO - reach : HALO, :] = mh_ref[...].astype(jnp.float32)
    xa[HALO:rows, :] = mg_ref[...].astype(jnp.float32)
    blk = lo_ref.shape[1]
    q2 = short_conv_rows(xa, wq_ref, HALO, rel_dist(rel_ref, blk - HALO, rows))
    blk = lo_ref.shape[1]
    tile = lo_ref.shape[2]
    taps_n, filters = filt_ref.shape
    width = 2 * taps_n
    local_groups = tile // group_ch
    pick = lax.broadcasted_iota(jnp.int32, (local_groups, filters), 1) == (
        pl.program_id(0) * local_groups + lax.broadcasted_iota(jnp.int32, (local_groups, filters), 0)
    )
    cols = lax.dot_general(
        pick.astype(filt_ref.dtype), filt_ref[...], (((1,), (1,)), ((), ())),
        preferred_element_type=jnp.float32,
    ).astype(filt_ref.dtype)
    flip = lax.broadcasted_iota(jnp.int32, (taps_n, width), 1) == (
        taps_n - lax.broadcasted_iota(jnp.int32, (taps_n, width), 0)
    )
    u_val = jnp.dot(cols, flip.astype(filt_ref.dtype), preferred_element_type=jnp.float32)
    per_group = tile // local_groups
    lo = lo_ref[0]
    hi = hi_ref[0]
    windows = (jnp.concatenate([prev_ref[0], lo], axis=0), jnp.concatenate([lo, hi], axis=0))
    masks = [
        lax.broadcasted_iota(jnp.int32, (1, width), 1) + b * blk >= rel_ref[(b + 1) * blk : (b + 2) * blk, :]
        for b in range(2)
    ]
    lane_grp = lax.broadcasted_iota(jnp.int32, (1, GROUP_LANES), 1) // per_group
    halves = tile // GROUP_LANES
    groups_half = GROUP_LANES // per_group
    acc = [[jnp.zeros((blk, GROUP_LANES), jnp.float32) for _ in range(halves)] for _ in range(2)]
    for g in range(local_groups):
        half = g // groups_half
        row = jnp.broadcast_to(u_val[g : g + 1, :], (blk, width))
        taps = pltpu.roll(row, 0, 1, stride=1, stride_axis=0)
        for b in range(2):
            mat = jnp.where(masks[b], taps, 0.0).astype(jnp.bfloat16)
            part = windows[b][:, half * GROUP_LANES : (half + 1) * GROUP_LANES]
            res = jnp.dot(mat, part, preferred_element_type=jnp.float32)
            acc[b][half] = jnp.where(lane_grp == g % groups_half, res, acc[b][half])
    conv = jnp.concatenate([jnp.concatenate(acc[b], axis=1) for b in range(2)], axis=0)
    z = jnp.concatenate([lo, hi], axis=0).astype(jnp.float32)
    mixed = (conv + skip_ref[...].astype(jnp.float32) * z).astype(jnp.bfloat16)
    out_ref[...] = (q2 * mixed.astype(jnp.float32)).astype(jnp.bfloat16)


def long_conv_out(rel, mr_gates, mr_halo, mr_feat, prev_z, z_lo, z_hi, skip, mr_filter):
    steps, blk, lanes = z_lo.shape
    tok_rows = 2 * blk
    channels = steps * lanes
    piece = pl.BlockSpec((1, blk, lanes), lambda j: (j, 0, 0))
    return pl.pallas_call(
        functools.partial(long_kernel, group_ch=channels // mr_filter.shape[1]),
        grid=(steps,),
        in_specs=[
            pl.BlockSpec(rel.shape, lambda j: (0, 0)),
            pl.BlockSpec((tok_rows, lanes), lambda j: (0, j)),
            pl.BlockSpec((mr_halo.shape[0], lanes), lambda j: (0, j)),
            pl.BlockSpec((mr_feat.shape[0], lanes), lambda j: (0, j)),
            piece,
            piece,
            piece,
            pl.BlockSpec((1, lanes), lambda j: (0, j)),
            pl.BlockSpec(mr_filter.shape, lambda j: (0, 0)),
        ],
        out_specs=pl.BlockSpec((tok_rows, lanes), lambda j: (0, j)),
        out_shape=jax.ShapeDtypeStruct((tok_rows, channels), jnp.bfloat16),
        scratch_shapes=[pltpu.VMEM((tok_rows + HALO, lanes), jnp.float32)],
    )(rel, mr_gates, mr_halo, mr_feat, prev_z, z_lo, z_hi, skip, mr_filter)


def tail_kernel(begin_ref, first_ref, lo_ref, hi_ref, out_ref, z_all):
    shards, blk, lanes = lo_ref.shape
    tail_len = out_ref.shape[0]
    total = z_all.shape[0]
    for src in range(shards):
        z_all[2 * src * blk : (2 * src + 1) * blk, :] = lo_ref[src].astype(jnp.float32)
        z_all[(2 * src + 1) * blk : (2 * src + 2) * blk, :] = hi_ref[src].astype(jnp.float32)
    for t in range(out_ref.shape[1]):
        begin = begin_ref[t]
        start = jnp.clip((begin // 16) * 16, 0, total - WINDOW)
        shift = begin - start
        window = z_all[pl.ds(pl.multiple_of(start, 16), WINDOW), :]
        moved = pltpu.roll(window, (WINDOW - shift) % WINDOW, 0)[:tail_len]
        pos = begin + lax.broadcasted_iota(jnp.int32, (tail_len, 1), 0)
        out_ref[:, t, :] = jnp.where(pos >= first_ref[t], moved, 0.0).astype(out_ref.dtype)


def cut_tails_all(z_lo, z_hi, begins, firsts, tail_len):
    shards, blk, lanes = z_lo.shape
    count = begins.shape[0]
    smem = pl.BlockSpec(memory_space=pltpu.SMEM)
    vmem = pl.BlockSpec(memory_space=pltpu.VMEM)
    out = pl.pallas_call(
        tail_kernel,
        in_specs=[smem, smem, vmem, vmem],
        out_specs=vmem,
        out_shape=jax.ShapeDtypeStruct((tail_len, count, lanes), z_lo.dtype),
        scratch_shapes=[pltpu.VMEM((2 * shards * blk, lanes), jnp.float32)],
    )(begins, firsts, z_lo, z_hi)
    return jnp.transpose(out, (1, 0, 2))


def seg_start(positions, req_ends):
    seg = request_of(positions, req_ends)
    prev_end = jnp.where(seg > 0, pick_entries(req_ends, jnp.maximum(seg - 1, 0)), -1)
    return prev_end + 1


def pick_entries(lookup_table, indices):
    hits = indices[:, None] == jnp.arange(lookup_table.shape[0], dtype=jnp.int32)[None, :]
    return jnp.sum(jnp.where(hits, lookup_table[None, :], 0), axis=1)


def local(
    se_streams, mr_gates, se_feat, se_filter, mr_feat, mr_filter, mr_skip, req_ends, decode_row
):
    tok_rows = se_streams.shape[0]
    channels = mr_gates.shape[1] // 2
    shards = lax.axis_size("seq")
    device = lax.axis_index("seq")
    offset = device * tok_rows
    reach_rows = se_feat.shape[0] - 1
    tap_count = mr_filter.shape[0]
    tail_len = tap_count - 1
    group_ch = channels // se_filter.shape[1]
    total_req = req_ends.shape[0]
    slot_total = ENDS_MAX + 1
    rim_depth = 2 * reach_rows
    prev_se, prev_mr = passed_along(
        (se_streams[tok_rows - 3 * reach_rows :], mr_gates[tok_rows - reach_rows :]), "seq", 1
    )
    blk = tok_rows // 2
    se_filt = se_filter

    window_pos = offset - blk + jnp.arange(tok_rows + blk, dtype=jnp.int32)
    rel = (seg_start(window_pos, req_ends) - (offset - blk))[:, None]
    z_hi = short_chain(
        rel, se_streams, se_streams, mr_gates, mr_gates, se_feat, se_filt, mr_feat, shards, 1
    )
    prev_z = passed_along(z_hi, "seq", 1)
    z_hi, prev_se, prev_mr = lax.optimization_barrier((z_hi, prev_se, prev_mr))
    recv_hi = lax.all_to_all(z_hi, "seq", split_axis=0, concat_axis=0, tiled=True)
    z_lo = short_chain(
        rel, se_streams, prev_se, mr_gates, prev_mr, se_feat, se_filt, mr_feat, shards, 0
    )
    z_lo, recv_hi, prev_z = lax.optimization_barrier((z_lo, recv_hi, prev_z))
    recv_lo = lax.all_to_all(z_lo, "seq", split_axis=0, concat_axis=0, tiled=True)
    hyena_out = long_conv_out(
        rel, mr_gates, prev_mr, mr_feat, prev_z, z_lo, z_hi, mr_skip[None, :], mr_filter
    )
    rows_ids = jnp.arange(total_req, dtype=jnp.int32)
    owner = jnp.sum(
        jnp.where(decode_row[None, :] == rows_ids[:, None], rows_ids[None, :], 0), axis=1
    )
    last_pos = pick_entries(req_ends, owner)
    first_pos = jnp.where(owner > 0, pick_entries(req_ends, jnp.maximum(owner - 1, 0)) + 1, 0)
    tail_cache = cut_tails_all(recv_lo, recv_hi, last_pos - tail_len + 1, first_pos, tail_len)
    return (hyena_out, tail_cache)


def solution(mesh):
    placed = (
        P(("groups", "seq"), None),
        P(("groups", "seq"), None),
        P(),
        P(),
        P(),
        P(),
        P(),
        P("groups"),
        P("groups"),
    )
    return jax.shard_map(
        local,
        mesh=mesh,
        in_specs=placed,
        out_specs=(P(("groups", "seq"), None), P("groups", None, "seq")),
        check_vma=False,
    )
```

```python
import functools

import jax
import jax.numpy as jnp
from jax import lax
from jax.sharding import PartitionSpec as P
from jax.experimental import pallas as pl
from jax.experimental.pallas import tpu as pltpu

ENDS_MAX = 4


def passed_along(x, axis, by):
    length = lax.axis_size(axis)
    pairs = [(i, i + by) for i in range(length) if 0 <= i + by < length]
    return lax.ppermute(x, axis, pairs)


def request_of(positions, req_ends):
    return jnp.sum((req_ends[None, :] < positions[:, None]).astype(jnp.int32), axis=1)


def short_conv(values, weights, segment):
    length = weights.shape[0]
    out_count = values.shape[0] - length + 1
    latest = length - 1
    current = segment[latest:]
    summed = values[latest:].astype(jnp.float32) * weights[0].astype(jnp.float32)
    for lag_step in range(1, length):
        earlier = values[latest - lag_step : latest - lag_step + out_count].astype(jnp.float32)
        same_req = segment[latest - lag_step : latest - lag_step + out_count] == current
        summed = summed + jnp.where(
            same_req[:, None], earlier * weights[lag_step].astype(jnp.float32), 0.0
        )
    return summed


HALO = 32
TILE = 512
GROUP_LANES = 128
WINDOW = 144


def short_conv_rows(x, w, first, dist_all):
    rows = x.shape[0]
    dist = dist_all[first:rows, :]
    acc = x[first:rows, :] * w[0:1, :].astype(jnp.float32)
    for lag in range(1, w.shape[0]):
        term = x[first - lag : rows - lag, :] * w[lag : lag + 1, :].astype(jnp.float32)
        acc = acc + jnp.where(dist >= lag, term, 0.0)
    return acc


def rel_dist(rel_ref, base, count):
    index = base + lax.broadcasted_iota(jnp.int32, (count, 1), 0)
    return index - rel_ref[base : base + count, :]


def chain_kernel(rel_ref, sq, sk, sv, hq, hk, hv, mk, gk_h, fq, fk, fv, filt_ref, wk, wv,
                 z2_ref, xq, xk, xv, xb, zs, ys, group_ch, base):
    rows, tile = xq.shape
    dist_ref = rel_dist(rel_ref, base, rows)
    filters = filt_ref.shape[1]
    lane_ch = pl.program_id(0) * tile + lax.broadcasted_iota(jnp.int32, (filters, tile), 1)
    spread = (lane_ch // group_ch == lax.broadcasted_iota(jnp.int32, (filters, tile), 0))
    filt = jnp.dot(filt_ref[...], spread.astype(filt_ref.dtype), preferred_element_type=jnp.float32)
    for main, halo, x in ((sq, hq, xq), (sk, hk, xk), (sv, hv, xv), (mk, gk_h, xb)):
        reach = halo.shape[0]
        if reach < HALO:
            x[0 : HALO - reach, :] = jnp.zeros((HALO - reach, x.shape[1]), jnp.float32)
        x[HALO - reach : HALO, :] = halo[...].astype(jnp.float32)
        x[HALO:rows, :] = main[...].astype(jnp.float32)

    k1 = short_conv_rows(xk, fk, 16, dist_ref)
    v1 = short_conv_rows(xv, fv, 16, dist_ref)
    zs[16:rows, :] = (k1 * v1).astype(jnp.bfloat16).astype(jnp.float32)
    q1 = short_conv_rows(xq, fq, 24, dist_ref)
    c1 = short_conv_rows(zs, filt, 24, dist_ref)
    ys[24:rows, :] = (q1 * c1).astype(jnp.bfloat16).astype(jnp.float32)
    v2 = short_conv_rows(ys, wv, HALO, dist_ref)
    k2 = short_conv_rows(xb, wk, HALO, dist_ref)
    z2 = (k2 * v2).astype(jnp.bfloat16)
    chunk = z2_ref.shape[2]
    for i in range(z2_ref.shape[0]):
        z2_ref[i] = z2[:, i * chunk : (i + 1) * chunk]


def short_chain(rel, se_streams, se_halo, mr_gates, mr_halo, se_feat, se_filt, mr_feat, shards, half):
    tok_rows = se_streams.shape[0] // 2
    channels = mr_gates.shape[1] // 2
    steps = channels // TILE
    rows = tok_rows + HALO
    taps = se_feat.shape[0]
    chunk = channels // shards

    def col(part, row_block=half):
        return lambda j: (row_block, j + part * steps)

    def halo_spec(halo, part):
        if halo.shape[0] < HALO:
            return pl.BlockSpec((halo.shape[0], TILE), col(part, 0))
        return pl.BlockSpec((HALO, TILE), col(part, half * tok_rows // HALO - 1))

    main = [pl.BlockSpec((tok_rows, TILE), col(p)) for p in range(3)]
    halo = [halo_spec(se_halo, p) for p in range(3)]
    wts = [pl.BlockSpec((taps, TILE), col(p, 0)) for p in range(3)]
    return pl.pallas_call(
        functools.partial(
            chain_kernel, group_ch=channels // se_filt.shape[1], base=half * tok_rows + tok_rows - HALO
        ),
        grid=(steps,),
        in_specs=[pl.BlockSpec(rel.shape, lambda j: (0, 0))] + main + halo
        + [main[1], halo_spec(mr_halo, 1)] + wts
        + [pl.BlockSpec(se_filt.shape, lambda j: (0, 0)), wts[1], wts[2]],
        out_specs=pl.BlockSpec((TILE // chunk, tok_rows, chunk), lambda j: (j, 0, 0)),
        out_shape=jax.ShapeDtypeStruct((shards, tok_rows, chunk), jnp.bfloat16),
        scratch_shapes=[pltpu.VMEM((rows, TILE), jnp.float32) for _ in range(6)],
    )(rel, se_streams, se_streams, se_streams, se_halo, se_halo, se_halo, mr_gates,
      mr_halo, se_feat, se_feat, se_feat, se_filt, mr_feat, mr_feat)


def long_kernel(rel_ref, mg_ref, mh_ref, wq_ref, prev_ref, lo_ref, hi_ref, skip_ref,
                u_ref, out_ref, xa):
    rows = xa.shape[0]
    reach = mh_ref.shape[0]
    xa[HALO - reach : HALO, :] = mh_ref[...].astype(jnp.float32)
    xa[HALO:rows, :] = mg_ref[...].astype(jnp.float32)
    blk = lo_ref.shape[1]
    q2 = short_conv_rows(xa, wq_ref, HALO, rel_dist(rel_ref, blk - HALO, rows))
    blk = lo_ref.shape[1]
    tile = lo_ref.shape[2]
    width = u_ref.shape[1]
    per_group = tile // u_ref.shape[0]
    lo = lo_ref[0]
    hi = hi_ref[0]
    windows = (jnp.concatenate([prev_ref[0], lo], axis=0), jnp.concatenate([lo, hi], axis=0))
    masks = [
        lax.broadcasted_iota(jnp.int32, (1, width), 1) + b * blk >= rel_ref[(b + 1) * blk : (b + 2) * blk, :]
        for b in range(2)
    ]
    lane_grp = lax.broadcasted_iota(jnp.int32, (1, GROUP_LANES), 1) // per_group
    halves = tile // GROUP_LANES
    groups_half = GROUP_LANES // per_group
    acc = [[jnp.zeros((blk, GROUP_LANES), jnp.float32) for _ in range(halves)] for _ in range(2)]
    for g in range(u_ref.shape[0]):
        half = g // groups_half
        row = jnp.broadcast_to(u_ref[g : g + 1, :], (blk, width))
        taps = pltpu.roll(row, 0, 1, stride=1, stride_axis=0)
        for b in range(2):
            mat = jnp.where(masks[b], taps, 0.0).astype(jnp.bfloat16)
            part = windows[b][:, half * GROUP_LANES : (half + 1) * GROUP_LANES]
            res = jnp.dot(mat, part, preferred_element_type=jnp.float32)
            acc[b][half] = jnp.where(lane_grp == g % groups_half, res, acc[b][half])
    conv = jnp.concatenate([jnp.concatenate(acc[b], axis=1) for b in range(2)], axis=0)
    z = jnp.concatenate([lo, hi], axis=0).astype(jnp.float32)
    mixed = (conv + skip_ref[...].astype(jnp.float32) * z).astype(jnp.bfloat16)
    out_ref[...] = (q2 * mixed.astype(jnp.float32)).astype(jnp.bfloat16)


def long_conv_out(rel, mr_gates, mr_halo, mr_feat, prev_z, z_lo, z_hi, skip, taps_rows):
    steps, blk, lanes = z_lo.shape
    tok_rows = 2 * blk
    channels = steps * lanes
    per_group = channels // taps_rows.shape[0]
    piece = pl.BlockSpec((1, blk, lanes), lambda j: (j, 0, 0))
    return pl.pallas_call(
        long_kernel,
        grid=(steps,),
        in_specs=[
            pl.BlockSpec(rel.shape, lambda j: (0, 0)),
            pl.BlockSpec((tok_rows, lanes), lambda j: (0, j)),
            pl.BlockSpec((mr_halo.shape[0], lanes), lambda j: (0, j)),
            pl.BlockSpec((mr_feat.shape[0], lanes), lambda j: (0, j)),
            piece,
            piece,
            piece,
            pl.BlockSpec((1, lanes), lambda j: (0, j)),
            pl.BlockSpec((lanes // per_group, taps_rows.shape[1]), lambda j: (j, 0)),
        ],
        out_specs=pl.BlockSpec((tok_rows, lanes), lambda j: (0, j)),
        out_shape=jax.ShapeDtypeStruct((tok_rows, channels), jnp.bfloat16),
        scratch_shapes=[pltpu.VMEM((tok_rows + HALO, lanes), jnp.float32)],
    )(rel, mr_gates, mr_halo, mr_feat, prev_z, z_lo, z_hi, skip, taps_rows)


def tail_kernel(begin_ref, first_ref, lo_ref, hi_ref, out_ref, z_all):
    shards, blk, lanes = lo_ref.shape
    tail_len = out_ref.shape[0]
    total = z_all.shape[0]
    for src in range(shards):
        z_all[2 * src * blk : (2 * src + 1) * blk, :] = lo_ref[src]
        z_all[(2 * src + 1) * blk : (2 * src + 2) * blk, :] = hi_ref[src]
    for t in range(out_ref.shape[1]):
        begin = begin_ref[t]
        start = jnp.clip((begin // 16) * 16, 0, total - WINDOW)
        shift = begin - start
        window = z_all[pl.ds(pl.multiple_of(start, 16), WINDOW), :].astype(jnp.float32)
        moved = pltpu.roll(window, (WINDOW - shift) % WINDOW, 0)[:tail_len]
        pos = begin + lax.broadcasted_iota(jnp.int32, (tail_len, 1), 0)
        out_ref[:, t, :] = jnp.where(pos >= first_ref[t], moved, 0.0).astype(out_ref.dtype)


def cut_tails_all(z_lo, z_hi, begins, firsts, tail_len):
    shards, blk, lanes = z_lo.shape
    count = begins.shape[0]
    smem = pl.BlockSpec(memory_space=pltpu.SMEM)
    vmem = pl.BlockSpec(memory_space=pltpu.VMEM)
    out = pl.pallas_call(
        tail_kernel,
        in_specs=[smem, smem, vmem, vmem],
        out_specs=vmem,
        out_shape=jax.ShapeDtypeStruct((tail_len, count, lanes), z_lo.dtype),
        scratch_shapes=[pltpu.VMEM((2 * shards * blk, lanes), z_lo.dtype)],
    )(begins, firsts, z_lo, z_hi)
    return jnp.transpose(out, (1, 0, 2))


def seg_start(positions, req_ends):
    seg = request_of(positions, req_ends)
    prev_end = jnp.where(seg > 0, pick_entries(req_ends, jnp.maximum(seg - 1, 0)), -1)
    return prev_end + 1


def pick_entries(lookup_table, indices):
    hits = indices[:, None] == jnp.arange(lookup_table.shape[0], dtype=jnp.int32)[None, :]
    return jnp.sum(jnp.where(hits, lookup_table[None, :], 0), axis=1)


def local(
    se_streams, mr_gates, se_feat, se_filter, mr_feat, mr_filter, mr_skip, req_ends, decode_row
):
    tok_rows = se_streams.shape[0]
    channels = mr_gates.shape[1] // 2
    shards = lax.axis_size("seq")
    device = lax.axis_index("seq")
    offset = device * tok_rows
    reach_rows = se_feat.shape[0] - 1
    tap_count = mr_filter.shape[0]
    tail_len = tap_count - 1
    group_ch = channels // se_filter.shape[1]
    total_req = req_ends.shape[0]
    slot_total = ENDS_MAX + 1
    rim_depth = 2 * reach_rows
    prev_se, prev_mr = passed_along(
        (se_streams[tok_rows - 3 * reach_rows :], mr_gates[tok_rows - reach_rows :]), "seq", 1
    )
    blk = tok_rows // 2
    se_filt = se_filter

    window_pos = offset - blk + jnp.arange(tok_rows + blk, dtype=jnp.int32)
    rel = (seg_start(window_pos, req_ends) - (offset - blk))[:, None]
    z_hi = short_chain(
        rel, se_streams, se_streams, mr_gates, mr_gates, se_feat, se_filt, mr_feat, shards, 1
    )
    prev_z = passed_along(z_hi, "seq", 1)
    z_hi, prev_se, prev_mr = lax.optimization_barrier((z_hi, prev_se, prev_mr))
    recv_hi = lax.all_to_all(z_hi, "seq", split_axis=0, concat_axis=0, tiled=True)
    z_lo = short_chain(
        rel, se_streams, prev_se, mr_gates, prev_mr, se_feat, se_filt, mr_feat, shards, 0
    )
    z_lo, recv_hi, prev_z = lax.optimization_barrier((z_lo, recv_hi, prev_z))
    recv_lo = lax.all_to_all(z_lo, "seq", split_axis=0, concat_axis=0, tiled=True)
    filt_t = mr_filter[::-1].T.astype(jnp.float32)
    filters = filt_t.shape[0]
    taps_rows = jnp.concatenate(
        [jnp.zeros((filters, 1), jnp.float32), filt_t, jnp.zeros((filters, tap_count - 1), jnp.float32)],
        axis=1,
    )

    hyena_out = long_conv_out(
        rel, mr_gates, prev_mr, mr_feat, prev_z, z_lo, z_hi, mr_skip[None, :], taps_rows
    )
    rows_ids = jnp.arange(total_req, dtype=jnp.int32)
    owner = jnp.sum(
        jnp.where(decode_row[None, :] == rows_ids[:, None], rows_ids[None, :], 0), axis=1
    )
    last_pos = pick_entries(req_ends, owner)
    first_pos = jnp.where(owner > 0, pick_entries(req_ends, jnp.maximum(owner - 1, 0)) + 1, 0)
    tail_cache = cut_tails_all(recv_lo, recv_hi, last_pos - tail_len + 1, first_pos, tail_len)
    return (hyena_out, tail_cache)


def solution(mesh):
    placed = (
        P(("groups", "seq"), None),
        P(("groups", "seq"), None),
        P(),
        P(),
        P(),
        P(),
        P(),
        P("groups"),
        P("groups"),
    )
    return jax.shard_map(
        local,
        mesh=mesh,
        in_specs=placed,
        out_specs=(P(("groups", "seq"), None), P("groups", None, "seq")),
        check_vma=False,
    )
```

```python
import functools

import jax
import jax.numpy as jnp
from jax import lax
from jax.sharding import PartitionSpec as P
from jax.experimental import pallas as pl
from jax.experimental.pallas import tpu as pltpu

ENDS_MAX = 4


def passed_along(x, axis, by):
    length = lax.axis_size(axis)
    pairs = [(i, i + by) for i in range(length) if 0 <= i + by < length]
    return lax.ppermute(x, axis, pairs)


def request_of(positions, req_ends):
    return jnp.sum((req_ends[None, :] < positions[:, None]).astype(jnp.int32), axis=1)


def short_conv(values, weights, segment):
    length = weights.shape[0]
    out_count = values.shape[0] - length + 1
    latest = length - 1
    current = segment[latest:]
    summed = values[latest:].astype(jnp.float32) * weights[0].astype(jnp.float32)
    for lag_step in range(1, length):
        earlier = values[latest - lag_step : latest - lag_step + out_count].astype(jnp.float32)
        same_req = segment[latest - lag_step : latest - lag_step + out_count] == current
        summed = summed + jnp.where(
            same_req[:, None], earlier * weights[lag_step].astype(jnp.float32), 0.0
        )
    return summed


HALO = 32
TILE = 512
GROUP_LANES = 128
WINDOW = 144


def short_conv_rows(x, w, first, dist_all):
    rows = x.shape[0]
    dist = dist_all[first:rows, :]
    acc = x[first:rows, :] * w[0:1, :].astype(jnp.float32)
    for lag in range(1, w.shape[0]):
        term = x[first - lag : rows - lag, :] * w[lag : lag + 1, :].astype(jnp.float32)
        acc = acc + jnp.where(dist >= lag, term, 0.0)
    return acc


def rel_dist(rel_ref, base, count):
    index = base + lax.broadcasted_iota(jnp.int32, (count, 1), 0)
    return index - rel_ref[base : base + count, :]


def chain_kernel(rel_ref, sq, sk, sv, hq, hk, hv, mk, gk_h, fq, fk, fv, filt_ref, wk, wv,
                 z2_ref, xq, xk, xv, xb, zs, ys, group_ch, base):
    rows, tile = xq.shape
    dist_ref = rel_dist(rel_ref, base, rows)
    filters = filt_ref.shape[1]
    lane_ch = pl.program_id(0) * tile + lax.broadcasted_iota(jnp.int32, (filters, tile), 1)
    spread = (lane_ch // group_ch == lax.broadcasted_iota(jnp.int32, (filters, tile), 0))
    filt = jnp.dot(filt_ref[...], spread.astype(filt_ref.dtype), preferred_element_type=jnp.float32)
    for main, halo, x in ((sq, hq, xq), (sk, hk, xk), (sv, hv, xv), (mk, gk_h, xb)):
        reach = halo.shape[0]
        if reach < HALO:
            x[0 : HALO - reach, :] = jnp.zeros((HALO - reach, x.shape[1]), jnp.float32)
        x[HALO - reach : HALO, :] = halo[...].astype(jnp.float32)
        x[HALO:rows, :] = main[...].astype(jnp.float32)

    k1 = short_conv_rows(xk, fk, 16, dist_ref)
    v1 = short_conv_rows(xv, fv, 16, dist_ref)
    zs[16:rows, :] = (k1 * v1).astype(jnp.bfloat16).astype(jnp.float32)
    q1 = short_conv_rows(xq, fq, 24, dist_ref)
    c1 = short_conv_rows(zs, filt, 24, dist_ref)
    ys[24:rows, :] = (q1 * c1).astype(jnp.bfloat16).astype(jnp.float32)
    v2 = short_conv_rows(ys, wv, HALO, dist_ref)
    k2 = short_conv_rows(xb, wk, HALO, dist_ref)
    z2 = (k2 * v2).astype(jnp.bfloat16)
    chunk = z2_ref.shape[2]
    for i in range(z2_ref.shape[0]):
        z2_ref[i] = z2[:, i * chunk : (i + 1) * chunk]


def short_chain(rel, se_streams, se_halo, mr_gates, mr_halo, se_feat, se_filt, mr_feat, shards, half):
    tok_rows = se_streams.shape[0] // 2
    channels = mr_gates.shape[1] // 2
    steps = channels // TILE
    rows = tok_rows + HALO
    taps = se_feat.shape[0]
    chunk = channels // shards

    def col(part, row_block=half):
        return lambda j: (row_block, j + part * steps)

    def halo_spec(halo, part):
        if halo.shape[0] < HALO:
            return pl.BlockSpec((halo.shape[0], TILE), col(part, 0))
        return pl.BlockSpec((HALO, TILE), col(part, half * tok_rows // HALO - 1))

    main = [pl.BlockSpec((tok_rows, TILE), col(p)) for p in range(3)]
    halo = [halo_spec(se_halo, p) for p in range(3)]
    wts = [pl.BlockSpec((taps, TILE), col(p, 0)) for p in range(3)]
    return pl.pallas_call(
        functools.partial(
            chain_kernel, group_ch=channels // se_filt.shape[1], base=half * tok_rows + tok_rows - HALO
        ),
        grid=(steps,),
        in_specs=[pl.BlockSpec(rel.shape, lambda j: (0, 0))] + main + halo
        + [main[1], halo_spec(mr_halo, 1)] + wts
        + [pl.BlockSpec(se_filt.shape, lambda j: (0, 0)), wts[1], wts[2]],
        out_specs=pl.BlockSpec((TILE // chunk, tok_rows, chunk), lambda j: (j, 0, 0)),
        out_shape=jax.ShapeDtypeStruct((shards, tok_rows, chunk), jnp.bfloat16),
        scratch_shapes=[pltpu.VMEM((rows, TILE), jnp.float32) for _ in range(6)],
    )(rel, se_streams, se_streams, se_streams, se_halo, se_halo, se_halo, mr_gates,
      mr_halo, se_feat, se_feat, se_feat, se_filt, mr_feat, mr_feat)


def long_kernel(rel_ref, mg_ref, mh_ref, wq_ref, prev_ref, lo_ref, hi_ref, skip_ref,
                u_ref, out_ref, xa):
    rows = xa.shape[0]
    reach = mh_ref.shape[0]
    xa[HALO - reach : HALO, :] = mh_ref[...].astype(jnp.float32)
    xa[HALO:rows, :] = mg_ref[...].astype(jnp.float32)
    blk = lo_ref.shape[1]
    q2 = short_conv_rows(xa, wq_ref, HALO, rel_dist(rel_ref, blk - HALO, rows))
    blk = lo_ref.shape[1]
    tile = lo_ref.shape[2]
    width = u_ref.shape[1]
    per_group = tile // u_ref.shape[0]
    lo = lo_ref[0]
    hi = hi_ref[0]
    windows = (jnp.concatenate([prev_ref[0], lo], axis=0), jnp.concatenate([lo, hi], axis=0))
    masks = [
        lax.broadcasted_iota(jnp.int32, (1, width), 1) + b * blk >= rel_ref[(b + 1) * blk : (b + 2) * blk, :]
        for b in range(2)
    ]
    keep = [m.astype(jnp.bfloat16) for m in masks]
    lane_grp = lax.broadcasted_iota(jnp.int32, (1, GROUP_LANES), 1) // per_group
    halves = tile // GROUP_LANES
    groups_half = GROUP_LANES // per_group
    acc = [[jnp.zeros((blk, GROUP_LANES), jnp.float32) for _ in range(halves)] for _ in range(2)]
    for g in range(u_ref.shape[0]):
        half = g // groups_half
        row = jnp.broadcast_to(u_ref[g : g + 1, :], (blk, width))
        taps = pltpu.roll(row, 0, 1, stride=1, stride_axis=0).astype(jnp.bfloat16)
        for b in range(2):
            mat = taps * keep[b]
            part = windows[b][:, half * GROUP_LANES : (half + 1) * GROUP_LANES]
            res = jnp.dot(mat, part, preferred_element_type=jnp.float32)
            acc[b][half] = jnp.where(lane_grp == g % groups_half, res, acc[b][half])
    conv = jnp.concatenate([jnp.concatenate(acc[b], axis=1) for b in range(2)], axis=0)
    z = jnp.concatenate([lo, hi], axis=0).astype(jnp.float32)
    mixed = (conv + skip_ref[...].astype(jnp.float32) * z).astype(jnp.bfloat16)
    out_ref[...] = (q2 * mixed.astype(jnp.float32)).astype(jnp.bfloat16)


def long_conv_out(rel, mr_gates, mr_halo, mr_feat, prev_z, z_lo, z_hi, skip, taps_rows):
    steps, blk, lanes = z_lo.shape
    tok_rows = 2 * blk
    channels = steps * lanes
    per_group = channels // taps_rows.shape[0]
    piece = pl.BlockSpec((1, blk, lanes), lambda j: (j, 0, 0))
    return pl.pallas_call(
        long_kernel,
        grid=(steps,),
        in_specs=[
            pl.BlockSpec(rel.shape, lambda j: (0, 0)),
            pl.BlockSpec((tok_rows, lanes), lambda j: (0, j)),
            pl.BlockSpec((mr_halo.shape[0], lanes), lambda j: (0, j)),
            pl.BlockSpec((mr_feat.shape[0], lanes), lambda j: (0, j)),
            piece,
            piece,
            piece,
            pl.BlockSpec((1, lanes), lambda j: (0, j)),
            pl.BlockSpec((lanes // per_group, taps_rows.shape[1]), lambda j: (j, 0)),
        ],
        out_specs=pl.BlockSpec((tok_rows, lanes), lambda j: (0, j)),
        out_shape=jax.ShapeDtypeStruct((tok_rows, channels), jnp.bfloat16),
        scratch_shapes=[pltpu.VMEM((tok_rows + HALO, lanes), jnp.float32)],
    )(rel, mr_gates, mr_halo, mr_feat, prev_z, z_lo, z_hi, skip, taps_rows)


def tail_kernel(begin_ref, first_ref, lo_ref, hi_ref, out_ref, z_all):
    shards, blk, lanes = lo_ref.shape
    tail_len = out_ref.shape[0]
    total = z_all.shape[0]
    for src in range(shards):
        z_all[2 * src * blk : (2 * src + 1) * blk, :] = lo_ref[src]
        z_all[(2 * src + 1) * blk : (2 * src + 2) * blk, :] = hi_ref[src]
    for t in range(out_ref.shape[1]):
        begin = begin_ref[t]
        start = jnp.clip((begin // 16) * 16, 0, total - WINDOW)
        shift = begin - start
        window = z_all[pl.ds(pl.multiple_of(start, 16), WINDOW), :].astype(jnp.float32)
        moved = pltpu.roll(window, (WINDOW - shift) % WINDOW, 0)[:tail_len]
        pos = begin + lax.broadcasted_iota(jnp.int32, (tail_len, 1), 0)
        out_ref[:, t, :] = jnp.where(pos >= first_ref[t], moved, 0.0).astype(out_ref.dtype)


def cut_tails_all(z_lo, z_hi, begins, firsts, tail_len):
    shards, blk, lanes = z_lo.shape
    count = begins.shape[0]
    smem = pl.BlockSpec(memory_space=pltpu.SMEM)
    vmem = pl.BlockSpec(memory_space=pltpu.VMEM)
    out = pl.pallas_call(
        tail_kernel,
        in_specs=[smem, smem, vmem, vmem],
        out_specs=vmem,
        out_shape=jax.ShapeDtypeStruct((tail_len, count, lanes), z_lo.dtype),
        scratch_shapes=[pltpu.VMEM((2 * shards * blk, lanes), z_lo.dtype)],
    )(begins, firsts, z_lo, z_hi)
    return jnp.transpose(out, (1, 0, 2))


def seg_start(positions, req_ends):
    seg = request_of(positions, req_ends)
    prev_end = jnp.where(seg > 0, pick_entries(req_ends, jnp.maximum(seg - 1, 0)), -1)
    return prev_end + 1


def pick_entries(lookup_table, indices):
    hits = indices[:, None] == jnp.arange(lookup_table.shape[0], dtype=jnp.int32)[None, :]
    return jnp.sum(jnp.where(hits, lookup_table[None, :], 0), axis=1)


def local(
    se_streams, mr_gates, se_feat, se_filter, mr_feat, mr_filter, mr_skip, req_ends, decode_row
):
    tok_rows = se_streams.shape[0]
    channels = mr_gates.shape[1] // 2
    shards = lax.axis_size("seq")
    device = lax.axis_index("seq")
    offset = device * tok_rows
    reach_rows = se_feat.shape[0] - 1
    tap_count = mr_filter.shape[0]
    tail_len = tap_count - 1
    group_ch = channels // se_filter.shape[1]
    total_req = req_ends.shape[0]
    slot_total = ENDS_MAX + 1
    rim_depth = 2 * reach_rows
    prev_se, prev_mr = passed_along(
        (se_streams[tok_rows - 3 * reach_rows :], mr_gates[tok_rows - reach_rows :]), "seq", 1
    )
    blk = tok_rows // 2
    se_filt = se_filter

    window_pos = offset - blk + jnp.arange(tok_rows + blk, dtype=jnp.int32)
    rel = (seg_start(window_pos, req_ends) - (offset - blk))[:, None]
    z_hi = short_chain(
        rel, se_streams, se_streams, mr_gates, mr_gates, se_feat, se_filt, mr_feat, shards, 1
    )
    prev_z = passed_along(z_hi, "seq", 1)
    z_hi, prev_se, prev_mr = lax.optimization_barrier((z_hi, prev_se, prev_mr))
    recv_hi = lax.all_to_all(z_hi, "seq", split_axis=0, concat_axis=0, tiled=True)
    z_lo = short_chain(
        rel, se_streams, prev_se, mr_gates, prev_mr, se_feat, se_filt, mr_feat, shards, 0
    )
    z_lo, recv_hi, prev_z = lax.optimization_barrier((z_lo, recv_hi, prev_z))
    recv_lo = lax.all_to_all(z_lo, "seq", split_axis=0, concat_axis=0, tiled=True)
    filt_t = mr_filter[::-1].T.astype(jnp.float32)
    filters = filt_t.shape[0]
    taps_rows = jnp.concatenate(
        [jnp.zeros((filters, 1), jnp.float32), filt_t, jnp.zeros((filters, tap_count - 1), jnp.float32)],
        axis=1,
    )

    hyena_out = long_conv_out(
        rel, mr_gates, prev_mr, mr_feat, prev_z, z_lo, z_hi, mr_skip[None, :], taps_rows
    )
    rows_ids = jnp.arange(total_req, dtype=jnp.int32)
    owner = jnp.sum(
        jnp.where(decode_row[None, :] == rows_ids[:, None], rows_ids[None, :], 0), axis=1
    )
    last_pos = pick_entries(req_ends, owner)
    first_pos = jnp.where(owner > 0, pick_entries(req_ends, jnp.maximum(owner - 1, 0)) + 1, 0)
    tail_cache = cut_tails_all(recv_lo, recv_hi, last_pos - tail_len + 1, first_pos, tail_len)
    return (hyena_out, tail_cache)


def solution(mesh):
    placed = (
        P(("groups", "seq"), None),
        P(("groups", "seq"), None),
        P(),
        P(),
        P(),
        P(),
        P(),
        P("groups"),
        P("groups"),
    )
    return jax.shard_map(
        local,
        mesh=mesh,
        in_specs=placed,
        out_specs=(P(("groups", "seq"), None), P("groups", None, "seq")),
        check_vma=False,
    )
```

```python
import functools

import jax
import jax.numpy as jnp
from jax import lax
from jax.sharding import PartitionSpec as P
from jax.experimental import pallas as pl
from jax.experimental.pallas import tpu as pltpu

ENDS_MAX = 4


def passed_along(x, axis, by):
    length = lax.axis_size(axis)
    pairs = [(i, i + by) for i in range(length) if 0 <= i + by < length]
    return lax.ppermute(x, axis, pairs)


def request_of(positions, req_ends):
    return jnp.sum((req_ends[None, :] < positions[:, None]).astype(jnp.int32), axis=1)


def short_conv(values, weights, segment):
    length = weights.shape[0]
    out_count = values.shape[0] - length + 1
    latest = length - 1
    current = segment[latest:]
    summed = values[latest:].astype(jnp.float32) * weights[0].astype(jnp.float32)
    for lag_step in range(1, length):
        earlier = values[latest - lag_step : latest - lag_step + out_count].astype(jnp.float32)
        same_req = segment[latest - lag_step : latest - lag_step + out_count] == current
        summed = summed + jnp.where(
            same_req[:, None], earlier * weights[lag_step].astype(jnp.float32), 0.0
        )
    return summed


HALO = 32
TILE = 512
GROUP_LANES = 128
WINDOW = 144


def short_conv_rows(x, w, first, dist_all):
    rows = x.shape[0]
    dist = dist_all[first:rows, :]
    acc = x[first:rows, :] * w[0:1, :].astype(jnp.float32)
    for lag in range(1, w.shape[0]):
        term = x[first - lag : rows - lag, :] * w[lag : lag + 1, :].astype(jnp.float32)
        acc = acc + jnp.where(dist >= lag, term, 0.0)
    return acc


def rel_dist(rel_ref, base, count):
    index = base + lax.broadcasted_iota(jnp.int32, (count, 1), 0)
    return index - rel_ref[base : base + count, :]


def chain_kernel(rel_ref, sq, sk, sv, hq, hk, hv, mk, gk_h, fq, fk, fv, filt_ref, wk, wv,
                 z2_ref, xq, xk, xv, xb, zs, ys, group_ch, base):
    rows, tile = xq.shape
    dist_ref = rel_dist(rel_ref, base, rows)
    filters = filt_ref.shape[1]
    lane_ch = pl.program_id(0) * tile + lax.broadcasted_iota(jnp.int32, (filters, tile), 1)
    spread = (lane_ch // group_ch == lax.broadcasted_iota(jnp.int32, (filters, tile), 0))
    filt = jnp.dot(filt_ref[...], spread.astype(filt_ref.dtype), preferred_element_type=jnp.float32)
    for main, halo, x in ((sq, hq, xq), (sk, hk, xk), (sv, hv, xv), (mk, gk_h, xb)):
        reach = halo.shape[0]
        if reach < HALO:
            x[0 : HALO - reach, :] = jnp.zeros((HALO - reach, x.shape[1]), jnp.float32)
        x[HALO - reach : HALO, :] = halo[...].astype(jnp.float32)
        x[HALO:rows, :] = main[...].astype(jnp.float32)

    k1 = short_conv_rows(xk, fk, 16, dist_ref)
    v1 = short_conv_rows(xv, fv, 16, dist_ref)
    zs[16:rows, :] = (k1 * v1).astype(jnp.bfloat16).astype(jnp.float32)
    q1 = short_conv_rows(xq, fq, 24, dist_ref)
    c1 = short_conv_rows(zs, filt, 24, dist_ref)
    ys[24:rows, :] = (q1 * c1).astype(jnp.bfloat16).astype(jnp.float32)
    v2 = short_conv_rows(ys, wv, HALO, dist_ref)
    k2 = short_conv_rows(xb, wk, HALO, dist_ref)
    z2 = (k2 * v2).astype(jnp.bfloat16)
    chunk = z2_ref.shape[2]
    for i in range(z2_ref.shape[0]):
        z2_ref[i] = z2[:, i * chunk : (i + 1) * chunk]


def short_chain(rel, se_streams, se_halo, mr_gates, mr_halo, se_feat, se_filt, mr_feat, shards, half):
    tok_rows = se_streams.shape[0] // 2
    channels = mr_gates.shape[1] // 2
    steps = channels // TILE
    rows = tok_rows + HALO
    taps = se_feat.shape[0]
    chunk = channels // shards

    def col(part, row_block=half):
        return lambda j: (row_block, j + part * steps)

    def halo_spec(halo, part):
        if halo.shape[0] < HALO:
            return pl.BlockSpec((halo.shape[0], TILE), col(part, 0))
        return pl.BlockSpec((HALO, TILE), col(part, half * tok_rows // HALO - 1))

    main = [pl.BlockSpec((tok_rows, TILE), col(p)) for p in range(3)]
    halo = [halo_spec(se_halo, p) for p in range(3)]
    wts = [pl.BlockSpec((taps, TILE), col(p, 0)) for p in range(3)]
    return pl.pallas_call(
        functools.partial(
            chain_kernel, group_ch=channels // se_filt.shape[1], base=half * tok_rows + tok_rows - HALO
        ),
        grid=(steps,),
        in_specs=[pl.BlockSpec(rel.shape, lambda j: (0, 0))] + main + halo
        + [main[1], halo_spec(mr_halo, 1)] + wts
        + [pl.BlockSpec(se_filt.shape, lambda j: (0, 0)), wts[1], wts[2]],
        out_specs=pl.BlockSpec((TILE // chunk, tok_rows, chunk), lambda j: (j, 0, 0)),
        out_shape=jax.ShapeDtypeStruct((shards, tok_rows, chunk), jnp.bfloat16),
        scratch_shapes=[pltpu.VMEM((rows, TILE), jnp.float32) for _ in range(6)],
    )(rel, se_streams, se_streams, se_streams, se_halo, se_halo, se_halo, mr_gates,
      mr_halo, se_feat, se_feat, se_feat, se_filt, mr_feat, mr_feat)


def long_kernel(rel_ref, mg_ref, mh_ref, wq_ref, prev_ref, lo_ref, hi_ref, skip_ref,
                u_ref, out_ref, xa):
    rows = xa.shape[0]
    reach = mh_ref.shape[0]
    xa[HALO - reach : HALO, :] = mh_ref[...].astype(jnp.float32)
    xa[HALO:rows, :] = mg_ref[...].astype(jnp.float32)
    blk = lo_ref.shape[1]
    q2 = short_conv_rows(xa, wq_ref, HALO, rel_dist(rel_ref, blk - HALO, rows))
    blk = lo_ref.shape[1]
    tile = lo_ref.shape[2]
    width = u_ref.shape[1]
    per_group = tile // u_ref.shape[0]
    lo = lo_ref[0]
    hi = hi_ref[0]
    windows = (jnp.concatenate([prev_ref[0], lo], axis=0), jnp.concatenate([lo, hi], axis=0))
    masks = [
        lax.broadcasted_iota(jnp.int32, (1, width), 1) + b * blk >= rel_ref[(b + 1) * blk : (b + 2) * blk, :]
        for b in range(2)
    ]
    lane_grp = lax.broadcasted_iota(jnp.int32, (1, GROUP_LANES), 1) // per_group
    halves = tile // GROUP_LANES
    groups_half = GROUP_LANES // per_group
    acc = [[jnp.zeros((blk, GROUP_LANES), jnp.float32) for _ in range(halves)] for _ in range(2)]
    for g in range(u_ref.shape[0]):
        half = g // groups_half
        row = jnp.broadcast_to(u_ref[g : g + 1, :], (blk, width))
        taps = pltpu.roll(row, 0, 1, stride=1, stride_axis=0)
        for b in range(2):
            mat = jnp.where(masks[b], taps, 0.0).astype(jnp.bfloat16)
            part = windows[b][:, half * GROUP_LANES : (half + 1) * GROUP_LANES]
            res = jnp.dot(mat, part, preferred_element_type=jnp.float32)
            acc[b][half] = jnp.where(lane_grp == g % groups_half, res, acc[b][half])
    conv = jnp.concatenate([jnp.concatenate(acc[b], axis=1) for b in range(2)], axis=0)
    z = jnp.concatenate([lo, hi], axis=0).astype(jnp.float32)
    mixed = (conv + skip_ref[...].astype(jnp.float32) * z).astype(jnp.bfloat16)
    out_ref[...] = (q2 * mixed.astype(jnp.float32)).astype(jnp.bfloat16)


def long_conv_out(rel, mr_gates, mr_halo, mr_feat, prev_z, z_lo, z_hi, skip, taps_rows):
    steps, blk, lanes = z_lo.shape
    tok_rows = 2 * blk
    channels = steps * lanes
    per_group = channels // taps_rows.shape[0]
    piece = pl.BlockSpec((1, blk, lanes), lambda j: (j, 0, 0))
    return pl.pallas_call(
        long_kernel,
        grid=(steps,),
        in_specs=[
            pl.BlockSpec(rel.shape, lambda j: (0, 0)),
            pl.BlockSpec((tok_rows, lanes), lambda j: (0, j)),
            pl.BlockSpec((mr_halo.shape[0], lanes), lambda j: (0, j)),
            pl.BlockSpec((mr_feat.shape[0], lanes), lambda j: (0, j)),
            piece,
            piece,
            piece,
            pl.BlockSpec((1, lanes), lambda j: (0, j)),
            pl.BlockSpec((lanes // per_group, taps_rows.shape[1]), lambda j: (j, 0)),
        ],
        out_specs=pl.BlockSpec((tok_rows, lanes), lambda j: (0, j)),
        out_shape=jax.ShapeDtypeStruct((tok_rows, channels), jnp.bfloat16),
        scratch_shapes=[pltpu.VMEM((tok_rows + HALO, lanes), jnp.float32)],
    )(rel, mr_gates, mr_halo, mr_feat, prev_z, z_lo, z_hi, skip, taps_rows)


def tail_kernel(begin_ref, first_ref, lo_ref, hi_ref, out_ref, z_all):
    shards, blk, lanes = lo_ref.shape
    tail_len = out_ref.shape[0]
    total = z_all.shape[0]
    for src in range(shards):
        z_all[2 * src * blk : (2 * src + 1) * blk, :] = lo_ref[src]
        z_all[(2 * src + 1) * blk : (2 * src + 2) * blk, :] = hi_ref[src]
    for t in range(out_ref.shape[1]):
        begin = begin_ref[t]
        start = jnp.clip((begin // 16) * 16, 0, total - WINDOW)
        shift = begin - start
        window = z_all[pl.ds(pl.multiple_of(start, 16), WINDOW), :].astype(jnp.float32)
        moved = pltpu.roll(window, (WINDOW - shift) % WINDOW, 0)[:tail_len]
        pos = begin + lax.broadcasted_iota(jnp.int32, (tail_len, 1), 0)
        out_ref[:, t, :] = jnp.where(pos >= first_ref[t], moved, 0.0).astype(out_ref.dtype)


def cut_tails_all(z_lo, z_hi, begins, firsts, tail_len):
    shards, blk, lanes = z_lo.shape
    count = begins.shape[0]
    smem = pl.BlockSpec(memory_space=pltpu.SMEM)
    vmem = pl.BlockSpec(memory_space=pltpu.VMEM)
    out = pl.pallas_call(
        tail_kernel,
        in_specs=[smem, smem, vmem, vmem],
        out_specs=vmem,
        out_shape=jax.ShapeDtypeStruct((tail_len, count, lanes), z_lo.dtype),
        scratch_shapes=[pltpu.VMEM((2 * shards * blk, lanes), z_lo.dtype)],
    )(begins, firsts, z_lo, z_hi)
    return jnp.transpose(out, (1, 0, 2))


def seg_start(positions, req_ends):
    before = req_ends[None, :] < positions[:, None]
    return jnp.max(jnp.where(before, req_ends[None, :] + 1, 0), axis=1)


def pick_entries(lookup_table, indices):
    hits = indices[:, None] == jnp.arange(lookup_table.shape[0], dtype=jnp.int32)[None, :]
    return jnp.sum(jnp.where(hits, lookup_table[None, :], 0), axis=1)


def local(
    se_streams, mr_gates, se_feat, se_filter, mr_feat, mr_filter, mr_skip, req_ends, decode_row
):
    tok_rows = se_streams.shape[0]
    channels = mr_gates.shape[1] // 2
    shards = lax.axis_size("seq")
    device = lax.axis_index("seq")
    offset = device * tok_rows
    reach_rows = se_feat.shape[0] - 1
    tap_count = mr_filter.shape[0]
    tail_len = tap_count - 1
    group_ch = channels // se_filter.shape[1]
    total_req = req_ends.shape[0]
    slot_total = ENDS_MAX + 1
    rim_depth = 2 * reach_rows
    prev_se, prev_mr = passed_along(
        (se_streams[tok_rows - 3 * reach_rows :], mr_gates[tok_rows - reach_rows :]), "seq", 1
    )
    blk = tok_rows // 2
    se_filt = se_filter

    window_pos = offset - blk + jnp.arange(tok_rows + blk, dtype=jnp.int32)
    rel = (seg_start(window_pos, req_ends) - (offset - blk))[:, None]
    z_hi = short_chain(
        rel, se_streams, se_streams, mr_gates, mr_gates, se_feat, se_filt, mr_feat, shards, 1
    )
    prev_z = passed_along(z_hi, "seq", 1)
    z_hi, prev_se, prev_mr = lax.optimization_barrier((z_hi, prev_se, prev_mr))
    recv_hi = lax.all_to_all(z_hi, "seq", split_axis=0, concat_axis=0, tiled=True)
    z_lo = short_chain(
        rel, se_streams, prev_se, mr_gates, prev_mr, se_feat, se_filt, mr_feat, shards, 0
    )
    z_lo, recv_hi, prev_z = lax.optimization_barrier((z_lo, recv_hi, prev_z))
    recv_lo = lax.all_to_all(z_lo, "seq", split_axis=0, concat_axis=0, tiled=True)
    filt_t = mr_filter[::-1].T.astype(jnp.float32)
    filters = filt_t.shape[0]
    taps_rows = jnp.concatenate(
        [jnp.zeros((filters, 1), jnp.float32), filt_t, jnp.zeros((filters, tap_count - 1), jnp.float32)],
        axis=1,
    )

    hyena_out = long_conv_out(
        rel, mr_gates, prev_mr, mr_feat, prev_z, z_lo, z_hi, mr_skip[None, :], taps_rows
    )
    rows_ids = jnp.arange(total_req, dtype=jnp.int32)
    owner = jnp.sum(
        jnp.where(decode_row[None, :] == rows_ids[:, None], rows_ids[None, :], 0), axis=1
    )
    last_pos = pick_entries(req_ends, owner)
    first_pos = jnp.where(owner > 0, pick_entries(req_ends, jnp.maximum(owner - 1, 0)) + 1, 0)
    tail_cache = cut_tails_all(recv_lo, recv_hi, last_pos - tail_len + 1, first_pos, tail_len)
    return (hyena_out, tail_cache)


def solution(mesh):
    placed = (
        P(("groups", "seq"), None),
        P(("groups", "seq"), None),
        P(),
        P(),
        P(),
        P(),
        P(),
        P("groups"),
        P("groups"),
    )
    return jax.shard_map(
        local,
        mesh=mesh,
        in_specs=placed,
        out_specs=(P(("groups", "seq"), None), P("groups", None, "seq")),
        check_vma=False,
    )
```

```python
import functools

import jax
import jax.numpy as jnp
from jax import lax
from jax.sharding import PartitionSpec as P
from jax.experimental import pallas as pl
from jax.experimental.pallas import tpu as pltpu

ENDS_MAX = 4


def passed_along(x, axis, by):
    length = lax.axis_size(axis)
    pairs = [(i, i + by) for i in range(length) if 0 <= i + by < length]
    return lax.ppermute(x, axis, pairs)


def request_of(positions, req_ends):
    return jnp.sum((req_ends[None, :] < positions[:, None]).astype(jnp.int32), axis=1)


def short_conv(values, weights, segment):
    length = weights.shape[0]
    out_count = values.shape[0] - length + 1
    latest = length - 1
    current = segment[latest:]
    summed = values[latest:].astype(jnp.float32) * weights[0].astype(jnp.float32)
    for lag_step in range(1, length):
        earlier = values[latest - lag_step : latest - lag_step + out_count].astype(jnp.float32)
        same_req = segment[latest - lag_step : latest - lag_step + out_count] == current
        summed = summed + jnp.where(
            same_req[:, None], earlier * weights[lag_step].astype(jnp.float32), 0.0
        )
    return summed


HALO = 32
TILE = 512
GROUP_LANES = 128
WINDOW = 144


def short_conv_rows(x, w, first, dist_all):
    rows = x.shape[0]
    dist = dist_all[first:rows, :]
    acc = x[first:rows, :] * w[0:1, :].astype(jnp.float32)
    for lag in range(1, w.shape[0]):
        term = x[first - lag : rows - lag, :] * w[lag : lag + 1, :].astype(jnp.float32)
        acc = acc + jnp.where(dist >= lag, term, 0.0)
    return acc


def rel_dist(rel_ref, base, count):
    index = base + lax.broadcasted_iota(jnp.int32, (count, 1), 0)
    return index - rel_ref[base : base + count, :]


def chain_kernel(rel_ref, sq, sk, sv, hq, hk, hv, mk, gk_h, fq, fk, fv, filt_ref, wk, wv,
                 z2_ref, xq, xk, xv, xb, zs, ys, group_ch, base):
    rows, tile = xq.shape
    dist_ref = rel_dist(rel_ref, base, rows)
    filters = filt_ref.shape[1]
    lane_ch = pl.program_id(0) * tile + lax.broadcasted_iota(jnp.int32, (filters, tile), 1)
    spread = (lane_ch // group_ch == lax.broadcasted_iota(jnp.int32, (filters, tile), 0))
    filt = jnp.dot(filt_ref[...], spread.astype(filt_ref.dtype), preferred_element_type=jnp.float32)
    for main, halo, x in ((sq, hq, xq), (sk, hk, xk), (sv, hv, xv), (mk, gk_h, xb)):
        reach = halo.shape[0]
        if reach < HALO:
            x[0 : HALO - reach, :] = jnp.zeros((HALO - reach, x.shape[1]), jnp.float32)
        x[HALO - reach : HALO, :] = halo[...].astype(jnp.float32)
        x[HALO:rows, :] = main[...].astype(jnp.float32)

    k1 = short_conv_rows(xk, fk, 16, dist_ref)
    v1 = short_conv_rows(xv, fv, 16, dist_ref)
    zs[16:rows, :] = (k1 * v1).astype(jnp.bfloat16).astype(jnp.float32)
    q1 = short_conv_rows(xq, fq, 24, dist_ref)
    c1 = short_conv_rows(zs, filt, 24, dist_ref)
    ys[24:rows, :] = (q1 * c1).astype(jnp.bfloat16).astype(jnp.float32)
    v2 = short_conv_rows(ys, wv, HALO, dist_ref)
    k2 = short_conv_rows(xb, wk, HALO, dist_ref)
    z2 = (k2 * v2).astype(jnp.bfloat16)
    chunk = z2_ref.shape[2]
    for i in range(z2_ref.shape[0]):
        z2_ref[i] = z2[:, i * chunk : (i + 1) * chunk]


def short_chain(rel, se_streams, se_halo, mr_gates, mr_halo, se_feat, se_filt, mr_feat, shards, half):
    tok_rows = se_streams.shape[0] // 2
    channels = mr_gates.shape[1] // 2
    steps = channels // TILE
    rows = tok_rows + HALO
    taps = se_feat.shape[0]
    chunk = channels // shards

    def col(part, row_block=half):
        return lambda j: (row_block, j + part * steps)

    def halo_spec(halo, part, skip=0):
        if halo.shape[0] < HALO:
            return pl.BlockSpec((halo.shape[0], TILE), col(part + skip, 0))
        return pl.BlockSpec((HALO, TILE), col(part, half * tok_rows // HALO - 1))

    main = [pl.BlockSpec((tok_rows, TILE), col(p)) for p in range(3)]
    halo = [halo_spec(se_halo, p) for p in range(3)]
    wts = [pl.BlockSpec((taps, TILE), col(p, 0)) for p in range(3)]
    return pl.pallas_call(
        functools.partial(
            chain_kernel, group_ch=channels // se_filt.shape[1], base=half * tok_rows + tok_rows - HALO
        ),
        grid=(steps,),
        in_specs=[pl.BlockSpec(rel.shape, lambda j: (0, 0))] + main + halo
        + [main[1], halo_spec(mr_halo, 1, (mr_halo.shape[1] - mr_gates.shape[1]) // channels)] + wts
        + [pl.BlockSpec(se_filt.shape, lambda j: (0, 0)), wts[1], wts[2]],
        out_specs=pl.BlockSpec((TILE // chunk, tok_rows, chunk), lambda j: (j, 0, 0)),
        out_shape=jax.ShapeDtypeStruct((shards, tok_rows, chunk), jnp.bfloat16),
        scratch_shapes=[pltpu.VMEM((rows, TILE), jnp.float32) for _ in range(6)],
    )(rel, se_streams, se_streams, se_streams, se_halo, se_halo, se_halo, mr_gates,
      mr_halo, se_feat, se_feat, se_feat, se_filt, mr_feat, mr_feat)


def long_kernel(rel_ref, mg_ref, mh_ref, wq_ref, prev_ref, lo_ref, hi_ref, skip_ref,
                u_ref, out_ref, xa):
    rows = xa.shape[0]
    reach = mh_ref.shape[0]
    xa[HALO - reach : HALO, :] = mh_ref[...].astype(jnp.float32)
    xa[HALO:rows, :] = mg_ref[...].astype(jnp.float32)
    blk = lo_ref.shape[1]
    q2 = short_conv_rows(xa, wq_ref, HALO, rel_dist(rel_ref, blk - HALO, rows))
    blk = lo_ref.shape[1]
    tile = lo_ref.shape[2]
    width = u_ref.shape[1]
    per_group = tile // u_ref.shape[0]
    lo = lo_ref[0]
    hi = hi_ref[0]
    windows = (jnp.concatenate([prev_ref[0], lo], axis=0), jnp.concatenate([lo, hi], axis=0))
    masks = [
        lax.broadcasted_iota(jnp.int32, (1, width), 1) + b * blk >= rel_ref[(b + 1) * blk : (b + 2) * blk, :]
        for b in range(2)
    ]
    lane_grp = lax.broadcasted_iota(jnp.int32, (1, GROUP_LANES), 1) // per_group
    halves = tile // GROUP_LANES
    groups_half = GROUP_LANES // per_group
    acc = [[jnp.zeros((blk, GROUP_LANES), jnp.float32) for _ in range(halves)] for _ in range(2)]
    for g in range(u_ref.shape[0]):
        half = g // groups_half
        row = jnp.broadcast_to(u_ref[g : g + 1, :], (blk, width))
        taps = pltpu.roll(row, 0, 1, stride=1, stride_axis=0)
        for b in range(2):
            mat = jnp.where(masks[b], taps, 0.0).astype(jnp.bfloat16)
            part = windows[b][:, half * GROUP_LANES : (half + 1) * GROUP_LANES]
            res = jnp.dot(mat, part, preferred_element_type=jnp.float32)
            acc[b][half] = jnp.where(lane_grp == g % groups_half, res, acc[b][half])
    conv = jnp.concatenate([jnp.concatenate(acc[b], axis=1) for b in range(2)], axis=0)
    z = jnp.concatenate([lo, hi], axis=0).astype(jnp.float32)
    mixed = (conv + skip_ref[...].astype(jnp.float32) * z).astype(jnp.bfloat16)
    out_ref[...] = (q2 * mixed.astype(jnp.float32)).astype(jnp.bfloat16)


def long_conv_out(rel, mr_gates, mr_halo, mr_feat, prev_z, z_lo, z_hi, skip, taps_rows):
    steps, blk, lanes = z_lo.shape
    tok_rows = 2 * blk
    channels = steps * lanes
    per_group = channels // taps_rows.shape[0]
    piece = pl.BlockSpec((1, blk, lanes), lambda j: (j, 0, 0))
    return pl.pallas_call(
        long_kernel,
        grid=(steps,),
        in_specs=[
            pl.BlockSpec(rel.shape, lambda j: (0, 0)),
            pl.BlockSpec((tok_rows, lanes), lambda j: (0, j)),
            pl.BlockSpec(
                (mr_halo.shape[0], lanes), lambda j: (0, j + (mr_halo.shape[1] - mr_gates.shape[1]) // lanes)
            ),
            pl.BlockSpec((mr_feat.shape[0], lanes), lambda j: (0, j)),
            piece,
            piece,
            piece,
            pl.BlockSpec((1, lanes), lambda j: (0, j)),
            pl.BlockSpec((lanes // per_group, taps_rows.shape[1]), lambda j: (j, 0)),
        ],
        out_specs=pl.BlockSpec((tok_rows, lanes), lambda j: (0, j)),
        out_shape=jax.ShapeDtypeStruct((tok_rows, channels), jnp.bfloat16),
        scratch_shapes=[pltpu.VMEM((tok_rows + HALO, lanes), jnp.float32)],
    )(rel, mr_gates, mr_halo, mr_feat, prev_z, z_lo, z_hi, skip, taps_rows)


def tail_kernel(begin_ref, first_ref, lo_ref, hi_ref, out_ref, z_all):
    shards, blk, lanes = lo_ref.shape
    tail_len = out_ref.shape[0]
    total = z_all.shape[0]
    for src in range(shards):
        z_all[2 * src * blk : (2 * src + 1) * blk, :] = lo_ref[src]
        z_all[(2 * src + 1) * blk : (2 * src + 2) * blk, :] = hi_ref[src]
    for t in range(out_ref.shape[1]):
        begin = begin_ref[t]
        start = jnp.clip((begin // 16) * 16, 0, total - WINDOW)
        shift = begin - start
        window = z_all[pl.ds(pl.multiple_of(start, 16), WINDOW), :].astype(jnp.float32)
        moved = pltpu.roll(window, (WINDOW - shift) % WINDOW, 0)[:tail_len]
        pos = begin + lax.broadcasted_iota(jnp.int32, (tail_len, 1), 0)
        out_ref[:, t, :] = jnp.where(pos >= first_ref[t], moved, 0.0).astype(out_ref.dtype)


def cut_tails_all(z_lo, z_hi, begins, firsts, tail_len):
    shards, blk, lanes = z_lo.shape
    count = begins.shape[0]
    smem = pl.BlockSpec(memory_space=pltpu.SMEM)
    vmem = pl.BlockSpec(memory_space=pltpu.VMEM)
    out = pl.pallas_call(
        tail_kernel,
        in_specs=[smem, smem, vmem, vmem],
        out_specs=vmem,
        out_shape=jax.ShapeDtypeStruct((tail_len, count, lanes), z_lo.dtype),
        scratch_shapes=[pltpu.VMEM((2 * shards * blk, lanes), z_lo.dtype)],
    )(begins, firsts, z_lo, z_hi)
    return jnp.transpose(out, (1, 0, 2))


def seg_start(positions, req_ends):
    before = req_ends[None, :] < positions[:, None]
    return jnp.max(jnp.where(before, req_ends[None, :] + 1, 0), axis=1)


def pick_entries(lookup_table, indices):
    hits = indices[:, None] == jnp.arange(lookup_table.shape[0], dtype=jnp.int32)[None, :]
    return jnp.sum(jnp.where(hits, lookup_table[None, :], 0), axis=1)


def local(
    se_streams, mr_gates, se_feat, se_filter, mr_feat, mr_filter, mr_skip, req_ends, decode_row
):
    tok_rows = se_streams.shape[0]
    channels = mr_gates.shape[1] // 2
    shards = lax.axis_size("seq")
    device = lax.axis_index("seq")
    offset = device * tok_rows
    reach_rows = se_feat.shape[0] - 1
    tap_count = mr_filter.shape[0]
    tail_len = tap_count - 1
    group_ch = channels // se_filter.shape[1]
    total_req = req_ends.shape[0]
    slot_total = ENDS_MAX + 1
    rim_depth = 2 * reach_rows
    se_tail = se_streams[tok_rows - 3 * reach_rows :]
    mr_tail = jnp.pad(mr_gates[tok_rows - reach_rows :], ((2 * reach_rows, 0), (0, 0)))
    prev_se = passed_along(jnp.concatenate([se_tail, mr_tail], axis=1), "seq", 1)
    blk = tok_rows // 2
    se_filt = se_filter

    window_pos = offset - blk + jnp.arange(tok_rows + blk, dtype=jnp.int32)
    rel = (seg_start(window_pos, req_ends) - (offset - blk))[:, None]
    z_hi = short_chain(
        rel, se_streams, se_streams, mr_gates, mr_gates, se_feat, se_filt, mr_feat, shards, 1
    )
    prev_z = passed_along(z_hi, "seq", 1)
    z_hi, prev_se = lax.optimization_barrier((z_hi, prev_se))
    recv_hi = lax.all_to_all(z_hi, "seq", split_axis=0, concat_axis=0, tiled=True)
    z_lo = short_chain(
        rel, se_streams, prev_se, mr_gates, prev_se, se_feat, se_filt, mr_feat, shards, 0
    )
    z_lo, recv_hi, prev_z = lax.optimization_barrier((z_lo, recv_hi, prev_z))
    recv_lo = lax.all_to_all(z_lo, "seq", split_axis=0, concat_axis=0, tiled=True)
    filt_t = mr_filter[::-1].T.astype(jnp.float32)
    filters = filt_t.shape[0]
    taps_rows = jnp.concatenate(
        [jnp.zeros((filters, 1), jnp.float32), filt_t, jnp.zeros((filters, tap_count - 1), jnp.float32)],
        axis=1,
    )

    hyena_out = long_conv_out(
        rel, mr_gates, prev_se, mr_feat, prev_z, z_lo, z_hi, mr_skip[None, :], taps_rows
    )
    rows_ids = jnp.arange(total_req, dtype=jnp.int32)
    owner = jnp.sum(
        jnp.where(decode_row[None, :] == rows_ids[:, None], rows_ids[None, :], 0), axis=1
    )
    last_pos = pick_entries(req_ends, owner)
    first_pos = jnp.where(owner > 0, pick_entries(req_ends, jnp.maximum(owner - 1, 0)) + 1, 0)
    tail_cache = cut_tails_all(recv_lo, recv_hi, last_pos - tail_len + 1, first_pos, tail_len)
    return (hyena_out, tail_cache)


def solution(mesh):
    placed = (
        P(("groups", "seq"), None),
        P(("groups", "seq"), None),
        P(),
        P(),
        P(),
        P(),
        P(),
        P("groups"),
        P("groups"),
    )
    return jax.shard_map(
        local,
        mesh=mesh,
        in_specs=placed,
        out_specs=(P(("groups", "seq"), None), P("groups", None, "seq")),
        check_vma=False,
    )
```

```python
import functools

import jax
import jax.numpy as jnp
from jax import lax
from jax.sharding import PartitionSpec as P
from jax.experimental import pallas as pl
from jax.experimental.pallas import tpu as pltpu

ENDS_MAX = 4


def passed_along(x, axis, by):
    length = lax.axis_size(axis)
    pairs = [(i, i + by) for i in range(length) if 0 <= i + by < length]
    return lax.ppermute(x, axis, pairs)


def request_of(positions, req_ends):
    return jnp.sum((req_ends[None, :] < positions[:, None]).astype(jnp.int32), axis=1)


def short_conv(values, weights, segment):
    length = weights.shape[0]
    out_count = values.shape[0] - length + 1
    latest = length - 1
    current = segment[latest:]
    summed = values[latest:].astype(jnp.float32) * weights[0].astype(jnp.float32)
    for lag_step in range(1, length):
        earlier = values[latest - lag_step : latest - lag_step + out_count].astype(jnp.float32)
        same_req = segment[latest - lag_step : latest - lag_step + out_count] == current
        summed = summed + jnp.where(
            same_req[:, None], earlier * weights[lag_step].astype(jnp.float32), 0.0
        )
    return summed


HALO = 32
TILE = 256
GROUP_LANES = 128
WINDOW = 144


def short_conv_rows(x, w, first, dist_all):
    rows = x.shape[0]
    dist = dist_all[first:rows, :]
    acc = x[first:rows, :] * w[0:1, :].astype(jnp.float32)
    for lag in range(1, w.shape[0]):
        term = x[first - lag : rows - lag, :] * w[lag : lag + 1, :].astype(jnp.float32)
        acc = acc + jnp.where(dist >= lag, term, 0.0)
    return acc


def rel_dist(rel_ref, base, count):
    index = base + lax.broadcasted_iota(jnp.int32, (count, 1), 0)
    return index - rel_ref[base : base + count, :]


def chain_kernel(rel_ref, sq, sk, sv, hq, hk, hv, mk, gk_h, fq, fk, fv, filt_ref, wk, wv,
                 z2_ref, xq, xk, xv, xb, zs, ys, group_ch, base):
    rows, tile = xq.shape
    dist_ref = rel_dist(rel_ref, base, rows)
    filters = filt_ref.shape[1]
    lane_ch = pl.program_id(0) * tile + lax.broadcasted_iota(jnp.int32, (filters, tile), 1)
    spread = (lane_ch // group_ch == lax.broadcasted_iota(jnp.int32, (filters, tile), 0))
    filt = jnp.dot(filt_ref[...], spread.astype(filt_ref.dtype), preferred_element_type=jnp.float32)
    for main, halo, x in ((sq, hq, xq), (sk, hk, xk), (sv, hv, xv), (mk, gk_h, xb)):
        reach = halo.shape[0]
        if reach < HALO:
            x[0 : HALO - reach, :] = jnp.zeros((HALO - reach, x.shape[1]), jnp.float32)
        x[HALO - reach : HALO, :] = halo[...].astype(jnp.float32)
        x[HALO:rows, :] = main[...].astype(jnp.float32)

    k1 = short_conv_rows(xk, fk, 16, dist_ref)
    v1 = short_conv_rows(xv, fv, 16, dist_ref)
    zs[16:rows, :] = (k1 * v1).astype(jnp.bfloat16).astype(jnp.float32)
    q1 = short_conv_rows(xq, fq, 24, dist_ref)
    c1 = short_conv_rows(zs, filt, 24, dist_ref)
    ys[24:rows, :] = (q1 * c1).astype(jnp.bfloat16).astype(jnp.float32)
    v2 = short_conv_rows(ys, wv, HALO, dist_ref)
    k2 = short_conv_rows(xb, wk, HALO, dist_ref)
    z2 = (k2 * v2).astype(jnp.bfloat16)
    chunk = z2_ref.shape[2]
    for i in range(z2_ref.shape[0]):
        z2_ref[i] = z2[:, i * chunk : (i + 1) * chunk]


def short_chain(rel, se_streams, se_halo, mr_gates, mr_halo, se_feat, se_filt, mr_feat, shards, half):
    tok_rows = se_streams.shape[0] // 2
    channels = mr_gates.shape[1] // 2
    steps = channels // TILE
    rows = tok_rows + HALO
    taps = se_feat.shape[0]
    chunk = channels // shards

    def col(part, row_block=half):
        return lambda j: (row_block, j + part * steps)

    def halo_spec(halo, part, skip=0):
        if halo.shape[0] < HALO:
            return pl.BlockSpec((halo.shape[0], TILE), col(part + skip, 0))
        return pl.BlockSpec((HALO, TILE), col(part, half * tok_rows // HALO - 1))

    main = [pl.BlockSpec((tok_rows, TILE), col(p)) for p in range(3)]
    halo = [halo_spec(se_halo, p) for p in range(3)]
    wts = [pl.BlockSpec((taps, TILE), col(p, 0)) for p in range(3)]
    return pl.pallas_call(
        functools.partial(
            chain_kernel, group_ch=channels // se_filt.shape[1], base=half * tok_rows + tok_rows - HALO
        ),
        grid=(steps,),
        in_specs=[pl.BlockSpec(rel.shape, lambda j: (0, 0))] + main + halo
        + [main[1], halo_spec(mr_halo, 1, (mr_halo.shape[1] - mr_gates.shape[1]) // channels)] + wts
        + [pl.BlockSpec(se_filt.shape, lambda j: (0, 0)), wts[1], wts[2]],
        out_specs=pl.BlockSpec((TILE // chunk, tok_rows, chunk), lambda j: (j, 0, 0)),
        out_shape=jax.ShapeDtypeStruct((shards, tok_rows, chunk), jnp.bfloat16),
        scratch_shapes=[pltpu.VMEM((rows, TILE), jnp.float32) for _ in range(6)],
    )(rel, se_streams, se_streams, se_streams, se_halo, se_halo, se_halo, mr_gates,
      mr_halo, se_feat, se_feat, se_feat, se_filt, mr_feat, mr_feat)


def long_kernel(rel_ref, mg_ref, mh_ref, wq_ref, prev_ref, lo_ref, hi_ref, skip_ref,
                u_ref, out_ref, xa):
    rows = xa.shape[0]
    reach = mh_ref.shape[0]
    xa[HALO - reach : HALO, :] = mh_ref[...].astype(jnp.float32)
    xa[HALO:rows, :] = mg_ref[...].astype(jnp.float32)
    blk = lo_ref.shape[1]
    q2 = short_conv_rows(xa, wq_ref, HALO, rel_dist(rel_ref, blk - HALO, rows))
    blk = lo_ref.shape[1]
    tile = lo_ref.shape[2]
    width = u_ref.shape[1]
    per_group = tile // u_ref.shape[0]
    lo = lo_ref[0]
    hi = hi_ref[0]
    windows = (jnp.concatenate([prev_ref[0], lo], axis=0), jnp.concatenate([lo, hi], axis=0))
    masks = [
        lax.broadcasted_iota(jnp.int32, (1, width), 1) + b * blk >= rel_ref[(b + 1) * blk : (b + 2) * blk, :]
        for b in range(2)
    ]
    lane_grp = lax.broadcasted_iota(jnp.int32, (1, GROUP_LANES), 1) // per_group
    halves = tile // GROUP_LANES
    groups_half = GROUP_LANES // per_group
    acc = [[jnp.zeros((blk, GROUP_LANES), jnp.float32) for _ in range(halves)] for _ in range(2)]
    for g in range(u_ref.shape[0]):
        half = g // groups_half
        row = jnp.broadcast_to(u_ref[g : g + 1, :], (blk, width))
        taps = pltpu.roll(row, 0, 1, stride=1, stride_axis=0)
        for b in range(2):
            mat = jnp.where(masks[b], taps, 0.0).astype(jnp.bfloat16)
            part = windows[b][:, half * GROUP_LANES : (half + 1) * GROUP_LANES]
            res = jnp.dot(mat, part, preferred_element_type=jnp.float32)
            acc[b][half] = jnp.where(lane_grp == g % groups_half, res, acc[b][half])
    conv = jnp.concatenate([jnp.concatenate(acc[b], axis=1) for b in range(2)], axis=0)
    z = jnp.concatenate([lo, hi], axis=0).astype(jnp.float32)
    mixed = (conv + skip_ref[...].astype(jnp.float32) * z).astype(jnp.bfloat16)
    out_ref[...] = (q2 * mixed.astype(jnp.float32)).astype(jnp.bfloat16)


def long_conv_out(rel, mr_gates, mr_halo, mr_feat, prev_z, z_lo, z_hi, skip, taps_rows):
    steps, blk, lanes = z_lo.shape
    tok_rows = 2 * blk
    channels = steps * lanes
    per_group = channels // taps_rows.shape[0]
    piece = pl.BlockSpec((1, blk, lanes), lambda j: (j, 0, 0))
    return pl.pallas_call(
        long_kernel,
        grid=(steps,),
        in_specs=[
            pl.BlockSpec(rel.shape, lambda j: (0, 0)),
            pl.BlockSpec((tok_rows, lanes), lambda j: (0, j)),
            pl.BlockSpec(
                (mr_halo.shape[0], lanes), lambda j: (0, j + (mr_halo.shape[1] - mr_gates.shape[1]) // lanes)
            ),
            pl.BlockSpec((mr_feat.shape[0], lanes), lambda j: (0, j)),
            piece,
            piece,
            piece,
            pl.BlockSpec((1, lanes), lambda j: (0, j)),
            pl.BlockSpec((lanes // per_group, taps_rows.shape[1]), lambda j: (j, 0)),
        ],
        out_specs=pl.BlockSpec((tok_rows, lanes), lambda j: (0, j)),
        out_shape=jax.ShapeDtypeStruct((tok_rows, channels), jnp.bfloat16),
        scratch_shapes=[pltpu.VMEM((tok_rows + HALO, lanes), jnp.float32)],
    )(rel, mr_gates, mr_halo, mr_feat, prev_z, z_lo, z_hi, skip, taps_rows)


def tail_kernel(begin_ref, first_ref, lo_ref, hi_ref, out_ref, z_all):
    shards, blk, lanes = lo_ref.shape
    tail_len = out_ref.shape[0]
    total = z_all.shape[0]
    for src in range(shards):
        z_all[2 * src * blk : (2 * src + 1) * blk, :] = lo_ref[src]
        z_all[(2 * src + 1) * blk : (2 * src + 2) * blk, :] = hi_ref[src]
    for t in range(out_ref.shape[1]):
        begin = begin_ref[t]
        start = jnp.clip((begin // 16) * 16, 0, total - WINDOW)
        shift = begin - start
        window = z_all[pl.ds(pl.multiple_of(start, 16), WINDOW), :].astype(jnp.float32)
        moved = pltpu.roll(window, (WINDOW - shift) % WINDOW, 0)[:tail_len]
        pos = begin + lax.broadcasted_iota(jnp.int32, (tail_len, 1), 0)
        out_ref[:, t, :] = jnp.where(pos >= first_ref[t], moved, 0.0).astype(out_ref.dtype)


def cut_tails_all(z_lo, z_hi, begins, firsts, tail_len):
    shards, blk, lanes = z_lo.shape
    count = begins.shape[0]
    smem = pl.BlockSpec(memory_space=pltpu.SMEM)
    vmem = pl.BlockSpec(memory_space=pltpu.VMEM)
    out = pl.pallas_call(
        tail_kernel,
        in_specs=[smem, smem, vmem, vmem],
        out_specs=vmem,
        out_shape=jax.ShapeDtypeStruct((tail_len, count, lanes), z_lo.dtype),
        scratch_shapes=[pltpu.VMEM((2 * shards * blk, lanes), z_lo.dtype)],
    )(begins, firsts, z_lo, z_hi)
    return jnp.transpose(out, (1, 0, 2))


def seg_start(positions, req_ends):
    before = req_ends[None, :] < positions[:, None]
    return jnp.max(jnp.where(before, req_ends[None, :] + 1, 0), axis=1)


def pick_entries(lookup_table, indices):
    hits = indices[:, None] == jnp.arange(lookup_table.shape[0], dtype=jnp.int32)[None, :]
    return jnp.sum(jnp.where(hits, lookup_table[None, :], 0), axis=1)


def local(
    se_streams, mr_gates, se_feat, se_filter, mr_feat, mr_filter, mr_skip, req_ends, decode_row
):
    tok_rows = se_streams.shape[0]
    channels = mr_gates.shape[1] // 2
    shards = lax.axis_size("seq")
    device = lax.axis_index("seq")
    offset = device * tok_rows
    reach_rows = se_feat.shape[0] - 1
    tap_count = mr_filter.shape[0]
    tail_len = tap_count - 1
    group_ch = channels // se_filter.shape[1]
    total_req = req_ends.shape[0]
    slot_total = ENDS_MAX + 1
    rim_depth = 2 * reach_rows
    se_tail = se_streams[tok_rows - 3 * reach_rows :]
    mr_tail = jnp.pad(mr_gates[tok_rows - reach_rows :], ((2 * reach_rows, 0), (0, 0)))
    prev_se = passed_along(jnp.concatenate([se_tail, mr_tail], axis=1), "seq", 1)
    blk = tok_rows // 2
    se_filt = se_filter

    window_pos = offset - blk + jnp.arange(tok_rows + blk, dtype=jnp.int32)
    rel = (seg_start(window_pos, req_ends) - (offset - blk))[:, None]
    z_hi = short_chain(
        rel, se_streams, se_streams, mr_gates, mr_gates, se_feat, se_filt, mr_feat, shards, 1
    )
    prev_z = passed_along(z_hi, "seq", 1)
    z_hi, prev_se = lax.optimization_barrier((z_hi, prev_se))
    recv_hi = lax.all_to_all(z_hi, "seq", split_axis=0, concat_axis=0, tiled=True)
    z_lo = short_chain(
        rel, se_streams, prev_se, mr_gates, prev_se, se_feat, se_filt, mr_feat, shards, 0
    )
    z_lo, recv_hi, prev_z = lax.optimization_barrier((z_lo, recv_hi, prev_z))
    recv_lo = lax.all_to_all(z_lo, "seq", split_axis=0, concat_axis=0, tiled=True)
    filt_t = mr_filter[::-1].T.astype(jnp.float32)
    filters = filt_t.shape[0]
    taps_rows = jnp.concatenate(
        [jnp.zeros((filters, 1), jnp.float32), filt_t, jnp.zeros((filters, tap_count - 1), jnp.float32)],
        axis=1,
    )

    hyena_out = long_conv_out(
        rel, mr_gates, prev_se, mr_feat, prev_z, z_lo, z_hi, mr_skip[None, :], taps_rows
    )
    rows_ids = jnp.arange(total_req, dtype=jnp.int32)
    owner = jnp.sum(
        jnp.where(decode_row[None, :] == rows_ids[:, None], rows_ids[None, :], 0), axis=1
    )
    last_pos = pick_entries(req_ends, owner)
    first_pos = jnp.where(owner > 0, pick_entries(req_ends, jnp.maximum(owner - 1, 0)) + 1, 0)
    tail_cache = cut_tails_all(recv_lo, recv_hi, last_pos - tail_len + 1, first_pos, tail_len)
    return (hyena_out, tail_cache)


def solution(mesh):
    placed = (
        P(("groups", "seq"), None),
        P(("groups", "seq"), None),
        P(),
        P(),
        P(),
        P(),
        P(),
        P("groups"),
        P("groups"),
    )
    return jax.shard_map(
        local,
        mesh=mesh,
        in_specs=placed,
        out_specs=(P(("groups", "seq"), None), P("groups", None, "seq")),
        check_vma=False,
    )
```

```python
import functools

import jax
import jax.numpy as jnp
from jax import lax
from jax.sharding import PartitionSpec as P
from jax.experimental import pallas as pl
from jax.experimental.pallas import tpu as pltpu

ENDS_MAX = 4


def passed_along(x, axis, by):
    length = lax.axis_size(axis)
    pairs = [(i, i + by) for i in range(length) if 0 <= i + by < length]
    return lax.ppermute(x, axis, pairs)


def request_of(positions, req_ends):
    return jnp.sum((req_ends[None, :] < positions[:, None]).astype(jnp.int32), axis=1)


def short_conv(values, weights, segment):
    length = weights.shape[0]
    out_count = values.shape[0] - length + 1
    latest = length - 1
    current = segment[latest:]
    summed = values[latest:].astype(jnp.float32) * weights[0].astype(jnp.float32)
    for lag_step in range(1, length):
        earlier = values[latest - lag_step : latest - lag_step + out_count].astype(jnp.float32)
        same_req = segment[latest - lag_step : latest - lag_step + out_count] == current
        summed = summed + jnp.where(
            same_req[:, None], earlier * weights[lag_step].astype(jnp.float32), 0.0
        )
    return summed


HALO = 32
TILE = 512
GROUP_LANES = 128
WINDOW = 144


def short_conv_rows(x, w, first, dist_all):
    rows = x.shape[0]
    dist = dist_all[first:rows, :]
    acc = x[first:rows, :] * w[0:1, :].astype(jnp.float32)
    for lag in range(1, w.shape[0]):
        term = x[first - lag : rows - lag, :] * w[lag : lag + 1, :].astype(jnp.float32)
        acc = acc + jnp.where(dist >= lag, term, 0.0)
    return acc


def rel_dist(rel_ref, base, count):
    index = base + lax.broadcasted_iota(jnp.int32, (count, 1), 0)
    return index - rel_ref[base : base + count, :]


def chain_kernel(rel_ref, sq, sk, sv, hq, hk, hv, mk, gk_h, fq, fk, fv, filt_ref, wk, wv,
                 z2_ref, xq, xk, xv, xb, zs, ys, group_ch, base):
    rows, tile = xq.shape
    dist_ref = rel_dist(rel_ref, base, rows)
    filters = filt_ref.shape[1]
    lane_ch = pl.program_id(0) * tile + lax.broadcasted_iota(jnp.int32, (filters, tile), 1)
    spread = (lane_ch // group_ch == lax.broadcasted_iota(jnp.int32, (filters, tile), 0))
    filt = jnp.dot(filt_ref[...], spread.astype(filt_ref.dtype), preferred_element_type=jnp.float32)
    for main, halo, x in ((sq, hq, xq), (sk, hk, xk), (sv, hv, xv), (mk, gk_h, xb)):
        reach = halo.shape[0]
        if reach < HALO:
            x[0 : HALO - reach, :] = jnp.zeros((HALO - reach, x.shape[1]), jnp.float32)
        x[HALO - reach : HALO, :] = halo[...].astype(jnp.float32)
        x[HALO:rows, :] = main[...].astype(jnp.float32)

    k1 = short_conv_rows(xk, fk, 16, dist_ref)
    v1 = short_conv_rows(xv, fv, 16, dist_ref)
    zs[16:rows, :] = (k1 * v1).astype(jnp.bfloat16).astype(jnp.float32)
    q1 = short_conv_rows(xq, fq, 24, dist_ref)
    c1 = short_conv_rows(zs, filt, 24, dist_ref)
    ys[24:rows, :] = (q1 * c1).astype(jnp.bfloat16).astype(jnp.float32)
    v2 = short_conv_rows(ys, wv, HALO, dist_ref)
    k2 = short_conv_rows(xb, wk, HALO, dist_ref)
    z2 = (k2 * v2).astype(jnp.bfloat16)
    chunk = z2_ref.shape[2]
    for i in range(z2_ref.shape[0]):
        z2_ref[i] = z2[:, i * chunk : (i + 1) * chunk]


def short_chain(rel, se_streams, se_halo, mr_gates, mr_halo, se_feat, se_filt, mr_feat, shards, half):
    tok_rows = se_streams.shape[0] // 2
    channels = mr_gates.shape[1] // 2
    steps = channels // TILE
    rows = tok_rows + HALO
    taps = se_feat.shape[0]
    chunk = channels // shards

    def col(part, row_block=half):
        return lambda j: (row_block, j + part * steps)

    def halo_spec(halo, part, skip=0):
        if halo.shape[0] < HALO:
            return pl.BlockSpec((halo.shape[0], TILE), col(part + skip, 0))
        return pl.BlockSpec((HALO, TILE), col(part, half * tok_rows // HALO - 1))

    main = [pl.BlockSpec((tok_rows, TILE), col(p)) for p in range(3)]
    halo = [halo_spec(se_halo, p) for p in range(3)]
    wts = [pl.BlockSpec((taps, TILE), col(p, 0)) for p in range(3)]
    return pl.pallas_call(
        functools.partial(
            chain_kernel, group_ch=channels // se_filt.shape[1], base=half * tok_rows + tok_rows - HALO
        ),
        grid=(steps,),
        in_specs=[pl.BlockSpec(rel.shape, lambda j: (0, 0))] + main + halo
        + [main[1], halo_spec(mr_halo, 1, (mr_halo.shape[1] - mr_gates.shape[1]) // channels)] + wts
        + [pl.BlockSpec(se_filt.shape, lambda j: (0, 0)), wts[1], wts[2]],
        out_specs=pl.BlockSpec((TILE // chunk, tok_rows, chunk), lambda j: (j, 0, 0)),
        out_shape=jax.ShapeDtypeStruct((shards, tok_rows, chunk), jnp.bfloat16),
        scratch_shapes=[pltpu.VMEM((rows, TILE), jnp.float32) for _ in range(6)],
    )(rel, se_streams, se_streams, se_streams, se_halo, se_halo, se_halo, mr_gates,
      mr_halo, se_feat, se_feat, se_feat, se_filt, mr_feat, mr_feat)


def long_kernel(rel_ref, mg_ref, mh_ref, wq_ref, prev_ref, lo_ref, hi_ref, skip_ref,
                u_ref, out_ref, xa):
    rows = xa.shape[0]
    reach = mh_ref.shape[0]
    xa[HALO - reach : HALO, :] = mh_ref[...].astype(jnp.float32)
    xa[HALO:rows, :] = mg_ref[...].astype(jnp.float32)
    blk = lo_ref.shape[1]
    q2 = short_conv_rows(xa, wq_ref, HALO, rel_dist(rel_ref, blk - HALO, rows))
    blk = lo_ref.shape[1]
    tile = lo_ref.shape[2]
    width = u_ref.shape[1]
    per_group = tile // u_ref.shape[0]
    lo = lo_ref[0]
    hi = hi_ref[0]
    windows = (jnp.concatenate([prev_ref[0], lo], axis=0), jnp.concatenate([lo, hi], axis=0))
    masks = [
        lax.broadcasted_iota(jnp.int32, (1, width), 1) + b * blk >= rel_ref[(b + 1) * blk : (b + 2) * blk, :]
        for b in range(2)
    ]
    lane_grp = lax.broadcasted_iota(jnp.int32, (1, GROUP_LANES), 1) // per_group
    halves = tile // GROUP_LANES
    groups_half = GROUP_LANES // per_group
    acc = [[jnp.zeros((blk, GROUP_LANES), jnp.float32) for _ in range(halves)] for _ in range(2)]
    for g in range(u_ref.shape[0]):
        half = g // groups_half
        row = jnp.broadcast_to(u_ref[g : g + 1, :], (blk, width))
        taps = pltpu.roll(row, 0, 1, stride=1, stride_axis=0)
        for b in range(2):
            mat = jnp.where(masks[b], taps, 0.0).astype(jnp.bfloat16)
            part = windows[b][:, half * GROUP_LANES : (half + 1) * GROUP_LANES]
            res = jnp.dot(mat, part, preferred_element_type=jnp.float32)
            acc[b][half] = jnp.where(lane_grp == g % groups_half, res, acc[b][half])
    conv = jnp.concatenate([jnp.concatenate(acc[b], axis=1) for b in range(2)], axis=0)
    z = jnp.concatenate([lo, hi], axis=0).astype(jnp.float32)
    mixed = (conv + skip_ref[...].astype(jnp.float32) * z).astype(jnp.bfloat16)
    out_ref[...] = (q2 * mixed.astype(jnp.float32)).astype(jnp.bfloat16)


def long_conv_out(rel, mr_gates, mr_halo, mr_feat, prev_z, z_lo, z_hi, skip, taps_rows):
    steps, blk, lanes = z_lo.shape
    tok_rows = 2 * blk
    channels = steps * lanes
    per_group = channels // taps_rows.shape[0]
    piece = pl.BlockSpec((1, blk, lanes), lambda j: (j, 0, 0))
    return pl.pallas_call(
        long_kernel,
        grid=(steps,),
        in_specs=[
            pl.BlockSpec(rel.shape, lambda j: (0, 0)),
            pl.BlockSpec((tok_rows, lanes), lambda j: (0, j)),
            pl.BlockSpec(
                (mr_halo.shape[0], lanes), lambda j: (0, j + (mr_halo.shape[1] - mr_gates.shape[1]) // lanes)
            ),
            pl.BlockSpec((mr_feat.shape[0], lanes), lambda j: (0, j)),
            piece,
            piece,
            piece,
            pl.BlockSpec((1, lanes), lambda j: (0, j)),
            pl.BlockSpec((lanes // per_group, taps_rows.shape[1]), lambda j: (j, 0)),
        ],
        out_specs=pl.BlockSpec((tok_rows, lanes), lambda j: (0, j)),
        out_shape=jax.ShapeDtypeStruct((tok_rows, channels), jnp.bfloat16),
        scratch_shapes=[pltpu.VMEM((tok_rows + HALO, lanes), jnp.float32)],
    )(rel, mr_gates, mr_halo, mr_feat, prev_z, z_lo, z_hi, skip, taps_rows)


def tail_kernel(begin_ref, first_ref, lo_ref, hi_ref, out_ref, z_all):
    shards, blk, lanes = lo_ref.shape
    tail_len = out_ref.shape[0]
    total = z_all.shape[0]
    for src in range(shards):
        z_all[2 * src * blk : (2 * src + 1) * blk, :] = lo_ref[src]
        z_all[(2 * src + 1) * blk : (2 * src + 2) * blk, :] = hi_ref[src]
    for t in range(out_ref.shape[1]):
        begin = begin_ref[t]
        start = jnp.clip((begin // 16) * 16, 0, total - WINDOW)
        shift = begin - start
        window = z_all[pl.ds(pl.multiple_of(start, 16), WINDOW), :].astype(jnp.float32)
        moved = pltpu.roll(window, (WINDOW - shift) % WINDOW, 0)[:tail_len]
        pos = begin + lax.broadcasted_iota(jnp.int32, (tail_len, 1), 0)
        out_ref[:, t, :] = jnp.where(pos >= first_ref[t], moved, 0.0).astype(out_ref.dtype)


def cut_tails_all(z_lo, z_hi, begins, firsts, tail_len):
    shards, blk, lanes = z_lo.shape
    count = begins.shape[0]
    smem = pl.BlockSpec(memory_space=pltpu.SMEM)
    vmem = pl.BlockSpec(memory_space=pltpu.VMEM)
    out = pl.pallas_call(
        tail_kernel,
        in_specs=[smem, smem, vmem, vmem],
        out_specs=vmem,
        out_shape=jax.ShapeDtypeStruct((tail_len, count, lanes), z_lo.dtype),
        scratch_shapes=[pltpu.VMEM((2 * shards * blk, lanes), z_lo.dtype)],
    )(begins, firsts, z_lo, z_hi)
    return jnp.transpose(out, (1, 0, 2))


def seg_start(positions, req_ends):
    before = req_ends[None, :] < positions[:, None]
    return jnp.max(jnp.where(before, req_ends[None, :] + 1, 0), axis=1)


def pick_entries(lookup_table, indices):
    hits = indices[:, None] == jnp.arange(lookup_table.shape[0], dtype=jnp.int32)[None, :]
    return jnp.sum(jnp.where(hits, lookup_table[None, :], 0), axis=1)


def local(
    se_streams, mr_gates, se_feat, se_filter, mr_feat, mr_filter, mr_skip, req_ends, decode_row
):
    tok_rows = se_streams.shape[0]
    channels = mr_gates.shape[1] // 2
    shards = lax.axis_size("seq")
    device = lax.axis_index("seq")
    offset = device * tok_rows
    reach_rows = se_feat.shape[0] - 1
    tap_count = mr_filter.shape[0]
    tail_len = tap_count - 1
    group_ch = channels // se_filter.shape[1]
    total_req = req_ends.shape[0]
    slot_total = ENDS_MAX + 1
    rim_depth = 2 * reach_rows
    se_tail = se_streams[tok_rows - 3 * reach_rows :]
    mr_tail = mr_gates[tok_rows - 3 * reach_rows :]
    prev_se = passed_along(jnp.concatenate([se_tail, mr_tail], axis=1), "seq", 1)
    blk = tok_rows // 2
    se_filt = se_filter

    window_pos = offset - blk + jnp.arange(tok_rows + blk, dtype=jnp.int32)
    rel = (seg_start(window_pos, req_ends) - (offset - blk))[:, None]
    z_hi = short_chain(
        rel, se_streams, se_streams, mr_gates, mr_gates, se_feat, se_filt, mr_feat, shards, 1
    )
    prev_z = passed_along(z_hi, "seq", 1)
    z_hi, prev_se = lax.optimization_barrier((z_hi, prev_se))
    recv_hi = lax.all_to_all(z_hi, "seq", split_axis=0, concat_axis=0, tiled=True)
    z_lo = short_chain(
        rel, se_streams, prev_se, mr_gates, prev_se, se_feat, se_filt, mr_feat, shards, 0
    )
    z_lo, recv_hi, prev_z = lax.optimization_barrier((z_lo, recv_hi, prev_z))
    recv_lo = lax.all_to_all(z_lo, "seq", split_axis=0, concat_axis=0, tiled=True)
    filt_t = mr_filter[::-1].T.astype(jnp.float32)
    filters = filt_t.shape[0]
    taps_rows = jnp.concatenate(
        [jnp.zeros((filters, 1), jnp.float32), filt_t, jnp.zeros((filters, tap_count - 1), jnp.float32)],
        axis=1,
    )

    hyena_out = long_conv_out(
        rel, mr_gates, prev_se, mr_feat, prev_z, z_lo, z_hi, mr_skip[None, :], taps_rows
    )
    rows_ids = jnp.arange(total_req, dtype=jnp.int32)
    owner = jnp.sum(
        jnp.where(decode_row[None, :] == rows_ids[:, None], rows_ids[None, :], 0), axis=1
    )
    last_pos = pick_entries(req_ends, owner)
    first_pos = jnp.where(owner > 0, pick_entries(req_ends, jnp.maximum(owner - 1, 0)) + 1, 0)
    tail_cache = cut_tails_all(recv_lo, recv_hi, last_pos - tail_len + 1, first_pos, tail_len)
    return (hyena_out, tail_cache)


def solution(mesh):
    placed = (
        P(("groups", "seq"), None),
        P(("groups", "seq"), None),
        P(),
        P(),
        P(),
        P(),
        P(),
        P("groups"),
        P("groups"),
    )
    return jax.shard_map(
        local,
        mesh=mesh,
        in_specs=placed,
        out_specs=(P(("groups", "seq"), None), P("groups", None, "seq")),
        check_vma=False,
    )
```
